32 devices in a mesh: videos: 2 (over y), ha: 4 (over z), wa: 2 (over x), ta: 2 (over core).
Axes of the slice: x: 2, y: 2, z: 4, core: 2. Of those that a mesh axis runs over, the one named last changes fastest.
Arguments:
- latents: bfloat16 [12, 8, 64, 512], P(('videos', 'ta'), 'ha', 'wa'), parts along dimension 0, may hold values from -200 to 200
- norm1_gain: float32 [512], replicated, may hold values from 0.25 to 1.75
- norm1_shift: float32 [512], replicated, may hold values from -2.5 to 2.5
- up_weight: bfloat16 [3, 3, 512, 256], replicated, may hold values from -0.1875 to 0.1875
- norm2_gain: float32 [256], replicated, may hold values from 0.25 to 1.75
- norm2_shift: float32 [256], replicated, may hold values from -2.5 to 2.5
- conv_a: bfloat16 [3, 3, 3, 256, 256], replicated, may hold values from -0.078125 to 0.078125
- norm3_gain: float32 [256], replicated, may hold values from 0.25 to 1.75
- norm3_shift: float32 [256], replicated, may hold values from -2.5 to 2.5
- conv_b: bfloat16 [3, 3, 3, 256, 256], replicated, may hold values from -0.078125 to 0.078125
Outputs:
- decoded: bfloat16 [12, 16, 128, 256], P(('videos', 'ta'), 'ha', 'wa'), parts along dimension 0
The draws below stay inside these ranges and needn't reach their ends.
There are 2 independent parts, one for each index of `videos`. The reference program is written for one: setup_inputs(seed, part) draws one part's arguments, and reference() takes and returns one part's arrays. A program takes and returns all parts, laid end to end along the dimension named above; an argument that names none is the same for every part. Nothing has to cross between parts.
All inputs are finite; a program needn't handle non-finite values.
Results may differ from the reference program's by a relative error of at most 0.008.
Values may be sent and summed in bfloat16 or wider, within the bound.
No kernel may reach another device: no remote copies, remote signals or barrier semaphores. Data moves between devices by JAX's collectives and lax.ppermute only.
A program may use at most 64 MiB of HBM per device.

```python
import math
import jax
import jax.numpy as jnp
from jax import lax

C1 = 512
C2 = 256
GROUPS = 32
FRAMES = 6
ROWS = 8
COLS = 64


def draw_latents(key, part):
    keys = jax.random.split(key, 4)
    offsets = jax.random.uniform(keys[0], (C1,), jnp.float32, -1.5, 1.5)
    chan_scale = jnp.exp(jax.random.uniform(keys[1], (C1,), jnp.float32, 0.0, math.log(3.0)))
    pos_scale = jnp.exp(jax.random.uniform(keys[2], (FRAMES, ROWS, COLS, 1), jnp.float32, 0.0, math.log(2.0)))
    ramp = jnp.arange(ROWS, dtype=jnp.float32) / max(ROWS - 1, 1)
    col_ramp = jnp.arange(COLS, dtype=jnp.float32) / max(COLS - 1, 1)
    col_scale = jnp.exp(math.log(2.0) * col_ramp)
    frame_ids = jnp.arange(FRAMES, dtype=jnp.int32)
    early = frame_ids < FRAMES // 2
    frame_gain = jnp.where(early, 0.4, 1.0).astype(jnp.float32)
    frame_shift = jnp.where(early, -0.5, 0.0).astype(jnp.float32)
    noise = jnp.clip(jax.random.normal(keys[3], (FRAMES, ROWS, COLS, C1), jnp.float32), -4.0, 4.0)
    row_scale = 1.0 + 2.0 * ramp
    amplitude = row_scale[None, :, None, None] * col_scale[None, None, :, None] * frame_gain[:, None, None, None]
    values = offsets + frame_shift[:, None, None, None] + noise * amplitude * pos_scale * chan_scale
    return values.astype(jnp.bfloat16)


def normal_values(own_key, extent, scale, limit, kind=jnp.bfloat16):
    entries = jax.random.normal(own_key, extent, jnp.float32) * scale
    return jnp.minimum(jnp.maximum(entries, -limit), limit).astype(kind)


def setup_inputs(seed: int = 0, part: int = 0) -> dict:
    streams_of = jax.random.split(jax.random.key(seed), 11)
    part_splits = jax.random.split(jax.random.fold_in(streams_of[10], part), 11)
    latents = draw_latents(jax.random.fold_in(jax.random.fold_in(streams_of[10], part), 71), part)
    norm1_gain = jnp.clip(1.0 + 0.15 * jax.random.normal(streams_of[1], (C1,), jnp.float32), 0.25, 1.75)
    norm1_shift = normal_values(streams_of[2], (C1,), 0.5, 2.5, jnp.float32)
    up_weight = normal_values(streams_of[3], (3, 3, C1, C2), (2 * C1) ** -0.5, 0.1875)
    norm2_gain = jnp.clip(1.0 + 0.15 * jax.random.normal(streams_of[4], (C2,), jnp.float32), 0.25, 1.75)
    norm2_shift = normal_values(streams_of[5], (C2,), 0.5, 2.5, jnp.float32)
    conv_a = normal_values(streams_of[6], (3, 3, 3, C2, C2), (27 * C2) ** -0.5, 0.078125)
    norm3_gain = jnp.clip(1.0 + 0.15 * jax.random.normal(streams_of[7], (C2,), jnp.float32), 0.25, 1.75)
    norm3_shift = normal_values(streams_of[8], (C2,), 0.5, 2.5, jnp.float32)
    conv_b = normal_values(streams_of[9], (3, 3, 3, C2, C2), (27 * C2) ** -0.5, 0.078125)
    return dict(latents=latents, norm1_gain=norm1_gain, norm1_shift=norm1_shift, up_weight=up_weight, norm2_gain=norm2_gain, norm2_shift=norm2_shift, conv_a=conv_a, norm3_gain=norm3_gain, norm3_shift=norm3_shift, conv_b=conv_b)


EPSILON = 1e-06

def activate(values, scale_vec, shift_vec):
    channels = values.shape[-1]
    group_width = channels // GROUPS
    grouped = values.reshape(-1, GROUPS, group_width)
    average = lax.optimization_barrier(jnp.mean(grouped, axis=(0, 2)))
    centred = grouped - average[None, :, None]
    spread = lax.optimization_barrier(jnp.mean(centred * centred, axis=(0, 2)))
    scaling = 1.0 / jnp.sqrt(spread + EPSILON)
    normed = (values - jnp.repeat(average, group_width)) * jnp.repeat(scaling, group_width) * scale_vec + shift_vec
    return jax.nn.silu(normed).astype(jnp.bfloat16)

def parity_merge(lead_part, mid_part, tail_part, axis_pos):
    pad_end = [(0, 0)] * lead_part.ndim
    pad_front = [(0, 0)] * lead_part.ndim
    pad_end[axis_pos] = (0, 1)
    pad_front[axis_pos] = (1, 0)
    even_part = jnp.pad(lead_part, pad_end) + jnp.pad(tail_part, pad_front)
    odd_part = jnp.pad(mid_part, pad_end)
    stacked = jnp.stack([even_part, odd_part], axis=axis_pos + 1)
    new_shape = list(even_part.shape)
    new_shape[axis_pos] = new_shape[axis_pos] * 2
    return stacked.reshape(new_shape)

def spread_taps(source, kernel):
    frames, height, across, channels = source.shape
    flattened = source.reshape(-1, channels)
    products = [[jnp.dot(flattened, kernel[tap_y, tap_x], preferred_element_type=jnp.float32).reshape(frames, height, across, -1) for tap_x in range(3)] for tap_y in range(3)]
    columns = [parity_merge(products[0][tap_x], products[1][tap_x], products[2][tap_x], 1) for tap_x in range(3)]
    return parity_merge(columns[0], columns[1], columns[2], 2)

def valid_conv(padded, kernel, frames, height, across):
    result = jnp.zeros((frames * height * across, kernel.shape[-1]), jnp.float32)
    for step_t in range(3):
        for step_y in range(3):
            for step_x in range(3):
                window = padded[step_t:step_t + frames, step_y:step_y + height, step_x:step_x + across]
                result = result + jnp.dot(window.reshape(-1, window.shape[-1]), kernel[step_t, step_y, step_x], preferred_element_type=jnp.float32)
    return result.reshape(frames, height, across, -1)

def causal_pad(values):
    extended = jnp.concatenate([values[:1], values[:1], values], axis=0)
    return jnp.pad(extended, ((0, 0), (1, 1), (1, 1), (0, 0)))

def reference(latents, norm1_gain, norm1_shift, up_weight, norm2_gain, norm2_shift, conv_a, norm3_gain, norm3_shift, conv_b):
    frames, height, across, channels = latents.shape
    activated = activate(latents.astype(jnp.float32), norm1_gain, norm1_shift)
    lifted = spread_taps(activated, up_weight)[:, 1:2 * height + 1, 1:2 * across + 1].astype(jnp.bfloat16)
    lifted_f = lifted.astype(jnp.float32)
    first_act = activate(lifted_f, norm2_gain, norm2_shift)
    hidden = valid_conv(causal_pad(first_act), conv_a, frames, 2 * height, 2 * across).astype(jnp.bfloat16)
    second_act = activate(hidden.astype(jnp.float32), norm3_gain, norm3_shift)
    branch = valid_conv(causal_pad(second_act), conv_b, frames, 2 * height, 2 * across)
    return (lifted_f + branch).astype(jnp.bfloat16)
```

```python
import jax
import jax.numpy as jnp
from jax import lax
from jax.sharding import PartitionSpec as P

GROUPS = 32


EPSILON = 1e-06


def passed_along(block, axis, distance):
    devices = range(lax.axis_size(axis))
    route = [(i - distance, i) for i in devices if i - distance in devices]
    return lax.ppermute(block, axis, route)


def padded_2(x, sides, width):
    for axis, dim in sides:
        size, length = (lax.axis_size(axis), x.shape[dim])
        up = [(i, (i + 1) % size) for i in range(size - 1)]
        down = [(j, i) for i, j in up]
        last = lax.slice_in_dim(x, length - width, length, axis=dim)
        initial = lax.slice_in_dim(x, 0, width, axis=dim)
        before = lax.ppermute(last, axis, up)
        after = lax.ppermute(initial, axis, down)
        x = jnp.concatenate([before, x, after], axis=dim)
    return x


def group_allreduce(x, axes):
    sizes = [lax.axis_size(a) for a in axes]
    count = 1
    for s in sizes:
        count *= s
    if count & (count - 1):
        return lax.psum(x, axes)
    index = 0
    for a, s in zip(axes, sizes):
        index = index * s + lax.axis_index(a)
    shift = 0
    while (1 << shift) < count:
        width = min(2, (count.bit_length() - 1) - shift)
        slots = 1 << width
        position = (index >> shift) % slots
        received = [x] + [
            lax.ppermute(x, axes, [(i, i ^ (d << shift)) for i in range(count)])
            for d in range(1, slots)
        ]
        ordered = []
        for j in range(slots):
            value = jnp.zeros_like(x)
            for d in range(slots):
                value = jnp.where((position ^ d) == j, received[d], value)
            ordered.append(value)
        while len(ordered) > 1:
            ordered = [ordered[k] + ordered[k + 1] for k in range(0, len(ordered), 2)]
        x = ordered[0]
        shift += width
    return x


def activate(values, sample, scale_vec, shift_vec):
    channels = values.shape[-1]
    group_width = channels // GROUPS
    grouped = sample.reshape(-1, GROUPS, group_width)
    entries = (
        grouped.shape[0]
        * group_width
        * lax.axis_size("ha")
        * lax.axis_size("wa")
        * lax.axis_size("ta")
    )
    totals, squares = group_allreduce(
        jnp.stack([jnp.sum(grouped, axis=(0, 2)), jnp.sum(grouped * grouped, axis=(0, 2))]),
        ("ha", "wa", "ta"),
    )
    average = totals / entries
    spread = squares / entries - average * average
    scaling = lax.rsqrt(spread + EPSILON)
    normed = (values - jnp.repeat(average, group_width)) * jnp.repeat(
        scaling, group_width
    ) * scale_vec + shift_vec
    return jax.nn.silu(normed).astype(jnp.bfloat16)


def parity_merge(lead_part, mid_part, tail_part, axis_pos):
    pad_end = [(0, 0)] * lead_part.ndim
    pad_front = [(0, 0)] * lead_part.ndim
    pad_end[axis_pos] = (0, 1)
    pad_front[axis_pos] = (1, 0)
    even_part = jnp.pad(lead_part, pad_end) + jnp.pad(tail_part, pad_front)
    odd_part = jnp.pad(mid_part, pad_end)
    stacked = jnp.stack([even_part, odd_part], axis=axis_pos + 1)
    new_shape = list(even_part.shape)
    new_shape[axis_pos] = new_shape[axis_pos] * 2
    return stacked.reshape(new_shape)


def spread_taps(source, kernel):
    frames, height, across, channels = source.shape
    flattened = source.reshape(-1, channels)
    products = [
        [
            jnp.dot(flattened, kernel[tap_y, tap_x], preferred_element_type=jnp.float32).reshape(
                frames, height, across, -1
            )
            for tap_x in range(3)
        ]
        for tap_y in range(3)
    ]
    columns = [
        parity_merge(products[0][tap_x], products[1][tap_x], products[2][tap_x], 1)
        for tap_x in range(3)
    ]
    return parity_merge(columns[0], columns[1], columns[2], 2)


def valid_conv(padded, kernel, frames, height, across):
    result = jnp.zeros((frames * height * across, kernel.shape[-1]), jnp.float32)
    for step_t in range(3):
        for step_y in range(3):
            for step_x in range(3):
                window = padded[
                    step_t : step_t + frames, step_y : step_y + height, step_x : step_x + across
                ]
                result = result + jnp.dot(
                    window.reshape(-1, window.shape[-1]),
                    kernel[step_t, step_y, step_x],
                    preferred_element_type=jnp.float32,
                )
    return result.reshape(frames, height, across, -1)


def causal_extend(values):
    earlier = passed_along(values[-2:], "ta", 1)
    opening = jnp.concatenate([values[:1], values[:1]], axis=0)
    earlier = jnp.where(lax.axis_index("ta") == 0, opening, earlier)
    return jnp.concatenate([earlier, values], axis=0)


def bordered_one(values):
    return padded_2(values, (("ha", 1), ("wa", 2)), 1)


def per_device(
    latents,
    norm1_gain,
    norm1_shift,
    up_weight,
    norm2_gain,
    norm2_shift,
    conv_a,
    norm3_gain,
    norm3_shift,
    conv_b,
):
    frames, height, across, channels = latents.shape
    latent_f = latents.astype(jnp.float32)
    activated = activate(latent_f, latent_f, norm1_gain, norm1_shift)
    spilled = spread_taps(activated, up_weight)
    from_below = passed_along(spilled[:, 0], "ha", -1)
    row_fixed = spilled[:, 1 : 2 * height + 1]
    row_fixed = jnp.concatenate(
        [row_fixed[:, :-1], row_fixed[:, -1:] + from_below[:, None]], axis=1
    )
    beside = passed_along(row_fixed[:, :, 0], "wa", -1)
    lifted = jnp.concatenate(
        [
            row_fixed[:, :, 1 : 2 * across],
            row_fixed[:, :, 2 * across : 2 * across + 1] + beside[:, :, None],
        ],
        axis=2,
    )
    lifted = lifted.astype(jnp.bfloat16)
    lifted_f = lifted.astype(jnp.float32)
    first_act = activate(lifted_f, lifted_f, norm2_gain, norm2_shift)
    out_h = 2 * height
    out_w = 2 * across
    hidden = valid_conv(
        bordered_one(causal_extend(first_act)), conv_a, frames, out_h, out_w
    ).astype(jnp.bfloat16)
    hidden_f = hidden.astype(jnp.float32)
    second_act = activate(hidden_f, hidden_f, norm3_gain, norm3_shift)
    framed = bordered_one(causal_extend(second_act))
    branch = valid_conv(framed, conv_b, frames, out_h, out_w)
    return (lifted_f + branch).astype(jnp.bfloat16)


def solution(mesh):
    return jax.shard_map(
        per_device,
        mesh=mesh,
        in_specs=(
            P(("videos", "ta"), "ha", "wa", None),
            P(),
            P(),
            P(),
            P(),
            P(),
            P(),
            P(),
            P(),
            P(),
        ),
        out_specs=P(("videos", "ta"), "ha", "wa", None),
        check_vma=False,
    )
```

```python
import jax
import jax.numpy as jnp
from jax import lax
from jax.sharding import PartitionSpec as P

GROUPS = 32


EPSILON = 1e-06


def passed_along(block, axis, distance):
    devices = range(lax.axis_size(axis))
    route = [(i - distance, i) for i in devices if i - distance in devices]
    return lax.ppermute(block, axis, route)


def padded_2(x, sides, width):
    for axis, dim in sides:
        size, length = (lax.axis_size(axis), x.shape[dim])
        up = [(i, (i + 1) % size) for i in range(size - 1)]
        down = [(j, i) for i, j in up]
        last = lax.slice_in_dim(x, length - width, length, axis=dim)
        initial = lax.slice_in_dim(x, 0, width, axis=dim)
        before = lax.ppermute(last, axis, up)
        after = lax.ppermute(initial, axis, down)
        x = jnp.concatenate([before, x, after], axis=dim)
    return x


def group_allreduce(x, axes):
    sizes = [lax.axis_size(a) for a in axes]
    count = 1
    for s in sizes:
        count *= s
    if count & (count - 1):
        return lax.psum(x, axes)
    index = 0
    for a, s in zip(axes, sizes):
        index = index * s + lax.axis_index(a)
    shift = 0
    while (1 << shift) < count:
        width = min(2, (count.bit_length() - 1) - shift)
        slots = 1 << width
        position = (index >> shift) % slots
        received = [x] + [
            lax.ppermute(x, axes, [(i, i ^ (d << shift)) for i in range(count)])
            for d in range(1, slots)
        ]
        ordered = []
        for j in range(slots):
            value = jnp.zeros_like(x)
            for d in range(slots):
                value = jnp.where((position ^ d) == j, received[d], value)
            ordered.append(value)
        while len(ordered) > 1:
            ordered = [ordered[k] + ordered[k + 1] for k in range(0, len(ordered), 2)]
        x = ordered[0]
        shift += width
    return x


def group_stats(values):
    channels = values.shape[-1]
    group_width = channels // GROUPS
    grouped = values.reshape(-1, GROUPS, group_width)
    entries = (
        grouped.shape[0]
        * group_width
        * lax.axis_size("ha")
        * lax.axis_size("wa")
        * lax.axis_size("ta")
    )
    totals, squares = group_allreduce(
        jnp.stack([jnp.sum(grouped, axis=(0, 2)), jnp.sum(grouped * grouped, axis=(0, 2))]),
        ("ha", "wa", "ta"),
    )
    average = totals / entries
    spread = squares / entries - average * average
    scaling = lax.rsqrt(spread + EPSILON)
    return jnp.repeat(average, group_width), jnp.repeat(scaling, group_width)


def activate(values, stats, scale_vec, shift_vec):
    average, scaling = stats
    normed = (values - average) * scaling * scale_vec + shift_vec
    return jax.nn.silu(normed)


def inside_mask(rows, cols, low_pad):
    h, h_last = lax.axis_index("ha"), lax.axis_size("ha") - 1
    w, w_last = lax.axis_index("wa"), lax.axis_size("wa") - 1
    r = jnp.arange(rows)
    c = jnp.arange(cols)
    row_ok = jnp.logical_and(
        jnp.logical_or(r >= low_pad, h > 0), jnp.logical_or(r < rows - 1, h < h_last)
    )
    col_ok = jnp.logical_and(
        jnp.logical_or(c >= low_pad, w > 0), jnp.logical_or(c < cols - 1, w < w_last)
    )
    return jnp.logical_and(row_ok[:, None], col_ok[None, :])[None, :, :, None]


def latent_halo(x):
    h_size, w_size = lax.axis_size("ha"), lax.axis_size("wa")
    below = passed_along(x[:, :1], "ha", -1)
    right = passed_along(x[:, :, :1], "wa", -1)
    corner_route = [
        ((h + 1) * w_size + w + 1, h * w_size + w)
        for h in range(h_size - 1)
        for w in range(w_size - 1)
    ]
    corner = lax.ppermute(x[:, :1, :1], ("ha", "wa"), corner_route)
    top = jnp.concatenate([x, right], axis=2)
    bottom = jnp.concatenate([below, corner], axis=2)
    return jnp.concatenate([top, bottom], axis=1)


def upsample(act, kernel):
    frames, rows, cols, channels = act.shape
    height, across = rows - 1, cols - 1
    flat = lambda v: v.reshape(-1, channels)
    dot = lambda v, w: jnp.dot(flat(v), w, preferred_element_type=jnp.float32)
    a = act[:, :height, :across]
    b = act[:, :height, 1:]
    c = act[:, 1:, :across]
    d = act[:, 1:, 1:]
    out = kernel.shape[-1]
    pa = dot(a, jnp.concatenate([kernel[1, 1], kernel[1, 2], kernel[2, 1], kernel[2, 2]], axis=1))
    pb = dot(b, jnp.concatenate([kernel[1, 0], kernel[2, 0]], axis=1))
    pc = dot(c, jnp.concatenate([kernel[0, 1], kernel[0, 2]], axis=1))
    pd = dot(d, kernel[0, 0])
    ee = pa[:, :out]
    eo = pa[:, out : 2 * out] + pb[:, :out]
    oe = pa[:, 2 * out : 3 * out] + pc[:, :out]
    oo = pa[:, 3 * out :] + pb[:, out:] + pc[:, out:] + pd
    shape = (frames, height, across, 1, out)
    even = jnp.concatenate([ee.reshape(shape), eo.reshape(shape)], axis=3)
    odd = jnp.concatenate([oe.reshape(shape), oo.reshape(shape)], axis=3)
    even = even.reshape(frames, height, 1, 2 * across, out)
    odd = odd.reshape(frames, height, 1, 2 * across, out)
    return jnp.concatenate([even, odd], axis=2).reshape(frames, 2 * height, 2 * across, out)


def valid_conv(padded, kernel, frames, height, across):
    result = jnp.zeros((frames * height * across, kernel.shape[-1]), jnp.float32)
    for step_t in range(3):
        for step_y in range(3):
            for step_x in range(3):
                window = padded[
                    step_t : step_t + frames, step_y : step_y + height, step_x : step_x + across
                ]
                result = result + jnp.dot(
                    window.reshape(-1, window.shape[-1]),
                    kernel[step_t, step_y, step_x],
                    preferred_element_type=jnp.float32,
                )
    return result.reshape(frames, height, across, -1)


def conv_halo(values):
    x = padded_2(values, (("ha", 1), ("wa", 2)), 1)
    earlier = passed_along(x[-2:], "ta", 1)
    opening = jnp.concatenate([x[:1], x[:1]], axis=0)
    earlier = jnp.where(lax.axis_index("ta") == 0, opening, earlier)
    return jnp.concatenate([earlier, x], axis=0)


def norm_conv(values, gain, shift, kernel):
    frames, height, across, _ = values.shape
    values_f = values.astype(jnp.float32)
    stats = group_stats(values_f)
    extended = conv_halo(values).astype(jnp.float32)
    act = activate(extended, stats, gain, shift)
    act = jnp.where(inside_mask(height + 2, across + 2, 1), act, 0.0).astype(jnp.bfloat16)
    return valid_conv(act, kernel, frames, height, across)


def per_device(
    latents,
    norm1_gain,
    norm1_shift,
    up_weight,
    norm2_gain,
    norm2_shift,
    conv_a,
    norm3_gain,
    norm3_shift,
    conv_b,
):
    frames, height, across, channels = latents.shape
    stats = group_stats(latents.astype(jnp.float32))
    extended = latent_halo(latents).astype(jnp.float32)
    activated = activate(extended, stats, norm1_gain, norm1_shift)
    activated = jnp.where(inside_mask(height + 1, across + 1, 0), activated, 0.0)
    lifted = upsample(activated.astype(jnp.bfloat16), up_weight).astype(jnp.bfloat16)
    hidden = norm_conv(lifted, norm2_gain, norm2_shift, conv_a).astype(jnp.bfloat16)
    branch = norm_conv(hidden, norm3_gain, norm3_shift, conv_b)
    return (lifted.astype(jnp.float32) + branch).astype(jnp.bfloat16)


def solution(mesh):
    return jax.shard_map(
        per_device,
        mesh=mesh,
        in_specs=(
            P(("videos", "ta"), "ha", "wa", None),
            P(),
            P(),
            P(),
            P(),
            P(),
            P(),
            P(),
            P(),
            P(),
        ),
        out_specs=P(("videos", "ta"), "ha", "wa", None),
        check_vma=False,
    )
```

```python
import jax
import jax.numpy as jnp
from jax import lax
from jax.sharding import PartitionSpec as P

GROUPS = 32


EPSILON = 1e-06


def passed_along(block, axis, distance):
    devices = range(lax.axis_size(axis))
    route = [(i - distance, i) for i in devices if i - distance in devices]
    return lax.ppermute(block, axis, route)


def padded_2(x, sides, width):
    for axis, dim in sides:
        size, length = (lax.axis_size(axis), x.shape[dim])
        up = [(i, (i + 1) % size) for i in range(size - 1)]
        down = [(j, i) for i, j in up]
        last = lax.slice_in_dim(x, length - width, length, axis=dim)
        initial = lax.slice_in_dim(x, 0, width, axis=dim)
        before = lax.ppermute(last, axis, up)
        after = lax.ppermute(initial, axis, down)
        x = jnp.concatenate([before, x, after], axis=dim)
    return x


def group_allreduce(x, axes):
    sizes = [lax.axis_size(a) for a in axes]
    count = 1
    for s in sizes:
        count *= s
    if count & (count - 1):
        return lax.psum(x, axes)
    index = 0
    for a, s in zip(axes, sizes):
        index = index * s + lax.axis_index(a)
    shift = 0
    while (1 << shift) < count:
        width = min(2, (count.bit_length() - 1) - shift)
        slots = 1 << width
        position = (index >> shift) % slots
        received = [x] + [
            lax.ppermute(x, axes, [(i, i ^ (d << shift)) for i in range(count)])
            for d in range(1, slots)
        ]
        ordered = []
        for j in range(slots):
            value = jnp.zeros_like(x)
            for d in range(slots):
                value = jnp.where((position ^ d) == j, received[d], value)
            ordered.append(value)
        while len(ordered) > 1:
            ordered = [ordered[k] + ordered[k + 1] for k in range(0, len(ordered), 2)]
        x = ordered[0]
        shift += width
    return x


def group_stats(values):
    channels = values.shape[-1]
    group_width = channels // GROUPS
    grouped = values.reshape(-1, GROUPS, group_width)
    entries = (
        grouped.shape[0]
        * group_width
        * lax.axis_size("ha")
        * lax.axis_size("wa")
        * lax.axis_size("ta")
    )
    totals, squares = group_allreduce(
        jnp.stack([jnp.sum(grouped, axis=(0, 2)), jnp.sum(grouped * grouped, axis=(0, 2))]),
        ("ha", "wa", "ta"),
    )
    average = totals / entries
    spread = squares / entries - average * average
    scaling = lax.rsqrt(spread + EPSILON)
    return jnp.repeat(average, group_width), jnp.repeat(scaling, group_width)


def activate(values, stats, scale_vec, shift_vec):
    average, scaling = stats
    normed = (values - average) * scaling * scale_vec + shift_vec
    return jax.nn.silu(normed)


def inside_mask(rows, cols, low_pad):
    h, h_last = lax.axis_index("ha"), lax.axis_size("ha") - 1
    w, w_last = lax.axis_index("wa"), lax.axis_size("wa") - 1
    r = jnp.arange(rows)
    c = jnp.arange(cols)
    row_ok = jnp.logical_and(
        jnp.logical_or(r >= low_pad, h > 0), jnp.logical_or(r < rows - 1, h < h_last)
    )
    col_ok = jnp.logical_and(
        jnp.logical_or(c >= low_pad, w > 0), jnp.logical_or(c < cols - 1, w < w_last)
    )
    return jnp.logical_and(row_ok[:, None], col_ok[None, :])[None, :, :, None]


def latent_halo(x):
    h_size, w_size = lax.axis_size("ha"), lax.axis_size("wa")
    below = passed_along(x[:, :1], "ha", -1)
    right = passed_along(x[:, :, :1], "wa", -1)
    corner_route = [
        ((h + 1) * w_size + w + 1, h * w_size + w)
        for h in range(h_size - 1)
        for w in range(w_size - 1)
    ]
    corner = lax.ppermute(x[:, :1, :1], ("ha", "wa"), corner_route)
    top = jnp.concatenate([x, right], axis=2)
    bottom = jnp.concatenate([below, corner], axis=2)
    return jnp.concatenate([top, bottom], axis=1)


def upsample(act, kernel):
    frames, rows, cols, channels = act.shape
    height, across = rows - 1, cols - 1
    flat = lambda v: v.reshape(-1, channels)
    dot = lambda v, w: jnp.dot(flat(v), w, preferred_element_type=jnp.float32)
    a = act[:, :height, :across]
    b = act[:, :height, 1:]
    c = act[:, 1:, :across]
    d = act[:, 1:, 1:]
    out = kernel.shape[-1]
    pa = dot(a, jnp.concatenate([kernel[1, 1], kernel[1, 2], kernel[2, 1], kernel[2, 2]], axis=1))
    pb = dot(b, jnp.concatenate([kernel[1, 0], kernel[2, 0]], axis=1))
    pc = dot(c, jnp.concatenate([kernel[0, 1], kernel[0, 2]], axis=1))
    pd = dot(d, kernel[0, 0])
    ee = pa[:, :out]
    eo = pa[:, out : 2 * out] + pb[:, :out]
    oe = pa[:, 2 * out : 3 * out] + pc[:, :out]
    oo = pa[:, 3 * out :] + pb[:, out:] + pc[:, out:] + pd
    shape = (frames, height, across, 1, out)
    even = jnp.concatenate([ee.reshape(shape), eo.reshape(shape)], axis=3)
    odd = jnp.concatenate([oe.reshape(shape), oo.reshape(shape)], axis=3)
    even = even.reshape(frames, height, 1, 2 * across, out)
    odd = odd.reshape(frames, height, 1, 2 * across, out)
    return jnp.concatenate([even, odd], axis=2).reshape(frames, 2 * height, 2 * across, out)


def valid_conv(padded, kernel, frames, height, across):
    result = jnp.zeros((frames * height * across, kernel.shape[-1]), jnp.float32)
    for step_t in range(3):
        for step_y in range(3):
            for step_x in range(3):
                window = padded[
                    step_t : step_t + frames, step_y : step_y + height, step_x : step_x + across
                ]
                result = result + jnp.dot(
                    window.reshape(-1, window.shape[-1]),
                    kernel[step_t, step_y, step_x],
                    preferred_element_type=jnp.float32,
                )
    return result.reshape(frames, height, across, -1)


def conv_halo(values):
    x = padded_2(values, (("ha", 1), ("wa", 2)), 1)
    earlier = passed_along(x[-2:], "ta", 1)
    opening = jnp.concatenate([x[:1], x[:1]], axis=0)
    earlier = jnp.where(lax.axis_index("ta") == 0, opening, earlier)
    return jnp.concatenate([earlier, x], axis=0)


def swap(x, axis, distance):
    size = lax.axis_size(axis)
    return lax.ppermute(x, axis, [(i, i ^ distance) for i in range(size)])


def fast_mesh():
    return lax.axis_size("ta") == 2 and lax.axis_size("wa") == 2 and lax.axis_size("ha") == 4


def local_sums(values):
    grouped = values.reshape(-1, GROUPS, values.shape[-1] // GROUPS)
    return jnp.stack([jnp.sum(grouped, axis=(0, 2)), jnp.sum(grouped * grouped, axis=(0, 2))])


def finish_stats(sums, values):
    channels = values.shape[-1]
    group_width = channels // GROUPS
    entries = (
        values.size // GROUPS
        * lax.axis_size("ha")
        * lax.axis_size("wa")
        * lax.axis_size("ta")
    )
    average = sums[0] / entries
    spread = sums[1] / entries - average * average
    scaling = lax.rsqrt(spread + EPSILON)
    return jnp.repeat(average, group_width), jnp.repeat(scaling, group_width)


def ha_round(sums, upper, lower):
    h = lax.axis_index("ha")
    to_first = jnp.where(h % 2 == 1, upper, lower)
    to_third = jnp.where(h == 2, upper, lower)
    s1, got_first = swap((sums, to_first), "ha", 1)
    s2 = swap(sums, "ha", 2)
    s3, got_third = swap((sums, to_third), "ha", 3)
    sums = (sums + s1) + (s2 + s3)
    above = jnp.where(h % 2 == 1, got_first, got_third)
    below = jnp.where(h % 2 == 0, got_first, got_third)
    return sums, above, below


def fast_conv_input(values):
    sums = local_sums(values.astype(jnp.float32))
    s_t, earlier = swap((sums, values[-2:]), "ta", 1)
    sums = sums + s_t
    opening = jnp.concatenate([values[:1], values[:1]], axis=0)
    earlier = jnp.where(lax.axis_index("ta") == 0, opening, earlier)
    x = jnp.concatenate([earlier, values], axis=0)
    w = lax.axis_index("wa")
    s_w, beside = swap((sums, jnp.where(w == 0, x[:, :, -1:], x[:, :, :1])), "wa", 1)
    sums = sums + s_w
    x = jnp.concatenate([beside, x, beside], axis=2)
    sums, above, below = ha_round(sums, x[:, :1], x[:, -1:])
    x = jnp.concatenate([above, x, below], axis=1)
    return finish_stats(sums, values), x


def fast_latent_input(values):
    sums = local_sums(values.astype(jnp.float32))
    sums = sums + swap(sums, "ta", 1)
    s_w, beside = swap((sums, values[:, :, :1]), "wa", 1)
    sums = sums + s_w
    x = jnp.concatenate([values, beside], axis=2)
    sums, _, below = ha_round(sums, x[:, :1], x[:, :1])
    x = jnp.concatenate([x, below], axis=1)
    return finish_stats(sums, values), x


def norm_conv(values, gain, shift, kernel):
    frames, height, across, _ = values.shape
    if fast_mesh():
        stats, extended = fast_conv_input(values)
    else:
        stats = group_stats(values.astype(jnp.float32))
        extended = conv_halo(values)
    act = activate(extended.astype(jnp.float32), stats, gain, shift)
    act = jnp.where(inside_mask(height + 2, across + 2, 1), act, 0.0).astype(jnp.bfloat16)
    return valid_conv(act, kernel, frames, height, across)


def per_device(
    latents,
    norm1_gain,
    norm1_shift,
    up_weight,
    norm2_gain,
    norm2_shift,
    conv_a,
    norm3_gain,
    norm3_shift,
    conv_b,
):
    frames, height, across, channels = latents.shape
    if fast_mesh():
        stats, extended = fast_latent_input(latents)
    else:
        stats = group_stats(latents.astype(jnp.float32))
        extended = latent_halo(latents)
    activated = activate(extended.astype(jnp.float32), stats, norm1_gain, norm1_shift)
    activated = jnp.where(inside_mask(height + 1, across + 1, 0), activated, 0.0)
    lifted = upsample(activated.astype(jnp.bfloat16), up_weight).astype(jnp.bfloat16)
    hidden = norm_conv(lifted, norm2_gain, norm2_shift, conv_a).astype(jnp.bfloat16)
    branch = norm_conv(hidden, norm3_gain, norm3_shift, conv_b)
    return (lifted.astype(jnp.float32) + branch).astype(jnp.bfloat16)


def solution(mesh):
    return jax.shard_map(
        per_device,
        mesh=mesh,
        in_specs=(
            P(("videos", "ta"), "ha", "wa", None),
            P(),
            P(),
            P(),
            P(),
            P(),
            P(),
            P(),
            P(),
            P(),
        ),
        out_specs=P(("videos", "ta"), "ha", "wa", None),
        check_vma=False,
    )
```

```python
import jax
import jax.numpy as jnp
from jax import lax
from jax.sharding import PartitionSpec as P

GROUPS = 32


EPSILON = 1e-06


def passed_along(block, axis, distance):
    devices = range(lax.axis_size(axis))
    route = [(i - distance, i) for i in devices if i - distance in devices]
    return lax.ppermute(block, axis, route)


def padded_2(x, sides, width):
    for axis, dim in sides:
        size, length = (lax.axis_size(axis), x.shape[dim])
        up = [(i, (i + 1) % size) for i in range(size - 1)]
        down = [(j, i) for i, j in up]
        last = lax.slice_in_dim(x, length - width, length, axis=dim)
        initial = lax.slice_in_dim(x, 0, width, axis=dim)
        before = lax.ppermute(last, axis, up)
        after = lax.ppermute(initial, axis, down)
        x = jnp.concatenate([before, x, after], axis=dim)
    return x


def group_allreduce(x, axes):
    sizes = [lax.axis_size(a) for a in axes]
    count = 1
    for s in sizes:
        count *= s
    if count & (count - 1):
        return lax.psum(x, axes)
    index = 0
    for a, s in zip(axes, sizes):
        index = index * s + lax.axis_index(a)
    shift = 0
    while (1 << shift) < count:
        width = min(2, (count.bit_length() - 1) - shift)
        slots = 1 << width
        position = (index >> shift) % slots
        received = [x] + [
            lax.ppermute(x, axes, [(i, i ^ (d << shift)) for i in range(count)])
            for d in range(1, slots)
        ]
        ordered = []
        for j in range(slots):
            value = jnp.zeros_like(x)
            for d in range(slots):
                value = jnp.where((position ^ d) == j, received[d], value)
            ordered.append(value)
        while len(ordered) > 1:
            ordered = [ordered[k] + ordered[k + 1] for k in range(0, len(ordered), 2)]
        x = ordered[0]
        shift += width
    return x


def group_stats(values):
    channels = values.shape[-1]
    group_width = channels // GROUPS
    grouped = values.reshape(-1, GROUPS, group_width)
    entries = (
        grouped.shape[0]
        * group_width
        * lax.axis_size("ha")
        * lax.axis_size("wa")
        * lax.axis_size("ta")
    )
    totals, squares = group_allreduce(
        jnp.stack([jnp.sum(grouped, axis=(0, 2)), jnp.sum(grouped * grouped, axis=(0, 2))]),
        ("ha", "wa", "ta"),
    )
    average = totals / entries
    spread = squares / entries - average * average
    scaling = lax.rsqrt(spread + EPSILON)
    return jnp.repeat(average, group_width), jnp.repeat(scaling, group_width)


def activate(values, stats, scale_vec, shift_vec):
    average, scaling = stats
    normed = (values - average) * scaling * scale_vec + shift_vec
    return jax.nn.silu(normed)


def inside_mask(rows, cols, low_pad):
    h, h_last = lax.axis_index("ha"), lax.axis_size("ha") - 1
    w, w_last = lax.axis_index("wa"), lax.axis_size("wa") - 1
    r = jnp.arange(rows)
    c = jnp.arange(cols)
    row_ok = jnp.logical_and(
        jnp.logical_or(r >= low_pad, h > 0), jnp.logical_or(r < rows - 1, h < h_last)
    )
    col_ok = jnp.logical_and(
        jnp.logical_or(c >= low_pad, w > 0), jnp.logical_or(c < cols - 1, w < w_last)
    )
    return jnp.logical_and(row_ok[:, None], col_ok[None, :])[None, :, :, None]


def latent_halo(x):
    h_size, w_size = lax.axis_size("ha"), lax.axis_size("wa")
    below = passed_along(x[:, :1], "ha", -1)
    right = passed_along(x[:, :, :1], "wa", -1)
    corner_route = [
        ((h + 1) * w_size + w + 1, h * w_size + w)
        for h in range(h_size - 1)
        for w in range(w_size - 1)
    ]
    corner = lax.ppermute(x[:, :1, :1], ("ha", "wa"), corner_route)
    top = jnp.concatenate([x, right], axis=2)
    bottom = jnp.concatenate([below, corner], axis=2)
    return jnp.concatenate([top, bottom], axis=1)


def upsample(act, kernel):
    frames, rows, cols, channels = act.shape
    height, across = rows - 1, cols - 1
    flat = lambda v: v.reshape(-1, channels)
    dot = lambda v, w: jnp.dot(flat(v), w, preferred_element_type=jnp.float32)
    a = act[:, :height, :across]
    b = act[:, :height, 1:]
    c = act[:, 1:, :across]
    d = act[:, 1:, 1:]
    out = kernel.shape[-1]
    pa = dot(a, jnp.concatenate([kernel[1, 1], kernel[1, 2], kernel[2, 1], kernel[2, 2]], axis=1))
    pb = dot(b, jnp.concatenate([kernel[1, 0], kernel[2, 0]], axis=1))
    pc = dot(c, jnp.concatenate([kernel[0, 1], kernel[0, 2]], axis=1))
    pd = dot(d, kernel[0, 0])
    ee = pa[:, :out]
    eo = pa[:, out : 2 * out] + pb[:, :out]
    oe = pa[:, 2 * out : 3 * out] + pc[:, :out]
    oo = pa[:, 3 * out :] + pb[:, out:] + pc[:, out:] + pd
    shape = (frames, height, across, 1, out)
    even = jnp.concatenate([ee.reshape(shape), eo.reshape(shape)], axis=3)
    odd = jnp.concatenate([oe.reshape(shape), oo.reshape(shape)], axis=3)
    even = even.reshape(frames, height, 1, 2 * across, out)
    odd = odd.reshape(frames, height, 1, 2 * across, out)
    return jnp.concatenate([even, odd], axis=2).reshape(frames, 2 * height, 2 * across, out)


def valid_conv(padded, kernel, frames, height, across):
    channels = padded.shape[-1]
    wide = jnp.concatenate(
        [padded[:, dy : dy + height, dx : dx + across] for dy in range(3) for dx in range(3)], axis=-1
    )
    result = None
    for step_t in range(3):
        window = wide[step_t : step_t + frames].reshape(-1, 9 * channels)
        part = jnp.dot(
            window, kernel[step_t].reshape(9 * channels, -1), preferred_element_type=jnp.float32
        )
        result = part if result is None else result + part
    return result.reshape(frames, height, across, -1)


def conv_halo(values):
    x = padded_2(values, (("ha", 1), ("wa", 2)), 1)
    earlier = passed_along(x[-2:], "ta", 1)
    opening = jnp.concatenate([x[:1], x[:1]], axis=0)
    earlier = jnp.where(lax.axis_index("ta") == 0, opening, earlier)
    return jnp.concatenate([earlier, x], axis=0)


def norm_conv(values, gain, shift, kernel):
    frames, height, across, _ = values.shape
    values_f = values.astype(jnp.float32)
    stats = group_stats(values_f)
    extended = conv_halo(values).astype(jnp.float32)
    act = activate(extended, stats, gain, shift)
    act = jnp.where(inside_mask(height + 2, across + 2, 1), act, 0.0).astype(jnp.bfloat16)
    return valid_conv(act, kernel, frames, height, across)


def per_device(
    latents,
    norm1_gain,
    norm1_shift,
    up_weight,
    norm2_gain,
    norm2_shift,
    conv_a,
    norm3_gain,
    norm3_shift,
    conv_b,
):
    frames, height, across, channels = latents.shape
    stats = group_stats(latents.astype(jnp.float32))
    extended = latent_halo(latents).astype(jnp.float32)
    activated = activate(extended, stats, norm1_gain, norm1_shift)
    activated = jnp.where(inside_mask(height + 1, across + 1, 0), activated, 0.0)
    lifted = upsample(activated.astype(jnp.bfloat16), up_weight).astype(jnp.bfloat16)
    hidden = norm_conv(lifted, norm2_gain, norm2_shift, conv_a).astype(jnp.bfloat16)
    branch = norm_conv(hidden, norm3_gain, norm3_shift, conv_b)
    return (lifted.astype(jnp.float32) + branch).astype(jnp.bfloat16)


def solution(mesh):
    return jax.shard_map(
        per_device,
        mesh=mesh,
        in_specs=(
            P(("videos", "ta"), "ha", "wa", None),
            P(),
            P(),
            P(),
            P(),
            P(),
            P(),
            P(),
            P(),
            P(),
        ),
        out_specs=P(("videos", "ta"), "ha", "wa", None),
        check_vma=False,
    )
```

```python
import jax
import jax.numpy as jnp
from jax import lax
from jax.sharding import PartitionSpec as P

GROUPS = 32


EPSILON = 1e-06


def passed_along(block, axis, distance):
    devices = range(lax.axis_size(axis))
    route = [(i - distance, i) for i in devices if i - distance in devices]
    return lax.ppermute(block, axis, route)


def padded_2(x, sides, width):
    for axis, dim in sides:
        size, length = (lax.axis_size(axis), x.shape[dim])
        up = [(i, (i + 1) % size) for i in range(size - 1)]
        down = [(j, i) for i, j in up]
        last = lax.slice_in_dim(x, length - width, length, axis=dim)
        initial = lax.slice_in_dim(x, 0, width, axis=dim)
        before = lax.ppermute(last, axis, up)
        after = lax.ppermute(initial, axis, down)
        x = jnp.concatenate([before, x, after], axis=dim)
    return x


def group_allreduce(x, axes):
    sizes = [lax.axis_size(a) for a in axes]
    count = 1
    for s in sizes:
        count *= s
    if count & (count - 1):
        return lax.psum(x, axes)
    index = 0
    for a, s in zip(axes, sizes):
        index = index * s + lax.axis_index(a)
    shift = 0
    while (1 << shift) < count:
        width = min(2, (count.bit_length() - 1) - shift)
        slots = 1 << width
        position = (index >> shift) % slots
        received = [x] + [
            lax.ppermute(x, axes, [(i, i ^ (d << shift)) for i in range(count)])
            for d in range(1, slots)
        ]
        ordered = []
        for j in range(slots):
            value = jnp.zeros_like(x)
            for d in range(slots):
                value = jnp.where((position ^ d) == j, received[d], value)
            ordered.append(value)
        while len(ordered) > 1:
            ordered = [ordered[k] + ordered[k + 1] for k in range(0, len(ordered), 2)]
        x = ordered[0]
        shift += width
    return x


def group_stats(values):
    channels = values.shape[-1]
    group_width = channels // GROUPS
    grouped = values.reshape(-1, GROUPS, group_width)
    entries = (
        grouped.shape[0]
        * group_width
        * lax.axis_size("ha")
        * lax.axis_size("wa")
        * lax.axis_size("ta")
    )
    totals, squares = group_allreduce(
        jnp.stack([jnp.sum(grouped, axis=(0, 2)), jnp.sum(grouped * grouped, axis=(0, 2))]),
        ("ha", "wa", "ta"),
    )
    average = totals / entries
    spread = squares / entries - average * average
    scaling = lax.rsqrt(spread + EPSILON)
    return jnp.repeat(average, group_width), jnp.repeat(scaling, group_width)


def activate(values, stats, scale_vec, shift_vec):
    average, scaling = stats
    normed = (values - average) * scaling * scale_vec + shift_vec
    return jax.nn.silu(normed)


def inside_mask(rows, cols, low_pad):
    h, h_last = lax.axis_index("ha"), lax.axis_size("ha") - 1
    w, w_last = lax.axis_index("wa"), lax.axis_size("wa") - 1
    r = jnp.arange(rows)
    c = jnp.arange(cols)
    row_ok = jnp.logical_and(
        jnp.logical_or(r >= low_pad, h > 0), jnp.logical_or(r < rows - 1, h < h_last)
    )
    col_ok = jnp.logical_and(
        jnp.logical_or(c >= low_pad, w > 0), jnp.logical_or(c < cols - 1, w < w_last)
    )
    return jnp.logical_and(row_ok[:, None], col_ok[None, :])[None, :, :, None]


def latent_halo(x):
    h_size, w_size = lax.axis_size("ha"), lax.axis_size("wa")
    below = passed_along(x[:, :1], "ha", -1)
    right = passed_along(x[:, :, :1], "wa", -1)
    corner_route = [
        ((h + 1) * w_size + w + 1, h * w_size + w)
        for h in range(h_size - 1)
        for w in range(w_size - 1)
    ]
    corner = lax.ppermute(x[:, :1, :1], ("ha", "wa"), corner_route)
    top = jnp.concatenate([x, right], axis=2)
    bottom = jnp.concatenate([below, corner], axis=2)
    return jnp.concatenate([top, bottom], axis=1)


def upsample(act, kernel):
    frames, rows, cols, channels = act.shape
    height, across = rows - 1, cols - 1
    flat = lambda v: v.reshape(-1, channels)
    dot = lambda v, w: jnp.dot(flat(v), w, preferred_element_type=jnp.float32)
    a = act[:, :height, :across]
    b = act[:, :height, 1:]
    c = act[:, 1:, :across]
    d = act[:, 1:, 1:]
    out = kernel.shape[-1]
    pa = dot(a, jnp.concatenate([kernel[1, 1], kernel[1, 2], kernel[2, 1], kernel[2, 2]], axis=1))
    pb = dot(b, jnp.concatenate([kernel[1, 0], kernel[2, 0]], axis=1))
    pc = dot(c, jnp.concatenate([kernel[0, 1], kernel[0, 2]], axis=1))
    pd = dot(d, kernel[0, 0])
    ee = pa[:, :out]
    eo = pa[:, out : 2 * out] + pb[:, :out]
    oe = pa[:, 2 * out : 3 * out] + pc[:, :out]
    oo = pa[:, 3 * out :] + pb[:, out:] + pc[:, out:] + pd
    shape = (frames, height, across, 1, out)
    even = jnp.concatenate([ee.reshape(shape), eo.reshape(shape)], axis=3)
    odd = jnp.concatenate([oe.reshape(shape), oo.reshape(shape)], axis=3)
    even = even.reshape(frames, height, 1, 2 * across, out)
    odd = odd.reshape(frames, height, 1, 2 * across, out)
    return jnp.concatenate([even, odd], axis=2).reshape(frames, 2 * height, 2 * across, out)


def valid_conv(padded, kernel, frames, height, across):
    channels = padded.shape[-1]
    wide = jnp.concatenate(
        [padded[:, dy : dy + height, dx : dx + across] for dy in range(3) for dx in range(3)], axis=-1
    )
    result = None
    for step_t in range(3):
        window = wide[step_t : step_t + frames].reshape(-1, 9 * channels)
        part = jnp.dot(
            window, kernel[step_t].reshape(9 * channels, -1), preferred_element_type=jnp.float32
        )
        result = part if result is None else result + part
    return result.reshape(frames, height, across, -1)


def conv_halo(values):
    x = padded_2(values, (("ha", 1), ("wa", 2)), 1)
    earlier = passed_along(x[-2:], "ta", 1)
    opening = jnp.concatenate([x[:1], x[:1]], axis=0)
    earlier = jnp.where(lax.axis_index("ta") == 0, opening, earlier)
    return jnp.concatenate([earlier, x], axis=0)


def swap(x, axis, distance):
    size = lax.axis_size(axis)
    return lax.ppermute(x, axis, [(i, i ^ distance) for i in range(size)])


def fast_mesh():
    return lax.axis_size("ta") == 2 and lax.axis_size("wa") == 2 and lax.axis_size("ha") == 4


def local_sums(values):
    grouped = values.reshape(-1, GROUPS, values.shape[-1] // GROUPS)
    return jnp.stack([jnp.sum(grouped, axis=(0, 2)), jnp.sum(grouped * grouped, axis=(0, 2))])


def finish_stats(sums, values):
    channels = values.shape[-1]
    group_width = channels // GROUPS
    entries = (
        values.size // GROUPS
        * lax.axis_size("ha")
        * lax.axis_size("wa")
        * lax.axis_size("ta")
    )
    average = sums[0] / entries
    spread = sums[1] / entries - average * average
    scaling = lax.rsqrt(spread + EPSILON)
    return jnp.repeat(average, group_width), jnp.repeat(scaling, group_width)


def pack_sums(sums, width):
    high = sums.astype(jnp.bfloat16)
    rest = sums - high.astype(jnp.float32)
    middle = rest.astype(jnp.bfloat16)
    low = (rest - middle.astype(jnp.float32)).astype(jnp.bfloat16)
    flat = jnp.concatenate([high.reshape(-1), middle.reshape(-1), low.reshape(-1)])
    rows = -(-flat.size // width)
    return jnp.pad(flat, (0, rows * width - flat.size)).reshape(rows, width)


def unpack_sums(rows, like):
    flat = rows.reshape(-1)[: 3 * like.size].astype(jnp.float32).reshape(3, *like.shape)
    return (flat[0] + flat[1]) + flat[2]


def swap_with(sums, payload, axis, distance):
    width = payload.shape[-1]
    packed = pack_sums(sums, width)
    message = jnp.concatenate([payload.reshape(-1, width), packed], axis=0)
    got = swap(message, axis, distance)
    cut = got.shape[0] - packed.shape[0]
    return unpack_sums(got[cut:], sums), got[:cut].reshape(payload.shape)


def ha_round(sums, upper, lower):
    h = lax.axis_index("ha")
    to_first = jnp.where(h % 2 == 1, upper, lower)
    to_third = jnp.where(h == 2, upper, lower)
    s1, got_first = swap_with(sums, to_first, "ha", 1)
    s2 = swap(sums, "ha", 2)
    s3, got_third = swap_with(sums, to_third, "ha", 3)
    sums = (sums + s1) + (s2 + s3)
    above = jnp.where(h % 2 == 1, got_first, got_third)
    below = jnp.where(h % 2 == 0, got_first, got_third)
    return sums, above, below


def fast_conv_input(values):
    sums = local_sums(values.astype(jnp.float32))
    s_t, earlier = swap_with(sums, values[-2:], "ta", 1)
    sums = sums + s_t
    opening = jnp.concatenate([values[:1], values[:1]], axis=0)
    earlier = jnp.where(lax.axis_index("ta") == 0, opening, earlier)
    x = jnp.concatenate([earlier, values], axis=0)
    w = lax.axis_index("wa")
    s_w, beside = swap_with(sums, jnp.where(w == 0, x[:, :, -1:], x[:, :, :1]), "wa", 1)
    sums = sums + s_w
    x = jnp.concatenate([beside, x, beside], axis=2)
    sums, above, below = ha_round(sums, x[:, :1], x[:, -1:])
    x = jnp.concatenate([above, x, below], axis=1)
    return finish_stats(sums, values), x


def fast_latent_input(values):
    sums = local_sums(values.astype(jnp.float32))
    sums = sums + swap(sums, "ta", 1)
    s_w, beside = swap_with(sums, values[:, :, :1], "wa", 1)
    sums = sums + s_w
    x = jnp.concatenate([values, beside], axis=2)
    sums, _, below = ha_round(sums, x[:, :1], x[:, :1])
    x = jnp.concatenate([x, below], axis=1)
    return finish_stats(sums, values), x


def norm_conv(values, gain, shift, kernel):
    frames, height, across, _ = values.shape
    if fast_mesh():
        stats, extended = fast_conv_input(values)
    else:
        stats = group_stats(values.astype(jnp.float32))
        extended = conv_halo(values)
    act = activate(extended.astype(jnp.float32), stats, gain, shift)
    act = jnp.where(inside_mask(height + 2, across + 2, 1), act, 0.0).astype(jnp.bfloat16)
    return valid_conv(act, kernel, frames, height, across)


def per_device(
    latents,
    norm1_gain,
    norm1_shift,
    up_weight,
    norm2_gain,
    norm2_shift,
    conv_a,
    norm3_gain,
    norm3_shift,
    conv_b,
):
    frames, height, across, channels = latents.shape
    if fast_mesh():
        stats, extended = fast_latent_input(latents)
    else:
        stats = group_stats(latents.astype(jnp.float32))
        extended = latent_halo(latents)
    activated = activate(extended.astype(jnp.float32), stats, norm1_gain, norm1_shift)
    activated = jnp.where(inside_mask(height + 1, across + 1, 0), activated, 0.0)
    lifted = upsample(activated.astype(jnp.bfloat16), up_weight).astype(jnp.bfloat16)
    hidden = norm_conv(lifted, norm2_gain, norm2_shift, conv_a).astype(jnp.bfloat16)
    branch = norm_conv(hidden, norm3_gain, norm3_shift, conv_b)
    return (lifted.astype(jnp.float32) + branch).astype(jnp.bfloat16)


def solution(mesh):
    return jax.shard_map(
        per_device,
        mesh=mesh,
        in_specs=(
            P(("videos", "ta"), "ha", "wa", None),
            P(),
            P(),
            P(),
            P(),
            P(),
            P(),
            P(),
            P(),
            P(),
        ),
        out_specs=P(("videos", "ta"), "ha", "wa", None),
        check_vma=False,
    )
```

```python
import jax
import jax.numpy as jnp
from jax import lax
from jax.sharding import PartitionSpec as P

GROUPS = 32


EPSILON = 1e-06


def passed_along(block, axis, distance):
    devices = range(lax.axis_size(axis))
    route = [(i - distance, i) for i in devices if i - distance in devices]
    return lax.ppermute(block, axis, route)


def padded_2(x, sides, width):
    for axis, dim in sides:
        size, length = (lax.axis_size(axis), x.shape[dim])
        up = [(i, (i + 1) % size) for i in range(size - 1)]
        down = [(j, i) for i, j in up]
        last = lax.slice_in_dim(x, length - width, length, axis=dim)
        initial = lax.slice_in_dim(x, 0, width, axis=dim)
        before = lax.ppermute(last, axis, up)
        after = lax.ppermute(initial, axis, down)
        x = jnp.concatenate([before, x, after], axis=dim)
    return x


def group_allreduce(x, axes):
    sizes = [lax.axis_size(a) for a in axes]
    count = 1
    for s in sizes:
        count *= s
    if count & (count - 1):
        return lax.psum(x, axes)
    index = 0
    for a, s in zip(axes, sizes):
        index = index * s + lax.axis_index(a)
    shift = 0
    while (1 << shift) < count:
        width = min(2, (count.bit_length() - 1) - shift)
        slots = 1 << width
        position = (index >> shift) % slots
        received = [x] + [
            lax.ppermute(x, axes, [(i, i ^ (d << shift)) for i in range(count)])
            for d in range(1, slots)
        ]
        ordered = []
        for j in range(slots):
            value = jnp.zeros_like(x)
            for d in range(slots):
                value = jnp.where((position ^ d) == j, received[d], value)
            ordered.append(value)
        while len(ordered) > 1:
            ordered = [ordered[k] + ordered[k + 1] for k in range(0, len(ordered), 2)]
        x = ordered[0]
        shift += width
    return x


def group_stats(values):
    channels = values.shape[-1]
    group_width = channels // GROUPS
    grouped = values.reshape(-1, GROUPS, group_width)
    entries = (
        grouped.shape[0]
        * group_width
        * lax.axis_size("ha")
        * lax.axis_size("wa")
        * lax.axis_size("ta")
    )
    totals, squares = group_allreduce(
        jnp.stack([jnp.sum(grouped, axis=(0, 2)), jnp.sum(grouped * grouped, axis=(0, 2))]),
        ("ha", "wa", "ta"),
    )
    average = totals / entries
    spread = squares / entries - average * average
    scaling = lax.rsqrt(spread + EPSILON)
    return jnp.repeat(average, group_width), jnp.repeat(scaling, group_width)


def activate(values, stats, scale_vec, shift_vec):
    average, scaling = stats
    normed = (values - average) * scaling * scale_vec + shift_vec
    return jax.nn.silu(normed)


def inside_mask(rows, cols, low_pad):
    h, h_last = lax.axis_index("ha"), lax.axis_size("ha") - 1
    w, w_last = lax.axis_index("wa"), lax.axis_size("wa") - 1
    r = jnp.arange(rows)
    c = jnp.arange(cols)
    row_ok = jnp.logical_and(
        jnp.logical_or(r >= low_pad, h > 0), jnp.logical_or(r < rows - 1, h < h_last)
    )
    col_ok = jnp.logical_and(
        jnp.logical_or(c >= low_pad, w > 0), jnp.logical_or(c < cols - 1, w < w_last)
    )
    return jnp.logical_and(row_ok[:, None], col_ok[None, :])[None, :, :, None]


def latent_halo(x):
    h_size, w_size = lax.axis_size("ha"), lax.axis_size("wa")
    below = passed_along(x[:, :1], "ha", -1)
    right = passed_along(x[:, :, :1], "wa", -1)
    corner_route = [
        ((h + 1) * w_size + w + 1, h * w_size + w)
        for h in range(h_size - 1)
        for w in range(w_size - 1)
    ]
    corner = lax.ppermute(x[:, :1, :1], ("ha", "wa"), corner_route)
    top = jnp.concatenate([x, right], axis=2)
    bottom = jnp.concatenate([below, corner], axis=2)
    return jnp.concatenate([top, bottom], axis=1)


def upsample(act, kernel):
    frames, rows, cols, channels = act.shape
    height, across = rows - 1, cols - 1
    flat = lambda v: v.reshape(-1, channels)
    dot = lambda v, w: jnp.dot(flat(v), w, preferred_element_type=jnp.float32)
    a = act[:, :height, :across]
    b = act[:, :height, 1:]
    c = act[:, 1:, :across]
    d = act[:, 1:, 1:]
    out = kernel.shape[-1]
    pa = dot(a, jnp.concatenate([kernel[1, 1], kernel[1, 2], kernel[2, 1], kernel[2, 2]], axis=1))
    pb = dot(b, jnp.concatenate([kernel[1, 0], kernel[2, 0]], axis=1))
    pc = dot(c, jnp.concatenate([kernel[0, 1], kernel[0, 2]], axis=1))
    pd = dot(d, kernel[0, 0])
    ee = pa[:, :out]
    eo = pa[:, out : 2 * out] + pb[:, :out]
    oe = pa[:, 2 * out : 3 * out] + pc[:, :out]
    oo = pa[:, 3 * out :] + pb[:, out:] + pc[:, out:] + pd
    shape = (frames, height, across, 1, out)
    even = jnp.concatenate([ee.reshape(shape), eo.reshape(shape)], axis=3)
    odd = jnp.concatenate([oe.reshape(shape), oo.reshape(shape)], axis=3)
    even = even.reshape(frames, height, 1, 2 * across, out)
    odd = odd.reshape(frames, height, 1, 2 * across, out)
    return jnp.concatenate([even, odd], axis=2).reshape(frames, 2 * height, 2 * across, out)


def valid_conv(padded, kernel, frames, height, across):
    channels = padded.shape[-1]
    wide = jnp.concatenate(
        [padded[:, dy : dy + height, dx : dx + across] for dy in range(3) for dx in range(3)], axis=-1
    )
    result = None
    for step_t in range(3):
        window = wide[step_t : step_t + frames].reshape(-1, 9 * channels)
        part = jnp.dot(
            window, kernel[step_t].reshape(9 * channels, -1), preferred_element_type=jnp.float32
        )
        result = part if result is None else result + part
    return result.reshape(frames, height, across, -1)


def conv_halo(values):
    x = padded_2(values, (("ha", 1), ("wa", 2)), 1)
    earlier = passed_along(x[-2:], "ta", 1)
    opening = jnp.concatenate([x[:1], x[:1]], axis=0)
    earlier = jnp.where(lax.axis_index("ta") == 0, opening, earlier)
    return jnp.concatenate([earlier, x], axis=0)


def swap(x, axis, distance):
    size = lax.axis_size(axis)
    return lax.ppermute(x, axis, [(i, i ^ distance) for i in range(size)])


def fast_mesh():
    return lax.axis_size("ta") == 2 and lax.axis_size("wa") == 2 and lax.axis_size("ha") == 4


def local_sums(values):
    grouped = values.reshape(-1, GROUPS, values.shape[-1] // GROUPS)
    return jnp.stack([jnp.sum(grouped, axis=(0, 2)), jnp.sum(grouped * grouped, axis=(0, 2))])


def finish_stats(sums, values):
    channels = values.shape[-1]
    group_width = channels // GROUPS
    entries = (
        values.size // GROUPS
        * lax.axis_size("ha")
        * lax.axis_size("wa")
        * lax.axis_size("ta")
    )
    average = sums[0] / entries
    spread = sums[1] / entries - average * average
    scaling = lax.rsqrt(spread + EPSILON)
    return jnp.repeat(average, group_width), jnp.repeat(scaling, group_width)


def split_high(value):
    scaled = value * 65537.0
    return scaled - (scaled - value)


def pack_sums(sums, width):
    high = split_high(sums)
    rest = sums - high
    middle = split_high(rest)
    low = rest - middle
    flat = jnp.concatenate([high.reshape(-1), middle.reshape(-1), low.reshape(-1)])
    flat = flat.astype(jnp.bfloat16)
    rows = -(-flat.size // width)
    return jnp.pad(flat, (0, rows * width - flat.size)).reshape(rows, width)


def unpack_sums(rows, like):
    flat = rows.reshape(-1)[: 3 * like.size].astype(jnp.float32).reshape(3, *like.shape)
    return (flat[0] + flat[1]) + flat[2]


def swap_with(sums, payload, axis, distance):
    width = payload.shape[-1]
    packed = pack_sums(sums, width)
    message = jnp.concatenate([payload.reshape(-1, width), packed], axis=0)
    got = swap(message, axis, distance)
    cut = got.shape[0] - packed.shape[0]
    return unpack_sums(got[cut:], sums), got[:cut].reshape(payload.shape)


def ha_round(sums, upper, lower):
    h = lax.axis_index("ha")
    to_first = jnp.where(h % 2 == 1, upper, lower)
    to_third = jnp.where(h == 2, upper, lower)
    s1, got_first = swap_with(sums, to_first, "ha", 1)
    s2 = swap(sums, "ha", 2)
    s3, got_third = swap_with(sums, to_third, "ha", 3)
    sums = (sums + s1) + (s2 + s3)
    above = jnp.where(h % 2 == 1, got_first, got_third)
    below = jnp.where(h % 2 == 0, got_first, got_third)
    return sums, above, below


def fast_conv_input(values):
    sums = local_sums(values.astype(jnp.float32))
    s_t, earlier = swap_with(sums, values[-2:], "ta", 1)
    sums = sums + s_t
    opening = jnp.concatenate([values[:1], values[:1]], axis=0)
    earlier = jnp.where(lax.axis_index("ta") == 0, opening, earlier)
    x = jnp.concatenate([earlier, values], axis=0)
    w = lax.axis_index("wa")
    s_w, beside = swap_with(sums, jnp.where(w == 0, x[:, :, -1:], x[:, :, :1]), "wa", 1)
    sums = sums + s_w
    x = jnp.concatenate([beside, x, beside], axis=2)
    sums, above, below = ha_round(sums, x[:, :1], x[:, -1:])
    x = jnp.concatenate([above, x, below], axis=1)
    return finish_stats(sums, values), x


def fast_latent_input(values):
    sums = local_sums(values.astype(jnp.float32))
    sums = sums + swap(sums, "ta", 1)
    s_w, beside = swap_with(sums, values[:, :, :1], "wa", 1)
    sums = sums + s_w
    x = jnp.concatenate([values, beside], axis=2)
    sums, _, below = ha_round(sums, x[:, :1], x[:, :1])
    x = jnp.concatenate([x, below], axis=1)
    return finish_stats(sums, values), x


def norm_conv(values, gain, shift, kernel):
    frames, height, across, _ = values.shape
    if fast_mesh():
        stats, extended = fast_conv_input(values)
    else:
        stats = group_stats(values.astype(jnp.float32))
        extended = conv_halo(values)
    act = activate(extended.astype(jnp.float32), stats, gain, shift)
    act = jnp.where(inside_mask(height + 2, across + 2, 1), act, 0.0).astype(jnp.bfloat16)
    return valid_conv(act, kernel, frames, height, across)


def per_device(
    latents,
    norm1_gain,
    norm1_shift,
    up_weight,
    norm2_gain,
    norm2_shift,
    conv_a,
    norm3_gain,
    norm3_shift,
    conv_b,
):
    frames, height, across, channels = latents.shape
    if fast_mesh():
        stats, extended = fast_latent_input(latents)
    else:
        stats = group_stats(latents.astype(jnp.float32))
        extended = latent_halo(latents)
    activated = activate(extended.astype(jnp.float32), stats, norm1_gain, norm1_shift)
    activated = jnp.where(inside_mask(height + 1, across + 1, 0), activated, 0.0)
    lifted = upsample(activated.astype(jnp.bfloat16), up_weight).astype(jnp.bfloat16)
    hidden = norm_conv(lifted, norm2_gain, norm2_shift, conv_a).astype(jnp.bfloat16)
    branch = norm_conv(hidden, norm3_gain, norm3_shift, conv_b)
    return (lifted.astype(jnp.float32) + branch).astype(jnp.bfloat16)


def solution(mesh):
    return jax.shard_map(
        per_device,
        mesh=mesh,
        in_specs=(
            P(("videos", "ta"), "ha", "wa", None),
            P(),
            P(),
            P(),
            P(),
            P(),
            P(),
            P(),
            P(),
            P(),
        ),
        out_specs=P(("videos", "ta"), "ha", "wa", None),
        check_vma=False,
    )
```

```python
import jax
import jax.numpy as jnp
from jax import lax
from jax.sharding import PartitionSpec as P

GROUPS = 32


EPSILON = 1e-06


def passed_along(block, axis, distance):
    devices = range(lax.axis_size(axis))
    route = [(i - distance, i) for i in devices if i - distance in devices]
    return lax.ppermute(block, axis, route)


def padded_2(x, sides, width):
    for axis, dim in sides:
        size, length = (lax.axis_size(axis), x.shape[dim])
        up = [(i, (i + 1) % size) for i in range(size - 1)]
        down = [(j, i) for i, j in up]
        last = lax.slice_in_dim(x, length - width, length, axis=dim)
        initial = lax.slice_in_dim(x, 0, width, axis=dim)
        before = lax.ppermute(last, axis, up)
        after = lax.ppermute(initial, axis, down)
        x = jnp.concatenate([before, x, after], axis=dim)
    return x


def group_allreduce(x, axes):
    sizes = [lax.axis_size(a) for a in axes]
    count = 1
    for s in sizes:
        count *= s
    if count & (count - 1):
        return lax.psum(x, axes)
    index = 0
    for a, s in zip(axes, sizes):
        index = index * s + lax.axis_index(a)
    shift = 0
    while (1 << shift) < count:
        width = min(2, (count.bit_length() - 1) - shift)
        slots = 1 << width
        position = (index >> shift) % slots
        received = [x] + [
            lax.ppermute(x, axes, [(i, i ^ (d << shift)) for i in range(count)])
            for d in range(1, slots)
        ]
        ordered = []
        for j in range(slots):
            value = jnp.zeros_like(x)
            for d in range(slots):
                value = jnp.where((position ^ d) == j, received[d], value)
            ordered.append(value)
        while len(ordered) > 1:
            ordered = [ordered[k] + ordered[k + 1] for k in range(0, len(ordered), 2)]
        x = ordered[0]
        shift += width
    return x


def group_stats(values):
    channels = values.shape[-1]
    group_width = channels // GROUPS
    grouped = values.reshape(-1, GROUPS, group_width)
    entries = (
        grouped.shape[0]
        * group_width
        * lax.axis_size("ha")
        * lax.axis_size("wa")
        * lax.axis_size("ta")
    )
    totals, squares = group_allreduce(
        jnp.stack([jnp.sum(grouped, axis=(0, 2)), jnp.sum(grouped * grouped, axis=(0, 2))]),
        ("ha", "wa", "ta"),
    )
    average = totals / entries
    spread = squares / entries - average * average
    scaling = lax.rsqrt(spread + EPSILON)
    return jnp.repeat(average, group_width), jnp.repeat(scaling, group_width)


def activate(values, stats, scale_vec, shift_vec):
    average, scaling = stats
    normed = (values - average) * scaling * scale_vec + shift_vec
    return jax.nn.silu(normed)


def inside_mask(rows, cols, low_pad):
    h, h_last = lax.axis_index("ha"), lax.axis_size("ha") - 1
    w, w_last = lax.axis_index("wa"), lax.axis_size("wa") - 1
    r = jnp.arange(rows)
    c = jnp.arange(cols)
    row_ok = jnp.logical_and(
        jnp.logical_or(r >= low_pad, h > 0), jnp.logical_or(r < rows - 1, h < h_last)
    )
    col_ok = jnp.logical_and(
        jnp.logical_or(c >= low_pad, w > 0), jnp.logical_or(c < cols - 1, w < w_last)
    )
    return jnp.logical_and(row_ok[:, None], col_ok[None, :])[None, :, :, None]


def latent_halo(x):
    h_size, w_size = lax.axis_size("ha"), lax.axis_size("wa")
    below = passed_along(x[:, :1], "ha", -1)
    right = passed_along(x[:, :, :1], "wa", -1)
    corner_route = [
        ((h + 1) * w_size + w + 1, h * w_size + w)
        for h in range(h_size - 1)
        for w in range(w_size - 1)
    ]
    corner = lax.ppermute(x[:, :1, :1], ("ha", "wa"), corner_route)
    top = jnp.concatenate([x, right], axis=2)
    bottom = jnp.concatenate([below, corner], axis=2)
    return jnp.concatenate([top, bottom], axis=1)


def upsample(act, kernel):
    frames, rows, cols, channels = act.shape
    height, across = rows - 1, cols - 1
    flat = lambda v: v.reshape(-1, channels)
    dot = lambda v, w: jnp.dot(flat(v), w, preferred_element_type=jnp.float32)
    a = act[:, :height, :across]
    b = act[:, :height, 1:]
    c = act[:, 1:, :across]
    d = act[:, 1:, 1:]
    out = kernel.shape[-1]
    pa = dot(a, jnp.concatenate([kernel[1, 1], kernel[1, 2], kernel[2, 1], kernel[2, 2]], axis=1))
    pb = dot(b, jnp.concatenate([kernel[1, 0], kernel[2, 0]], axis=1))
    pc = dot(c, jnp.concatenate([kernel[0, 1], kernel[0, 2]], axis=1))
    pd = dot(d, kernel[0, 0])
    ee = pa[:, :out]
    eo = pa[:, out : 2 * out] + pb[:, :out]
    oe = pa[:, 2 * out : 3 * out] + pc[:, :out]
    oo = pa[:, 3 * out :] + pb[:, out:] + pc[:, out:] + pd
    shape = (frames, height, across, 1, out)
    even = jnp.concatenate([ee.reshape(shape), eo.reshape(shape)], axis=3)
    odd = jnp.concatenate([oe.reshape(shape), oo.reshape(shape)], axis=3)
    even = even.reshape(frames, height, 1, 2 * across, out)
    odd = odd.reshape(frames, height, 1, 2 * across, out)
    return jnp.concatenate([even, odd], axis=2).reshape(frames, 2 * height, 2 * across, out)


def valid_conv(padded, kernel, frames, height, across):
    channels = padded.shape[-1]
    wide = jnp.concatenate(
        [padded[:, dy : dy + height, dx : dx + across] for dy in range(3) for dx in range(3)], axis=-1
    )
    result = None
    for step_t in range(3):
        window = wide[step_t : step_t + frames].reshape(-1, 9 * channels)
        part = jnp.dot(
            window, kernel[step_t].reshape(9 * channels, -1), preferred_element_type=jnp.float32
        )
        result = part if result is None else result + part
    return result.reshape(frames, height, across, -1)


def conv_halo(values):
    x = padded_2(values, (("ha", 1), ("wa", 2)), 1)
    earlier = passed_along(x[-2:], "ta", 1)
    opening = jnp.concatenate([x[:1], x[:1]], axis=0)
    earlier = jnp.where(lax.axis_index("ta") == 0, opening, earlier)
    return jnp.concatenate([earlier, x], axis=0)


def swap(x, axis, distance):
    size = lax.axis_size(axis)
    return lax.ppermute(x, axis, [(i, i ^ distance) for i in range(size)])


def fast_mesh():
    return lax.axis_size("ta") == 2 and lax.axis_size("wa") == 2 and lax.axis_size("ha") == 4


def local_sums(values):
    channels = values.shape[-1]
    flat = values.reshape(-1, channels)
    per_channel = jnp.stack([jnp.sum(flat, axis=0), jnp.sum(flat * flat, axis=0)])
    return jnp.sum(per_channel.reshape(2, GROUPS, channels // GROUPS), axis=2)


def finish_stats(sums, values):
    channels = values.shape[-1]
    group_width = channels // GROUPS
    entries = (
        values.size // GROUPS
        * lax.axis_size("ha")
        * lax.axis_size("wa")
        * lax.axis_size("ta")
    )
    average = sums[0] / entries
    spread = sums[1] / entries - average * average
    scaling = lax.rsqrt(spread + EPSILON)
    return jnp.repeat(average, group_width), jnp.repeat(scaling, group_width)


def split_high(value):
    scaled = value * 65537.0
    return scaled - (scaled - value)


def pack_sums(sums, width):
    high = split_high(sums)
    rest = sums - high
    middle = split_high(rest)
    low = rest - middle
    flat = jnp.concatenate([high.reshape(-1), middle.reshape(-1), low.reshape(-1)])
    flat = flat.astype(jnp.bfloat16)
    rows = -(-flat.size // width)
    return jnp.pad(flat, (0, rows * width - flat.size)).reshape(rows, width)


def unpack_sums(rows, like):
    flat = rows.reshape(-1)[: 3 * like.size].astype(jnp.float32).reshape(3, *like.shape)
    return (flat[0] + flat[1]) + flat[2]


def swap_with(sums, payload, axis, distance):
    width = payload.shape[-1]
    packed = pack_sums(sums, width)
    message = jnp.concatenate([payload.reshape(-1, width), packed], axis=0)
    got = swap(message, axis, distance)
    cut = got.shape[0] - packed.shape[0]
    return unpack_sums(got[cut:], sums), got[:cut].reshape(payload.shape)


def ha_round(sums, upper, lower):
    h = lax.axis_index("ha")
    s1, got_first = swap_with(sums, jnp.where(h % 2 == 1, upper, lower), "ha", 1)
    s2 = swap(sums, "ha", 2)
    inner = jnp.where(h == 2, upper, lower)
    width = inner.shape[-1]
    packed = pack_sums(sums, width)
    message = jnp.concatenate([inner.reshape(-1, width), packed], axis=0)
    got = lax.ppermute(message, "ha", [(1, 2), (2, 1)])
    cut = got.shape[0] - packed.shape[0]
    got_inner = got[:cut].reshape(inner.shape)
    s_outer = lax.ppermute(sums, "ha", [(0, 3), (3, 0)])
    s3 = jnp.where(jnp.logical_or(h == 1, h == 2), unpack_sums(got[cut:], sums), s_outer)
    sums = (sums + s1) + (s2 + s3)
    above = jnp.where(h % 2 == 1, got_first, got_inner)
    below = jnp.where(h % 2 == 0, got_first, got_inner)
    return sums, above, below


def fast_conv_input(values):
    sums = local_sums(values.astype(jnp.float32))
    s_t, earlier = swap_with(sums, values[-2:], "ta", 1)
    sums = sums + s_t
    opening = jnp.concatenate([values[:1], values[:1]], axis=0)
    earlier = jnp.where(lax.axis_index("ta") == 0, opening, earlier)
    x = jnp.concatenate([earlier, values], axis=0)
    w = lax.axis_index("wa")
    s_w, beside = swap_with(sums, jnp.where(w == 0, x[:, :, -1:], x[:, :, :1]), "wa", 1)
    sums = sums + s_w
    x = jnp.concatenate([beside, x, beside], axis=2)
    sums, above, below = ha_round(sums, x[:, :1], x[:, -1:])
    x = jnp.concatenate([above, x, below], axis=1)
    return finish_stats(sums, values), x


def fast_latent_input(values):
    sums = local_sums(values.astype(jnp.float32))
    sums = sums + swap(sums, "ta", 1)
    s_w, beside = swap_with(sums, values[:, :, :1], "wa", 1)
    sums = sums + s_w
    x = jnp.concatenate([values, beside], axis=2)
    sums, _, below = ha_round(sums, x[:, :1], x[:, :1])
    x = jnp.concatenate([x, below], axis=1)
    return finish_stats(sums, values), x


def norm_conv(values, gain, shift, kernel):
    frames, height, across, _ = values.shape
    if fast_mesh():
        stats, extended = fast_conv_input(values)
    else:
        stats = group_stats(values.astype(jnp.float32))
        extended = conv_halo(values)
    act = activate(extended.astype(jnp.float32), stats, gain, shift)
    act = jnp.where(inside_mask(height + 2, across + 2, 1), act, 0.0).astype(jnp.bfloat16)
    return valid_conv(act, kernel, frames, height, across)


def per_device(
    latents,
    norm1_gain,
    norm1_shift,
    up_weight,
    norm2_gain,
    norm2_shift,
    conv_a,
    norm3_gain,
    norm3_shift,
    conv_b,
):
    frames, height, across, channels = latents.shape
    if fast_mesh():
        stats, extended = fast_latent_input(latents)
    else:
        stats = group_stats(latents.astype(jnp.float32))
        extended = latent_halo(latents)
    activated = activate(extended.astype(jnp.float32), stats, norm1_gain, norm1_shift)
    activated = jnp.where(inside_mask(height + 1, across + 1, 0), activated, 0.0)
    lifted = upsample(activated.astype(jnp.bfloat16), up_weight).astype(jnp.bfloat16)
    hidden = norm_conv(lifted, norm2_gain, norm2_shift, conv_a).astype(jnp.bfloat16)
    branch = norm_conv(hidden, norm3_gain, norm3_shift, conv_b)
    return (lifted.astype(jnp.float32) + branch).astype(jnp.bfloat16)


def solution(mesh):
    return jax.shard_map(
        per_device,
        mesh=mesh,
        in_specs=(
            P(("videos", "ta"), "ha", "wa", None),
            P(),
            P(),
            P(),
            P(),
            P(),
            P(),
            P(),
            P(),
            P(),
        ),
        out_specs=P(("videos", "ta"), "ha", "wa", None),
        check_vma=False,
    )
```

```python
import jax
import jax.numpy as jnp
from jax import lax
from jax.sharding import PartitionSpec as P

GROUPS = 32


EPSILON = 1e-06


def passed_along(block, axis, distance):
    devices = range(lax.axis_size(axis))
    route = [(i - distance, i) for i in devices if i - distance in devices]
    return lax.ppermute(block, axis, route)


def padded_2(x, sides, width):
    for axis, dim in sides:
        size, length = (lax.axis_size(axis), x.shape[dim])
        up = [(i, (i + 1) % size) for i in range(size - 1)]
        down = [(j, i) for i, j in up]
        last = lax.slice_in_dim(x, length - width, length, axis=dim)
        initial = lax.slice_in_dim(x, 0, width, axis=dim)
        before = lax.ppermute(last, axis, up)
        after = lax.ppermute(initial, axis, down)
        x = jnp.concatenate([before, x, after], axis=dim)
    return x


def group_allreduce(x, axes):
    sizes = [lax.axis_size(a) for a in axes]
    count = 1
    for s in sizes:
        count *= s
    if count & (count - 1):
        return lax.psum(x, axes)
    index = 0
    for a, s in zip(axes, sizes):
        index = index * s + lax.axis_index(a)
    shift = 0
    while (1 << shift) < count:
        width = min(2, (count.bit_length() - 1) - shift)
        slots = 1 << width
        position = (index >> shift) % slots
        received = [x] + [
            lax.ppermute(x, axes, [(i, i ^ (d << shift)) for i in range(count)])
            for d in range(1, slots)
        ]
        ordered = []
        for j in range(slots):
            value = jnp.zeros_like(x)
            for d in range(slots):
                value = jnp.where((position ^ d) == j, received[d], value)
            ordered.append(value)
        while len(ordered) > 1:
            ordered = [ordered[k] + ordered[k + 1] for k in range(0, len(ordered), 2)]
        x = ordered[0]
        shift += width
    return x


def group_stats(values):
    channels = values.shape[-1]
    group_width = channels // GROUPS
    grouped = values.reshape(-1, GROUPS, group_width)
    entries = (
        grouped.shape[0]
        * group_width
        * lax.axis_size("ha")
        * lax.axis_size("wa")
        * lax.axis_size("ta")
    )
    totals, squares = group_allreduce(
        jnp.stack([jnp.sum(grouped, axis=(0, 2)), jnp.sum(grouped * grouped, axis=(0, 2))]),
        ("ha", "wa", "ta"),
    )
    average = totals / entries
    spread = squares / entries - average * average
    scaling = lax.rsqrt(spread + EPSILON)
    return jnp.repeat(average, group_width), jnp.repeat(scaling, group_width)


def activate(values, stats, scale_vec, shift_vec):
    average, scaling = stats
    normed = (values - average) * scaling * scale_vec + shift_vec
    return jax.nn.silu(normed)


def inside_mask(rows, cols, low_pad):
    h, h_last = lax.axis_index("ha"), lax.axis_size("ha") - 1
    w, w_last = lax.axis_index("wa"), lax.axis_size("wa") - 1
    r = jnp.arange(rows)
    c = jnp.arange(cols)
    row_ok = jnp.logical_and(
        jnp.logical_or(r >= low_pad, h > 0), jnp.logical_or(r < rows - 1, h < h_last)
    )
    col_ok = jnp.logical_and(
        jnp.logical_or(c >= low_pad, w > 0), jnp.logical_or(c < cols - 1, w < w_last)
    )
    return jnp.logical_and(row_ok[:, None], col_ok[None, :])[None, :, :, None]


def latent_halo(x):
    h_size, w_size = lax.axis_size("ha"), lax.axis_size("wa")
    below = passed_along(x[:, :1], "ha", -1)
    right = passed_along(x[:, :, :1], "wa", -1)
    corner_route = [
        ((h + 1) * w_size + w + 1, h * w_size + w)
        for h in range(h_size - 1)
        for w in range(w_size - 1)
    ]
    corner = lax.ppermute(x[:, :1, :1], ("ha", "wa"), corner_route)
    top = jnp.concatenate([x, right], axis=2)
    bottom = jnp.concatenate([below, corner], axis=2)
    return jnp.concatenate([top, bottom], axis=1)


def upsample(act, kernel):
    frames, rows, cols, channels = act.shape
    height, across = rows - 1, cols - 1
    flat = lambda v: v.reshape(-1, channels)
    dot = lambda v, w: jnp.dot(flat(v), w, preferred_element_type=jnp.float32)
    a = act[:, :height, :across]
    b = act[:, :height, 1:]
    c = act[:, 1:, :across]
    d = act[:, 1:, 1:]
    out = kernel.shape[-1]
    pa = dot(a, jnp.concatenate([kernel[1, 1], kernel[1, 2], kernel[2, 1], kernel[2, 2]], axis=1))
    pb = dot(b, jnp.concatenate([kernel[1, 0], kernel[2, 0]], axis=1))
    pc = dot(c, jnp.concatenate([kernel[0, 1], kernel[0, 2]], axis=1))
    pd = dot(d, kernel[0, 0])
    ee = pa[:, :out]
    eo = pa[:, out : 2 * out] + pb[:, :out]
    oe = pa[:, 2 * out : 3 * out] + pc[:, :out]
    oo = pa[:, 3 * out :] + pb[:, out:] + pc[:, out:] + pd
    shape = (frames, height, across, 1, out)
    even = jnp.concatenate([ee.reshape(shape), eo.reshape(shape)], axis=3)
    odd = jnp.concatenate([oe.reshape(shape), oo.reshape(shape)], axis=3)
    even = even.reshape(frames, height, 1, 2 * across, out)
    odd = odd.reshape(frames, height, 1, 2 * across, out)
    return jnp.concatenate([even, odd], axis=2).reshape(frames, 2 * height, 2 * across, out)


def valid_conv(padded, kernel, frames, height, across):
    channels = padded.shape[-1]
    wide = jnp.concatenate(
        [padded[:, dy : dy + height, dx : dx + across] for dy in range(3) for dx in range(3)], axis=-1
    )
    taps = kernel.reshape(3, 9 * channels, kernel.shape[-1])
    result = None
    for step_t in range(3):
        window = wide[step_t : step_t + frames].reshape(-1, 9 * channels)
        part = jnp.dot(window, taps[step_t], preferred_element_type=jnp.float32)
        result = part if result is None else result + part
    return result.reshape(frames, height, across, -1)


def conv_halo(values):
    x = padded_2(values, (("ha", 1), ("wa", 2)), 1)
    earlier = passed_along(x[-2:], "ta", 1)
    opening = jnp.concatenate([x[:1], x[:1]], axis=0)
    earlier = jnp.where(lax.axis_index("ta") == 0, opening, earlier)
    return jnp.concatenate([earlier, x], axis=0)


def swap(x, axis, distance):
    size = lax.axis_size(axis)
    return lax.ppermute(x, axis, [(i, i ^ distance) for i in range(size)])


def fast_mesh():
    return lax.axis_size("ta") == 2 and lax.axis_size("wa") == 2 and lax.axis_size("ha") == 4


def local_sums(values):
    grouped = values.reshape(-1, GROUPS, values.shape[-1] // GROUPS)
    return jnp.stack([jnp.sum(grouped, axis=(0, 2)), jnp.sum(grouped * grouped, axis=(0, 2))])


def finish_stats(sums, values):
    channels = values.shape[-1]
    group_width = channels // GROUPS
    entries = (
        values.size // GROUPS
        * lax.axis_size("ha")
        * lax.axis_size("wa")
        * lax.axis_size("ta")
    )
    average = sums[0] / entries
    spread = sums[1] / entries - average * average
    scaling = lax.rsqrt(spread + EPSILON)
    return jnp.repeat(average, group_width), jnp.repeat(scaling, group_width)


def split_high(value):
    scaled = value * 65537.0
    return scaled - (scaled - value)


def pack_sums(sums, width):
    high = split_high(sums)
    rest = sums - high
    middle = split_high(rest)
    low = rest - middle
    flat = jnp.concatenate([high.reshape(-1), middle.reshape(-1), low.reshape(-1)])
    flat = flat.astype(jnp.bfloat16)
    rows = -(-flat.size // width)
    return jnp.pad(flat, (0, rows * width - flat.size)).reshape(rows, width)


def unpack_sums(rows, like):
    flat = rows.reshape(-1)[: 3 * like.size].astype(jnp.float32).reshape(3, *like.shape)
    return (flat[0] + flat[1]) + flat[2]


def swap_with(sums, payload, axis, distance, along):
    slot = list(payload.shape)
    slot[along] = 1
    size = 1
    for s in slot:
        size *= s
    packed = pack_sums(sums, size).reshape(slot)
    message = jnp.concatenate([payload, packed], axis=along)
    got = swap(message, axis, distance)
    cut = payload.shape[along]
    received = lax.slice_in_dim(got, 0, cut, axis=along)
    return unpack_sums(lax.slice_in_dim(got, cut, cut + 1, axis=along), sums), received


def ha_round(sums, upper, lower):
    h = lax.axis_index("ha")
    to_first = jnp.where(h % 2 == 1, upper, lower)
    to_third = jnp.where(h == 2, upper, lower)
    s1, got_first = swap_with(sums, to_first, "ha", 1, 0)
    s2 = swap(sums, "ha", 2)
    s3, got_third = swap_with(sums, to_third, "ha", 3, 0)
    sums = (sums + s1) + (s2 + s3)
    above = jnp.where(h % 2 == 1, got_first, got_third)
    below = jnp.where(h % 2 == 0, got_first, got_third)
    return sums, above, below


def fast_conv_input(values):
    sums = local_sums(values.astype(jnp.float32))
    s_t, earlier = swap_with(sums, values[-2:], "ta", 1, 1)
    sums = sums + s_t
    opening = jnp.concatenate([values[:1], values[:1]], axis=0)
    earlier = jnp.where(lax.axis_index("ta") == 0, opening, earlier)
    x = jnp.concatenate([earlier, values], axis=0)
    w = lax.axis_index("wa")
    s_w, beside = swap_with(sums, jnp.where(w == 0, x[:, :, -1:], x[:, :, :1]), "wa", 1, 1)
    sums = sums + s_w
    x = jnp.concatenate([beside, x, beside], axis=2)
    sums, above, below = ha_round(sums, x[:, :1], x[:, -1:])
    x = jnp.concatenate([above, x, below], axis=1)
    return finish_stats(sums, values), x


def fast_latent_input(values):
    sums = local_sums(values.astype(jnp.float32))
    sums = sums + swap(sums, "ta", 1)
    s_w, beside = swap_with(sums, values[:, :, :1], "wa", 1, 1)
    sums = sums + s_w
    x = jnp.concatenate([values, beside], axis=2)
    sums, _, below = ha_round(sums, x[:, :1], x[:, :1])
    x = jnp.concatenate([x, below], axis=1)
    return finish_stats(sums, values), x


def norm_conv(values, gain, shift, kernel):
    frames, height, across, _ = values.shape
    if fast_mesh():
        stats, extended = fast_conv_input(values)
    else:
        stats = group_stats(values.astype(jnp.float32))
        extended = conv_halo(values)
    act = activate(extended.astype(jnp.float32), stats, gain, shift)
    act = jnp.where(inside_mask(height + 2, across + 2, 1), act, 0.0).astype(jnp.bfloat16)
    return valid_conv(act, kernel, frames, height, across)


def per_device(
    latents,
    norm1_gain,
    norm1_shift,
    up_weight,
    norm2_gain,
    norm2_shift,
    conv_a,
    norm3_gain,
    norm3_shift,
    conv_b,
):
    frames, height, across, channels = latents.shape
    if fast_mesh():
        stats, extended = fast_latent_input(latents)
    else:
        stats = group_stats(latents.astype(jnp.float32))
        extended = latent_halo(latents)
    activated = activate(extended.astype(jnp.float32), stats, norm1_gain, norm1_shift)
    activated = jnp.where(inside_mask(height + 1, across + 1, 0), activated, 0.0)
    lifted = upsample(activated.astype(jnp.bfloat16), up_weight).astype(jnp.bfloat16)
    hidden = norm_conv(lifted, norm2_gain, norm2_shift, conv_a).astype(jnp.bfloat16)
    branch = norm_conv(hidden, norm3_gain, norm3_shift, conv_b)
    return (lifted.astype(jnp.float32) + branch).astype(jnp.bfloat16)


def solution(mesh):
    return jax.shard_map(
        per_device,
        mesh=mesh,
        in_specs=(
            P(("videos", "ta"), "ha", "wa", None),
            P(),
            P(),
            P(),
            P(),
            P(),
            P(),
            P(),
            P(),
            P(),
        ),
        out_specs=P(("videos", "ta"), "ha", "wa", None),
        check_vma=False,
    )
```

```python
import jax
import jax.numpy as jnp
from jax import lax
from jax.sharding import PartitionSpec as P

GROUPS = 32


EPSILON = 1e-06


def passed_along(block, axis, distance):
    devices = range(lax.axis_size(axis))
    route = [(i - distance, i) for i in devices if i - distance in devices]
    return lax.ppermute(block, axis, route)


def padded_2(x, sides, width):
    for axis, dim in sides:
        size, length = (lax.axis_size(axis), x.shape[dim])
        up = [(i, (i + 1) % size) for i in range(size - 1)]
        down = [(j, i) for i, j in up]
        last = lax.slice_in_dim(x, length - width, length, axis=dim)
        initial = lax.slice_in_dim(x, 0, width, axis=dim)
        before = lax.ppermute(last, axis, up)
        after = lax.ppermute(initial, axis, down)
        x = jnp.concatenate([before, x, after], axis=dim)
    return x


def group_allreduce(x, axes):
    sizes = [lax.axis_size(a) for a in axes]
    count = 1
    for s in sizes:
        count *= s
    if count & (count - 1):
        return lax.psum(x, axes)
    index = 0
    for a, s in zip(axes, sizes):
        index = index * s + lax.axis_index(a)
    shift = 0
    while (1 << shift) < count:
        width = min(2, (count.bit_length() - 1) - shift)
        slots = 1 << width
        position = (index >> shift) % slots
        received = [x] + [
            lax.ppermute(x, axes, [(i, i ^ (d << shift)) for i in range(count)])
            for d in range(1, slots)
        ]
        ordered = []
        for j in range(slots):
            value = jnp.zeros_like(x)
            for d in range(slots):
                value = jnp.where((position ^ d) == j, received[d], value)
            ordered.append(value)
        while len(ordered) > 1:
            ordered = [ordered[k] + ordered[k + 1] for k in range(0, len(ordered), 2)]
        x = ordered[0]
        shift += width
    return x


def group_stats(values):
    channels = values.shape[-1]
    group_width = channels // GROUPS
    grouped = values.reshape(-1, GROUPS, group_width)
    entries = (
        grouped.shape[0]
        * group_width
        * lax.axis_size("ha")
        * lax.axis_size("wa")
        * lax.axis_size("ta")
    )
    totals, squares = group_allreduce(
        jnp.stack([jnp.sum(grouped, axis=(0, 2)), jnp.sum(grouped * grouped, axis=(0, 2))]),
        ("ha", "wa", "ta"),
    )
    average = totals / entries
    spread = squares / entries - average * average
    scaling = lax.rsqrt(spread + EPSILON)
    return jnp.repeat(average, group_width), jnp.repeat(scaling, group_width)


def activate(values, stats, scale_vec, shift_vec):
    average, scaling = stats
    normed = (values - average) * scaling * scale_vec + shift_vec
    return jax.nn.silu(normed)


def inside_mask(rows, cols, low_pad):
    h, h_last = lax.axis_index("ha"), lax.axis_size("ha") - 1
    w, w_last = lax.axis_index("wa"), lax.axis_size("wa") - 1
    r = jnp.arange(rows)
    c = jnp.arange(cols)
    row_ok = jnp.logical_and(
        jnp.logical_or(r >= low_pad, h > 0), jnp.logical_or(r < rows - 1, h < h_last)
    )
    col_ok = jnp.logical_and(
        jnp.logical_or(c >= low_pad, w > 0), jnp.logical_or(c < cols - 1, w < w_last)
    )
    return jnp.logical_and(row_ok[:, None], col_ok[None, :])[None, :, :, None]


def latent_halo(x):
    h_size, w_size = lax.axis_size("ha"), lax.axis_size("wa")
    below = passed_along(x[:, :1], "ha", -1)
    right = passed_along(x[:, :, :1], "wa", -1)
    corner_route = [
        ((h + 1) * w_size + w + 1, h * w_size + w)
        for h in range(h_size - 1)
        for w in range(w_size - 1)
    ]
    corner = lax.ppermute(x[:, :1, :1], ("ha", "wa"), corner_route)
    top = jnp.concatenate([x, right], axis=2)
    bottom = jnp.concatenate([below, corner], axis=2)
    return jnp.concatenate([top, bottom], axis=1)


def upsample(act, kernel):
    frames, rows, cols, channels = act.shape
    height, across = rows - 1, cols - 1
    flat = lambda v: v.reshape(-1, channels)
    dot = lambda v, w: jnp.dot(flat(v), w, preferred_element_type=jnp.float32)
    a = act[:, :height, :across]
    b = act[:, :height, 1:]
    c = act[:, 1:, :across]
    d = act[:, 1:, 1:]
    out = kernel.shape[-1]
    pa = dot(a, jnp.concatenate([kernel[1, 1], kernel[1, 2], kernel[2, 1], kernel[2, 2]], axis=1))
    pb = dot(b, jnp.concatenate([kernel[1, 0], kernel[2, 0]], axis=1))
    pc = dot(c, jnp.concatenate([kernel[0, 1], kernel[0, 2]], axis=1))
    pd = dot(d, kernel[0, 0])
    ee = pa[:, :out]
    eo = pa[:, out : 2 * out] + pb[:, :out]
    oe = pa[:, 2 * out : 3 * out] + pc[:, :out]
    oo = pa[:, 3 * out :] + pb[:, out:] + pc[:, out:] + pd
    shape = (frames, height, across, 1, out)
    even = jnp.concatenate([ee.reshape(shape), eo.reshape(shape)], axis=3)
    odd = jnp.concatenate([oe.reshape(shape), oo.reshape(shape)], axis=3)
    even = even.reshape(frames, height, 1, 2 * across, out)
    odd = odd.reshape(frames, height, 1, 2 * across, out)
    return jnp.concatenate([even, odd], axis=2).reshape(frames, 2 * height, 2 * across, out)


def valid_conv(padded, kernel, frames, height, across):
    out = lax.conv_general_dilated(
        padded[None],
        kernel,
        (1, 1, 1),
        "VALID",
        dimension_numbers=("NDHWC", "DHWIO", "NDHWC"),
        preferred_element_type=jnp.float32,
    )
    return out[0]


def conv_halo(values):
    x = padded_2(values, (("ha", 1), ("wa", 2)), 1)
    earlier = passed_along(x[-2:], "ta", 1)
    opening = jnp.concatenate([x[:1], x[:1]], axis=0)
    earlier = jnp.where(lax.axis_index("ta") == 0, opening, earlier)
    return jnp.concatenate([earlier, x], axis=0)


def swap(x, axis, distance):
    size = lax.axis_size(axis)
    return lax.ppermute(x, axis, [(i, i ^ distance) for i in range(size)])


def fast_mesh():
    return lax.axis_size("ta") == 2 and lax.axis_size("wa") == 2 and lax.axis_size("ha") == 4


def local_sums(values):
    channels = values.shape[-1]
    flat = values.reshape(-1, channels)
    per_channel = jnp.stack([jnp.sum(flat, axis=0), jnp.sum(flat * flat, axis=0)])
    member = jnp.arange(channels)[:, None] // (channels // GROUPS) == jnp.arange(GROUPS)[None, :]
    return jnp.dot(per_channel, member.astype(jnp.float32), precision=lax.Precision.HIGHEST)


def finish_stats(sums, values):
    channels = values.shape[-1]
    group_width = channels // GROUPS
    entries = (
        values.size // GROUPS
        * lax.axis_size("ha")
        * lax.axis_size("wa")
        * lax.axis_size("ta")
    )
    average = sums[0] / entries
    spread = sums[1] / entries - average * average
    scaling = lax.rsqrt(spread + EPSILON)
    return jnp.repeat(average, group_width), jnp.repeat(scaling, group_width)


def split_high(value):
    scaled = value * 65537.0
    return scaled - (scaled - value)


def pack_sums(sums, width):
    high = split_high(sums)
    rest = sums - high
    middle = split_high(rest)
    low = rest - middle
    flat = jnp.concatenate([high.reshape(-1), middle.reshape(-1), low.reshape(-1)])
    flat = flat.astype(jnp.bfloat16)
    rows = -(-flat.size // width)
    return jnp.pad(flat, (0, rows * width - flat.size)).reshape(rows, width)


def unpack_sums(rows, like):
    flat = rows.reshape(-1)[: 3 * like.size].astype(jnp.float32).reshape(3, *like.shape)
    return (flat[0] + flat[1]) + flat[2]


def swap_with(sums, payload, axis, distance):
    width = payload.shape[-1]
    packed = pack_sums(sums, width)
    message = jnp.concatenate([payload.reshape(-1, width), packed], axis=0)
    got = swap(message, axis, distance)
    cut = got.shape[0] - packed.shape[0]
    return unpack_sums(got[cut:], sums), got[:cut].reshape(payload.shape)


def ha_round(sums, upper, lower):
    h = lax.axis_index("ha")
    to_first = jnp.where(h % 2 == 1, upper, lower)
    to_third = jnp.where(h == 2, upper, lower)
    s1, got_first = swap_with(sums, to_first, "ha", 1)
    s2 = swap(sums, "ha", 2)
    s3, got_third = swap_with(sums, to_third, "ha", 3)
    sums = (sums + s1) + (s2 + s3)
    above = jnp.where(h % 2 == 1, got_first, got_third)
    below = jnp.where(h % 2 == 0, got_first, got_third)
    return sums, above, below


def fast_conv_input(values):
    sums = local_sums(values.astype(jnp.float32))
    s_t, earlier = swap_with(sums, values[-2:], "ta", 1)
    sums = sums + s_t
    opening = jnp.concatenate([values[:1], values[:1]], axis=0)
    earlier = jnp.where(lax.axis_index("ta") == 0, opening, earlier)
    x = jnp.concatenate([earlier, values], axis=0)
    w = lax.axis_index("wa")
    s_w, beside = swap_with(sums, jnp.where(w == 0, x[:, :, -1:], x[:, :, :1]), "wa", 1)
    sums = sums + s_w
    x = jnp.concatenate([beside, x, beside], axis=2)
    sums, above, below = ha_round(sums, x[:, :1], x[:, -1:])
    x = jnp.concatenate([above, x, below], axis=1)
    return finish_stats(sums, values), x


def fast_latent_input(values):
    sums = local_sums(values.astype(jnp.float32))
    sums = sums + swap(sums, "ta", 1)
    s_w, beside = swap_with(sums, values[:, :, :1], "wa", 1)
    sums = sums + s_w
    x = jnp.concatenate([values, beside], axis=2)
    sums, _, below = ha_round(sums, x[:, :1], x[:, :1])
    x = jnp.concatenate([x, below], axis=1)
    return finish_stats(sums, values), x


def norm_conv(values, gain, shift, kernel):
    frames, height, across, _ = values.shape
    if fast_mesh():
        stats, extended = fast_conv_input(values)
    else:
        stats = group_stats(values.astype(jnp.float32))
        extended = conv_halo(values)
    act = activate(extended.astype(jnp.float32), stats, gain, shift)
    act = jnp.where(inside_mask(height + 2, across + 2, 1), act, 0.0).astype(jnp.bfloat16)
    return valid_conv(act, kernel, frames, height, across)


def per_device(
    latents,
    norm1_gain,
    norm1_shift,
    up_weight,
    norm2_gain,
    norm2_shift,
    conv_a,
    norm3_gain,
    norm3_shift,
    conv_b,
):
    frames, height, across, channels = latents.shape
    if fast_mesh():
        stats, extended = fast_latent_input(latents)
    else:
        stats = group_stats(latents.astype(jnp.float32))
        extended = latent_halo(latents)
    activated = activate(extended.astype(jnp.float32), stats, norm1_gain, norm1_shift)
    activated = jnp.where(inside_mask(height + 1, across + 1, 0), activated, 0.0)
    lifted = upsample(activated.astype(jnp.bfloat16), up_weight).astype(jnp.bfloat16)
    hidden = norm_conv(lifted, norm2_gain, norm2_shift, conv_a).astype(jnp.bfloat16)
    branch = norm_conv(hidden, norm3_gain, norm3_shift, conv_b)
    return (lifted.astype(jnp.float32) + branch).astype(jnp.bfloat16)


def solution(mesh):
    return jax.shard_map(
        per_device,
        mesh=mesh,
        in_specs=(
            P(("videos", "ta"), "ha", "wa", None),
            P(),
            P(),
            P(),
            P(),
            P(),
            P(),
            P(),
            P(),
            P(),
        ),
        out_specs=P(("videos", "ta"), "ha", "wa", None),
        check_vma=False,
    )
```

```python
import jax
import jax.numpy as jnp
from jax import lax
from jax.sharding import PartitionSpec as P

GROUPS = 32


EPSILON = 1e-06


def passed_along(block, axis, distance):
    devices = range(lax.axis_size(axis))
    route = [(i - distance, i) for i in devices if i - distance in devices]
    return lax.ppermute(block, axis, route)


def padded_2(x, sides, width):
    for axis, dim in sides:
        size, length = (lax.axis_size(axis), x.shape[dim])
        up = [(i, (i + 1) % size) for i in range(size - 1)]
        down = [(j, i) for i, j in up]
        last = lax.slice_in_dim(x, length - width, length, axis=dim)
        initial = lax.slice_in_dim(x, 0, width, axis=dim)
        before = lax.ppermute(last, axis, up)
        after = lax.ppermute(initial, axis, down)
        x = jnp.concatenate([before, x, after], axis=dim)
    return x


def group_allreduce(x, axes):
    sizes = [lax.axis_size(a) for a in axes]
    count = 1
    for s in sizes:
        count *= s
    if count & (count - 1):
        return lax.psum(x, axes)
    index = 0
    for a, s in zip(axes, sizes):
        index = index * s + lax.axis_index(a)
    shift = 0
    while (1 << shift) < count:
        width = min(2, (count.bit_length() - 1) - shift)
        slots = 1 << width
        position = (index >> shift) % slots
        received = [x] + [
            lax.ppermute(x, axes, [(i, i ^ (d << shift)) for i in range(count)])
            for d in range(1, slots)
        ]
        ordered = []
        for j in range(slots):
            value = jnp.zeros_like(x)
            for d in range(slots):
                value = jnp.where((position ^ d) == j, received[d], value)
            ordered.append(value)
        while len(ordered) > 1:
            ordered = [ordered[k] + ordered[k + 1] for k in range(0, len(ordered), 2)]
        x = ordered[0]
        shift += width
    return x


def group_stats(values):
    channels = values.shape[-1]
    group_width = channels // GROUPS
    grouped = values.reshape(-1, GROUPS, group_width)
    entries = (
        grouped.shape[0]
        * group_width
        * lax.axis_size("ha")
        * lax.axis_size("wa")
        * lax.axis_size("ta")
    )
    totals, squares = group_allreduce(
        jnp.stack([jnp.sum(grouped, axis=(0, 2)), jnp.sum(grouped * grouped, axis=(0, 2))]),
        ("ha", "wa", "ta"),
    )
    average = totals / entries
    spread = squares / entries - average * average
    scaling = lax.rsqrt(spread + EPSILON)
    return jnp.repeat(average, group_width), jnp.repeat(scaling, group_width)


def activate(values, stats, scale_vec, shift_vec):
    average, scaling = stats
    normed = (values - average) * scaling * scale_vec + shift_vec
    return jax.nn.silu(normed)


def inside_mask(rows, cols, low_pad):
    h, h_last = lax.axis_index("ha"), lax.axis_size("ha") - 1
    w, w_last = lax.axis_index("wa"), lax.axis_size("wa") - 1
    r = jnp.arange(rows)
    c = jnp.arange(cols)
    row_ok = jnp.logical_and(
        jnp.logical_or(r >= low_pad, h > 0), jnp.logical_or(r < rows - 1, h < h_last)
    )
    col_ok = jnp.logical_and(
        jnp.logical_or(c >= low_pad, w > 0), jnp.logical_or(c < cols - 1, w < w_last)
    )
    return jnp.logical_and(row_ok[:, None], col_ok[None, :])[None, :, :, None]


def latent_halo(x):
    h_size, w_size = lax.axis_size("ha"), lax.axis_size("wa")
    below = passed_along(x[:, :1], "ha", -1)
    right = passed_along(x[:, :, :1], "wa", -1)
    corner_route = [
        ((h + 1) * w_size + w + 1, h * w_size + w)
        for h in range(h_size - 1)
        for w in range(w_size - 1)
    ]
    corner = lax.ppermute(x[:, :1, :1], ("ha", "wa"), corner_route)
    top = jnp.concatenate([x, right], axis=2)
    bottom = jnp.concatenate([below, corner], axis=2)
    return jnp.concatenate([top, bottom], axis=1)


def upsample(act, kernel):
    frames, rows, cols, channels = act.shape
    height, across = rows - 1, cols - 1
    flat = lambda v: v.reshape(-1, channels)
    dot = lambda v, w: jnp.dot(flat(v), w, preferred_element_type=jnp.float32)
    a = act[:, :height, :across]
    b = act[:, :height, 1:]
    c = act[:, 1:, :across]
    d = act[:, 1:, 1:]
    out = kernel.shape[-1]
    pa = dot(a, jnp.concatenate([kernel[1, 1], kernel[1, 2], kernel[2, 1], kernel[2, 2]], axis=1))
    pb = dot(b, jnp.concatenate([kernel[1, 0], kernel[2, 0]], axis=1))
    pc = dot(c, jnp.concatenate([kernel[0, 1], kernel[0, 2]], axis=1))
    pd = dot(d, kernel[0, 0])
    ee = pa[:, :out]
    eo = pa[:, out : 2 * out] + pb[:, :out]
    oe = pa[:, 2 * out : 3 * out] + pc[:, :out]
    oo = pa[:, 3 * out :] + pb[:, out:] + pc[:, out:] + pd
    shape = (frames, height, across, 1, out)
    even = jnp.concatenate([ee.reshape(shape), eo.reshape(shape)], axis=3)
    odd = jnp.concatenate([oe.reshape(shape), oo.reshape(shape)], axis=3)
    even = even.reshape(frames, height, 1, 2 * across, out)
    odd = odd.reshape(frames, height, 1, 2 * across, out)
    return jnp.concatenate([even, odd], axis=2).reshape(frames, 2 * height, 2 * across, out)


def valid_conv(padded, kernel, frames, height, across):
    channels = padded.shape[-1]
    wide = jnp.concatenate(
        [padded[:, dy : dy + height, dx : dx + across] for dy in range(3) for dx in range(3)], axis=-1
    )
    result = None
    for step_t in range(3):
        window = wide[step_t : step_t + frames].reshape(-1, 9 * channels)
        part = jnp.dot(
            window, kernel[step_t].reshape(9 * channels, -1), preferred_element_type=jnp.float32
        )
        result = part if result is None else result + part
    return result.reshape(frames, height, across, -1)


def conv_halo(values):
    x = padded_2(values, (("ha", 1), ("wa", 2)), 1)
    earlier = passed_along(x[-2:], "ta", 1)
    opening = jnp.concatenate([x[:1], x[:1]], axis=0)
    earlier = jnp.where(lax.axis_index("ta") == 0, opening, earlier)
    return jnp.concatenate([earlier, x], axis=0)


def swap(x, axis, distance):
    size = lax.axis_size(axis)
    return lax.ppermute(x, axis, [(i, i ^ distance) for i in range(size)])


def fast_mesh():
    return lax.axis_size("ta") == 2 and lax.axis_size("wa") == 2 and lax.axis_size("ha") == 4


def local_sums(values):
    grouped = values.reshape(-1, GROUPS, values.shape[-1] // GROUPS)
    return jnp.stack([jnp.sum(grouped, axis=(0, 2)), jnp.sum(grouped * grouped, axis=(0, 2))])


def finish_stats(sums, values):
    channels = values.shape[-1]
    group_width = channels // GROUPS
    entries = (
        values.size // GROUPS
        * lax.axis_size("ha")
        * lax.axis_size("wa")
        * lax.axis_size("ta")
    )
    average = sums[0] / entries
    spread = sums[1] / entries - average * average
    scaling = lax.rsqrt(spread + EPSILON)
    return jnp.repeat(average, group_width), jnp.repeat(scaling, group_width)


def split_high(value):
    scaled = value * 65537.0
    return scaled - (scaled - value)


def pack_sums(sums, width):
    high = split_high(sums)
    rest = sums - high
    middle = split_high(rest)
    low = rest - middle
    flat = jnp.concatenate([high.reshape(-1), middle.reshape(-1), low.reshape(-1)])
    flat = flat.astype(jnp.bfloat16)
    rows = -(-flat.size // width)
    return jnp.pad(flat, (0, rows * width - flat.size)).reshape(rows, width)


def unpack_sums(rows, like):
    flat = rows.reshape(-1)[: 3 * like.size].astype(jnp.float32).reshape(3, *like.shape)
    return (flat[0] + flat[1]) + flat[2]


def swap_with(sums, payload, axis, distance):
    width = payload.shape[-1]
    packed = pack_sums(sums, width)
    message = jnp.concatenate([payload.reshape(-1, width), packed], axis=0)
    got = swap(message, axis, distance)
    cut = got.shape[0] - packed.shape[0]
    return unpack_sums(got[cut:], sums), got[:cut].reshape(payload.shape)


def ha_round(sums, upper, lower):
    h = lax.axis_index("ha")
    to_first = jnp.where(h % 2 == 1, upper, lower)
    to_third = jnp.where(h == 2, upper, lower)
    s1, got_first = swap_with(sums, to_first, "ha", 1)
    s2 = swap(sums, "ha", 2)
    s3, got_third = swap_with(sums, to_third, "ha", 3)
    sums = (sums + s1) + (s2 + s3)
    above = jnp.where(h % 2 == 1, got_first, got_third)
    below = jnp.where(h % 2 == 0, got_first, got_third)
    return sums, above, below


def fast_conv_input(values):
    sums = local_sums(values.astype(jnp.float32))
    w = lax.axis_index("wa")
    s_w, beside = swap_with(sums, jnp.where(w == 0, values[:, :, -1:], values[:, :, :1]), "wa", 1)
    sums = sums + s_w
    x = jnp.concatenate([beside, values, beside], axis=2)
    sums, above, below = ha_round(sums, x[:, :1], x[:, -1:])
    x = jnp.concatenate([above, x, below], axis=1)
    s_t, earlier = swap_with(sums, x[-2:], "ta", 1)
    sums = sums + s_t
    opening = jnp.concatenate([x[:1], x[:1]], axis=0)
    earlier = jnp.where(lax.axis_index("ta") == 0, opening, earlier)
    x = jnp.concatenate([earlier, x], axis=0)
    return finish_stats(sums, values), x


def fast_latent_input(values):
    sums = local_sums(values.astype(jnp.float32))
    sums = sums + swap(sums, "ta", 1)
    s_w, beside = swap_with(sums, values[:, :, :1], "wa", 1)
    sums = sums + s_w
    x = jnp.concatenate([values, beside], axis=2)
    sums, _, below = ha_round(sums, x[:, :1], x[:, :1])
    x = jnp.concatenate([x, below], axis=1)
    return finish_stats(sums, values), x


def norm_conv(values, gain, shift, kernel):
    frames, height, across, _ = values.shape
    if fast_mesh():
        stats, extended = fast_conv_input(values)
    else:
        stats = group_stats(values.astype(jnp.float32))
        extended = conv_halo(values)
    act = activate(extended.astype(jnp.float32), stats, gain, shift)
    act = jnp.where(inside_mask(height + 2, across + 2, 1), act, 0.0).astype(jnp.bfloat16)
    return valid_conv(act, kernel, frames, height, across)


def per_device(
    latents,
    norm1_gain,
    norm1_shift,
    up_weight,
    norm2_gain,
    norm2_shift,
    conv_a,
    norm3_gain,
    norm3_shift,
    conv_b,
):
    frames, height, across, channels = latents.shape
    if fast_mesh():
        stats, extended = fast_latent_input(latents)
    else:
        stats = group_stats(latents.astype(jnp.float32))
        extended = latent_halo(latents)
    activated = activate(extended.astype(jnp.float32), stats, norm1_gain, norm1_shift)
    activated = jnp.where(inside_mask(height + 1, across + 1, 0), activated, 0.0)
    lifted = upsample(activated.astype(jnp.bfloat16), up_weight).astype(jnp.bfloat16)
    hidden = norm_conv(lifted, norm2_gain, norm2_shift, conv_a).astype(jnp.bfloat16)
    branch = norm_conv(hidden, norm3_gain, norm3_shift, conv_b)
    return (lifted.astype(jnp.float32) + branch).astype(jnp.bfloat16)


def solution(mesh):
    return jax.shard_map(
        per_device,
        mesh=mesh,
        in_specs=(
            P(("videos", "ta"), "ha", "wa", None),
            P(),
            P(),
            P(),
            P(),
            P(),
            P(),
            P(),
            P(),
            P(),
        ),
        out_specs=P(("videos", "ta"), "ha", "wa", None),
        check_vma=False,
    )
```

```python
import jax
import jax.numpy as jnp
from jax import lax
from jax.sharding import PartitionSpec as P

GROUPS = 32


EPSILON = 1e-06


def passed_along(block, axis, distance):
    devices = range(lax.axis_size(axis))
    route = [(i - distance, i) for i in devices if i - distance in devices]
    return lax.ppermute(block, axis, route)


def padded_2(x, sides, width):
    for axis, dim in sides:
        size, length = (lax.axis_size(axis), x.shape[dim])
        up = [(i, (i + 1) % size) for i in range(size - 1)]
        down = [(j, i) for i, j in up]
        last = lax.slice_in_dim(x, length - width, length, axis=dim)
        initial = lax.slice_in_dim(x, 0, width, axis=dim)
        before = lax.ppermute(last, axis, up)
        after = lax.ppermute(initial, axis, down)
        x = jnp.concatenate([before, x, after], axis=dim)
    return x


def group_allreduce(x, axes):
    sizes = [lax.axis_size(a) for a in axes]
    count = 1
    for s in sizes:
        count *= s
    if count & (count - 1):
        return lax.psum(x, axes)
    index = 0
    for a, s in zip(axes, sizes):
        index = index * s + lax.axis_index(a)
    shift = 0
    while (1 << shift) < count:
        width = min(2, (count.bit_length() - 1) - shift)
        slots = 1 << width
        position = (index >> shift) % slots
        received = [x] + [
            lax.ppermute(x, axes, [(i, i ^ (d << shift)) for i in range(count)])
            for d in range(1, slots)
        ]
        ordered = []
        for j in range(slots):
            value = jnp.zeros_like(x)
            for d in range(slots):
                value = jnp.where((position ^ d) == j, received[d], value)
            ordered.append(value)
        while len(ordered) > 1:
            ordered = [ordered[k] + ordered[k + 1] for k in range(0, len(ordered), 2)]
        x = ordered[0]
        shift += width
    return x


def group_stats(values):
    channels = values.shape[-1]
    group_width = channels // GROUPS
    grouped = values.reshape(-1, GROUPS, group_width)
    entries = (
        grouped.shape[0]
        * group_width
        * lax.axis_size("ha")
        * lax.axis_size("wa")
        * lax.axis_size("ta")
    )
    totals, squares = group_allreduce(
        jnp.stack([jnp.sum(grouped, axis=(0, 2)), jnp.sum(grouped * grouped, axis=(0, 2))]),
        ("ha", "wa", "ta"),
    )
    average = totals / entries
    spread = squares / entries - average * average
    scaling = lax.rsqrt(spread + EPSILON)
    return jnp.repeat(average, group_width), jnp.repeat(scaling, group_width)


def activate(values, stats, scale_vec, shift_vec):
    average, scaling = stats
    normed = (values - average) * scaling * scale_vec + shift_vec
    return jax.nn.silu(normed)


def inside_mask(rows, cols, low_pad):
    h, h_last = lax.axis_index("ha"), lax.axis_size("ha") - 1
    w, w_last = lax.axis_index("wa"), lax.axis_size("wa") - 1
    r = jnp.arange(rows)
    c = jnp.arange(cols)
    row_ok = jnp.logical_and(
        jnp.logical_or(r >= low_pad, h > 0), jnp.logical_or(r < rows - 1, h < h_last)
    )
    col_ok = jnp.logical_and(
        jnp.logical_or(c >= low_pad, w > 0), jnp.logical_or(c < cols - 1, w < w_last)
    )
    return jnp.logical_and(row_ok[:, None], col_ok[None, :])[None, :, :, None]


def latent_halo(x):
    h_size, w_size = lax.axis_size("ha"), lax.axis_size("wa")
    below = passed_along(x[:, :1], "ha", -1)
    right = passed_along(x[:, :, :1], "wa", -1)
    corner_route = [
        ((h + 1) * w_size + w + 1, h * w_size + w)
        for h in range(h_size - 1)
        for w in range(w_size - 1)
    ]
    corner = lax.ppermute(x[:, :1, :1], ("ha", "wa"), corner_route)
    top = jnp.concatenate([x, right], axis=2)
    bottom = jnp.concatenate([below, corner], axis=2)
    return jnp.concatenate([top, bottom], axis=1)


def upsample(act, kernel):
    frames, rows, cols, channels = act.shape
    height, across = rows - 1, cols - 1
    flat = lambda v: v.reshape(-1, channels)
    dot = lambda v, w: jnp.dot(flat(v), w, preferred_element_type=jnp.float32)
    a = act[:, :height, :across]
    b = act[:, :height, 1:]
    c = act[:, 1:, :across]
    d = act[:, 1:, 1:]
    out = kernel.shape[-1]
    pa = dot(a, jnp.concatenate([kernel[1, 1], kernel[1, 2], kernel[2, 1], kernel[2, 2]], axis=1))
    pb = dot(b, jnp.concatenate([kernel[1, 0], kernel[2, 0]], axis=1))
    pc = dot(c, jnp.concatenate([kernel[0, 1], kernel[0, 2]], axis=1))
    pd = dot(d, kernel[0, 0])
    ee = pa[:, :out]
    eo = pa[:, out : 2 * out] + pb[:, :out]
    oe = pa[:, 2 * out : 3 * out] + pc[:, :out]
    oo = pa[:, 3 * out :] + pb[:, out:] + pc[:, out:] + pd
    shape = (frames, height, across, 1, out)
    even = jnp.concatenate([ee.reshape(shape), eo.reshape(shape)], axis=3)
    odd = jnp.concatenate([oe.reshape(shape), oo.reshape(shape)], axis=3)
    even = even.reshape(frames, height, 1, 2 * across, out)
    odd = odd.reshape(frames, height, 1, 2 * across, out)
    return jnp.concatenate([even, odd], axis=2).reshape(frames, 2 * height, 2 * across, out)


def conv_taps(kernel):
    channels = kernel.shape[-2]
    return [kernel[step_t].reshape(9 * channels, -1) for step_t in range(3)]


def valid_conv(padded, taps, frames, height, across):
    channels = padded.shape[-1]
    wide = jnp.concatenate(
        [padded[:, dy : dy + height, dx : dx + across] for dy in range(3) for dx in range(3)], axis=-1
    )
    result = None
    for step_t in range(3):
        window = wide[step_t : step_t + frames].reshape(-1, 9 * channels)
        part = jnp.dot(window, taps[step_t], preferred_element_type=jnp.float32)
        result = part if result is None else result + part
    return result.reshape(frames, height, across, -1)


def conv_halo(values):
    x = padded_2(values, (("ha", 1), ("wa", 2)), 1)
    earlier = passed_along(x[-2:], "ta", 1)
    opening = jnp.concatenate([x[:1], x[:1]], axis=0)
    earlier = jnp.where(lax.axis_index("ta") == 0, opening, earlier)
    return jnp.concatenate([earlier, x], axis=0)


def swap(x, axis, distance):
    size = lax.axis_size(axis)
    return lax.ppermute(x, axis, [(i, i ^ distance) for i in range(size)])


def fast_mesh():
    return lax.axis_size("ta") == 2 and lax.axis_size("wa") == 2 and lax.axis_size("ha") == 4


def local_sums(values):
    grouped = values.reshape(-1, GROUPS, values.shape[-1] // GROUPS)
    return jnp.stack([jnp.sum(grouped, axis=(0, 2)), jnp.sum(grouped * grouped, axis=(0, 2))])


def finish_stats(sums, values):
    channels = values.shape[-1]
    group_width = channels // GROUPS
    entries = (
        values.size // GROUPS
        * lax.axis_size("ha")
        * lax.axis_size("wa")
        * lax.axis_size("ta")
    )
    average = sums[0] / entries
    spread = sums[1] / entries - average * average
    scaling = lax.rsqrt(spread + EPSILON)
    return jnp.repeat(average, group_width), jnp.repeat(scaling, group_width)


def split_high(value):
    scaled = value * 65537.0
    return scaled - (scaled - value)


def pack_sums(sums, width):
    high = split_high(sums)
    rest = sums - high
    middle = split_high(rest)
    low = rest - middle
    flat = jnp.concatenate([high.reshape(-1), middle.reshape(-1), low.reshape(-1)])
    flat = flat.astype(jnp.bfloat16)
    rows = -(-flat.size // width)
    return jnp.pad(flat, (0, rows * width - flat.size)).reshape(rows, width)


def unpack_sums(rows, like):
    flat = rows.reshape(-1)[: 3 * like.size].astype(jnp.float32).reshape(3, *like.shape)
    return (flat[0] + flat[1]) + flat[2]


def swap_with(sums, payload, axis, distance):
    width = payload.shape[-1]
    packed = pack_sums(sums, width)
    message = jnp.concatenate([payload.reshape(-1, width), packed], axis=0)
    got = swap(message, axis, distance)
    cut = got.shape[0] - packed.shape[0]
    return unpack_sums(got[cut:], sums), got[:cut].reshape(payload.shape)


def ha_round(sums, upper, lower):
    h = lax.axis_index("ha")
    to_first = jnp.where(h % 2 == 1, upper, lower)
    to_third = jnp.where(h == 2, upper, lower)
    s1, got_first = swap_with(sums, to_first, "ha", 1)
    s2 = swap(sums, "ha", 2)
    s3, got_third = swap_with(sums, to_third, "ha", 3)
    sums = (sums + s1) + (s2 + s3)
    above = jnp.where(h % 2 == 1, got_first, got_third)
    below = jnp.where(h % 2 == 0, got_first, got_third)
    return sums, above, below


def fast_conv_input(values, ready):
    sums = local_sums(values.astype(jnp.float32))
    w = lax.axis_index("wa")
    s_w, beside = swap_with(sums, jnp.where(w == 0, values[:, :, -1:], values[:, :, :1]), "wa", 1)
    sums = sums + s_w
    x = jnp.concatenate([beside, values, beside], axis=2)
    sums, above, below = ha_round(sums, x[:, :1], x[:, -1:])
    x = jnp.concatenate([above, x, below], axis=1)
    x, sums, ready = lax.optimization_barrier((x, sums, ready))
    s_t, earlier = swap_with(sums, x[-2:], "ta", 1)
    sums = sums + s_t
    opening = jnp.concatenate([x[:1], x[:1]], axis=0)
    earlier = jnp.where(lax.axis_index("ta") == 0, opening, earlier)
    x = jnp.concatenate([earlier, x], axis=0)
    return finish_stats(sums, values), x, ready


def fast_latent_input(values):
    sums = local_sums(values.astype(jnp.float32))
    sums = sums + swap(sums, "ta", 1)
    s_w, beside = swap_with(sums, values[:, :, :1], "wa", 1)
    sums = sums + s_w
    x = jnp.concatenate([values, beside], axis=2)
    sums, _, below = ha_round(sums, x[:, :1], x[:, :1])
    x = jnp.concatenate([x, below], axis=1)
    return finish_stats(sums, values), x


def norm_conv(values, gain, shift, taps, ready):
    frames, height, across, _ = values.shape
    if fast_mesh():
        stats, extended, ready = fast_conv_input(values, ready)
    else:
        stats = group_stats(values.astype(jnp.float32))
        extended = conv_halo(values)
    act = activate(extended.astype(jnp.float32), stats, gain, shift)
    act = jnp.where(inside_mask(height + 2, across + 2, 1), act, 0.0).astype(jnp.bfloat16)
    return valid_conv(act, taps, frames, height, across), ready


def per_device(
    latents,
    norm1_gain,
    norm1_shift,
    up_weight,
    norm2_gain,
    norm2_shift,
    conv_a,
    norm3_gain,
    norm3_shift,
    conv_b,
):
    frames, height, across, channels = latents.shape
    taps_a = conv_taps(conv_a)
    if fast_mesh():
        stats, extended = fast_latent_input(latents)
        extended, stats, taps_a = lax.optimization_barrier((extended, stats, taps_a))
    else:
        stats = group_stats(latents.astype(jnp.float32))
        extended = latent_halo(latents)
    activated = activate(extended.astype(jnp.float32), stats, norm1_gain, norm1_shift)
    activated = jnp.where(inside_mask(height + 1, across + 1, 0), activated, 0.0)
    lifted = upsample(activated.astype(jnp.bfloat16), up_weight).astype(jnp.bfloat16)
    hidden, taps_b = norm_conv(lifted, norm2_gain, norm2_shift, taps_a, conv_taps(conv_b))
    branch, _ = norm_conv(hidden.astype(jnp.bfloat16), norm3_gain, norm3_shift, taps_b, None)
    return (lifted.astype(jnp.float32) + branch).astype(jnp.bfloat16)


def solution(mesh):
    return jax.shard_map(
        per_device,
        mesh=mesh,
        in_specs=(
            P(("videos", "ta"), "ha", "wa", None),
            P(),
            P(),
            P(),
            P(),
            P(),
            P(),
            P(),
            P(),
            P(),
        ),
        out_specs=P(("videos", "ta"), "ha", "wa", None),
        check_vma=False,
    )
```

```python
import jax
import jax.numpy as jnp
from jax import lax
from jax.sharding import PartitionSpec as P

GROUPS = 32


EPSILON = 1e-06


def passed_along(block, axis, distance):
    devices = range(lax.axis_size(axis))
    route = [(i - distance, i) for i in devices if i - distance in devices]
    return lax.ppermute(block, axis, route)


def padded_2(x, sides, width):
    for axis, dim in sides:
        size, length = (lax.axis_size(axis), x.shape[dim])
        up = [(i, (i + 1) % size) for i in range(size - 1)]
        down = [(j, i) for i, j in up]
        last = lax.slice_in_dim(x, length - width, length, axis=dim)
        initial = lax.slice_in_dim(x, 0, width, axis=dim)
        before = lax.ppermute(last, axis, up)
        after = lax.ppermute(initial, axis, down)
        x = jnp.concatenate([before, x, after], axis=dim)
    return x


def group_allreduce(x, axes):
    sizes = [lax.axis_size(a) for a in axes]
    count = 1
    for s in sizes:
        count *= s
    if count & (count - 1):
        return lax.psum(x, axes)
    index = 0
    for a, s in zip(axes, sizes):
        index = index * s + lax.axis_index(a)
    shift = 0
    while (1 << shift) < count:
        width = min(2, (count.bit_length() - 1) - shift)
        slots = 1 << width
        position = (index >> shift) % slots
        received = [x] + [
            lax.ppermute(x, axes, [(i, i ^ (d << shift)) for i in range(count)])
            for d in range(1, slots)
        ]
        ordered = []
        for j in range(slots):
            value = jnp.zeros_like(x)
            for d in range(slots):
                value = jnp.where((position ^ d) == j, received[d], value)
            ordered.append(value)
        while len(ordered) > 1:
            ordered = [ordered[k] + ordered[k + 1] for k in range(0, len(ordered), 2)]
        x = ordered[0]
        shift += width
    return x


def group_stats(values):
    channels = values.shape[-1]
    group_width = channels // GROUPS
    grouped = values.reshape(-1, GROUPS, group_width)
    entries = (
        grouped.shape[0]
        * group_width
        * lax.axis_size("ha")
        * lax.axis_size("wa")
        * lax.axis_size("ta")
    )
    totals, squares = group_allreduce(
        jnp.stack([jnp.sum(grouped, axis=(0, 2)), jnp.sum(grouped * grouped, axis=(0, 2))]),
        ("ha", "wa", "ta"),
    )
    average = totals / entries
    spread = squares / entries - average * average
    scaling = lax.rsqrt(spread + EPSILON)
    return jnp.repeat(average, group_width), jnp.repeat(scaling, group_width)


def activate(values, stats, scale_vec, shift_vec):
    average, scaling = stats
    normed = (values - average) * scaling * scale_vec + shift_vec
    return jax.nn.silu(normed)


def inside_mask(rows, cols, low_pad):
    h, h_last = lax.axis_index("ha"), lax.axis_size("ha") - 1
    w, w_last = lax.axis_index("wa"), lax.axis_size("wa") - 1
    r = jnp.arange(rows)
    c = jnp.arange(cols)
    row_ok = jnp.logical_and(
        jnp.logical_or(r >= low_pad, h > 0), jnp.logical_or(r < rows - 1, h < h_last)
    )
    col_ok = jnp.logical_and(
        jnp.logical_or(c >= low_pad, w > 0), jnp.logical_or(c < cols - 1, w < w_last)
    )
    return jnp.logical_and(row_ok[:, None], col_ok[None, :])[None, :, :, None]


def latent_halo(x):
    h_size, w_size = lax.axis_size("ha"), lax.axis_size("wa")
    below = passed_along(x[:, :1], "ha", -1)
    right = passed_along(x[:, :, :1], "wa", -1)
    corner_route = [
        ((h + 1) * w_size + w + 1, h * w_size + w)
        for h in range(h_size - 1)
        for w in range(w_size - 1)
    ]
    corner = lax.ppermute(x[:, :1, :1], ("ha", "wa"), corner_route)
    top = jnp.concatenate([x, right], axis=2)
    bottom = jnp.concatenate([below, corner], axis=2)
    return jnp.concatenate([top, bottom], axis=1)


def upsample(act, kernel):
    frames, rows, cols, channels = act.shape
    height, across = rows - 1, cols - 1
    flat = lambda v: v.reshape(-1, channels)
    dot = lambda v, w: jnp.dot(flat(v), w, preferred_element_type=jnp.float32)
    a = act[:, :height, :across]
    b = act[:, :height, 1:]
    c = act[:, 1:, :across]
    d = act[:, 1:, 1:]
    out = kernel.shape[-1]
    pa = dot(a, jnp.concatenate([kernel[1, 1], kernel[1, 2], kernel[2, 1], kernel[2, 2]], axis=1))
    pb = dot(b, jnp.concatenate([kernel[1, 0], kernel[2, 0]], axis=1))
    pc = dot(c, jnp.concatenate([kernel[0, 1], kernel[0, 2]], axis=1))
    pd = dot(d, kernel[0, 0])
    ee = pa[:, :out]
    eo = pa[:, out : 2 * out] + pb[:, :out]
    oe = pa[:, 2 * out : 3 * out] + pc[:, :out]
    oo = pa[:, 3 * out :] + pb[:, out:] + pc[:, out:] + pd
    shape = (frames, height, across, 1, out)
    even = jnp.concatenate([ee.reshape(shape), eo.reshape(shape)], axis=3)
    odd = jnp.concatenate([oe.reshape(shape), oo.reshape(shape)], axis=3)
    even = even.reshape(frames, height, 1, 2 * across, out)
    odd = odd.reshape(frames, height, 1, 2 * across, out)
    return jnp.concatenate([even, odd], axis=2).reshape(frames, 2 * height, 2 * across, out)


def valid_conv(padded, kernel, frames, height, across):
    channels = padded.shape[-1]
    wide = jnp.concatenate(
        [padded[:, dy : dy + height, dx : dx + across] for dy in range(3) for dx in range(3)], axis=-1
    )
    result = None
    for step_t in range(3):
        window = wide[step_t : step_t + frames].reshape(-1, 9 * channels)
        part = jnp.dot(
            window, kernel[step_t].reshape(9 * channels, -1), preferred_element_type=jnp.float32
        )
        result = part if result is None else result + part
    return result.reshape(frames, height, across, -1)


def conv_halo(values):
    x = padded_2(values, (("ha", 1), ("wa", 2)), 1)
    earlier = passed_along(x[-2:], "ta", 1)
    opening = jnp.concatenate([x[:1], x[:1]], axis=0)
    earlier = jnp.where(lax.axis_index("ta") == 0, opening, earlier)
    return jnp.concatenate([earlier, x], axis=0)


def swap(x, axis, distance):
    size = lax.axis_size(axis)
    return lax.ppermute(x, axis, [(i, i ^ distance) for i in range(size)])


def fast_mesh():
    return lax.axis_size("ta") == 2 and lax.axis_size("wa") == 2 and lax.axis_size("ha") == 4


def local_sums(values):
    grouped = values.reshape(-1, GROUPS, values.shape[-1] // GROUPS)
    return jnp.stack([jnp.sum(grouped, axis=(0, 2)), jnp.sum(grouped * grouped, axis=(0, 2))])


def finish_stats(sums, values):
    channels = values.shape[-1]
    group_width = channels // GROUPS
    entries = (
        values.size // GROUPS
        * lax.axis_size("ha")
        * lax.axis_size("wa")
        * lax.axis_size("ta")
    )
    average = sums[0] / entries
    spread = sums[1] / entries - average * average
    scaling = lax.rsqrt(spread + EPSILON)
    return jnp.repeat(average, group_width), jnp.repeat(scaling, group_width)


def split_high(value):
    scaled = value * 65537.0
    return scaled - (scaled - value)


def pack_sums(sums, width):
    high = split_high(sums)
    rest = sums - high
    middle = split_high(rest)
    low = rest - middle
    flat = jnp.concatenate([high.reshape(-1), middle.reshape(-1), low.reshape(-1)])
    flat = flat.astype(jnp.bfloat16)
    rows = -(-flat.size // width)
    return jnp.pad(flat, (0, rows * width - flat.size)).reshape(rows, width)


def unpack_sums(rows, like):
    flat = rows.reshape(-1)[: 3 * like.size].astype(jnp.float32).reshape(3, *like.shape)
    return (flat[0] + flat[1]) + flat[2]


def swap_with(sums, payload, axis, distance):
    width = payload.shape[-1]
    packed = pack_sums(sums, width)
    message = jnp.concatenate([payload.reshape(-1, width), packed], axis=0)
    got = swap(message, axis, distance)
    cut = got.shape[0] - packed.shape[0]
    return unpack_sums(got[cut:], sums), got[:cut].reshape(payload.shape)


def ha_round(sums, upper, lower):
    h = lax.axis_index("ha")
    s1, got_first = swap_with(sums, jnp.where(h % 2 == 1, upper, lower), "ha", 1)
    s2 = swap(sums, "ha", 2)
    inner = jnp.where(h == 2, upper, lower)
    width = inner.shape[-1]
    packed = pack_sums(sums, width)
    message = jnp.concatenate([inner.reshape(-1, width), packed], axis=0)
    got = lax.ppermute(message, "ha", [(1, 2), (2, 1)])
    cut = got.shape[0] - packed.shape[0]
    got_inner = got[:cut].reshape(inner.shape)
    s_outer = lax.ppermute(sums, "ha", [(0, 3), (3, 0)])
    s3 = jnp.where(jnp.logical_or(h == 1, h == 2), unpack_sums(got[cut:], sums), s_outer)
    sums = (sums + s1) + (s2 + s3)
    above = jnp.where(h % 2 == 1, got_first, got_inner)
    below = jnp.where(h % 2 == 0, got_first, got_inner)
    return sums, above, below


def fast_conv_input(values):
    sums = local_sums(values.astype(jnp.float32))
    w = lax.axis_index("wa")
    s_w, beside = swap_with(sums, jnp.where(w == 0, values[:, :, -1:], values[:, :, :1]), "wa", 1)
    sums = sums + s_w
    x = jnp.concatenate([beside, values, beside], axis=2)
    sums, above, below = ha_round(sums, x[:, :1], x[:, -1:])
    x = jnp.concatenate([above, x, below], axis=1)
    s_t, earlier = swap_with(sums, x[-2:], "ta", 1)
    sums = sums + s_t
    opening = jnp.concatenate([x[:1], x[:1]], axis=0)
    earlier = jnp.where(lax.axis_index("ta") == 0, opening, earlier)
    x = jnp.concatenate([earlier, x], axis=0)
    return finish_stats(sums, values), x


def fast_latent_input(values):
    sums = local_sums(values.astype(jnp.float32))
    sums = sums + swap(sums, "ta", 1)
    s_w, beside = swap_with(sums, values[:, :, :1], "wa", 1)
    sums = sums + s_w
    x = jnp.concatenate([values, beside], axis=2)
    sums, _, below = ha_round(sums, x[:, :1], x[:, :1])
    x = jnp.concatenate([x, below], axis=1)
    return finish_stats(sums, values), x


def norm_conv(values, gain, shift, kernel):
    frames, height, across, _ = values.shape
    if fast_mesh():
        stats, extended = fast_conv_input(values)
    else:
        stats = group_stats(values.astype(jnp.float32))
        extended = conv_halo(values)
    act = activate(extended.astype(jnp.float32), stats, gain, shift)
    act = jnp.where(inside_mask(height + 2, across + 2, 1), act, 0.0).astype(jnp.bfloat16)
    return valid_conv(act, kernel, frames, height, across)


def per_device(
    latents,
    norm1_gain,
    norm1_shift,
    up_weight,
    norm2_gain,
    norm2_shift,
    conv_a,
    norm3_gain,
    norm3_shift,
    conv_b,
):
    frames, height, across, channels = latents.shape
    if fast_mesh():
        stats, extended = fast_latent_input(latents)
    else:
        stats = group_stats(latents.astype(jnp.float32))
        extended = latent_halo(latents)
    activated = activate(extended.astype(jnp.float32), stats, norm1_gain, norm1_shift)
    activated = jnp.where(inside_mask(height + 1, across + 1, 0), activated, 0.0)
    lifted = upsample(activated.astype(jnp.bfloat16), up_weight).astype(jnp.bfloat16)
    hidden = norm_conv(lifted, norm2_gain, norm2_shift, conv_a).astype(jnp.bfloat16)
    branch = norm_conv(hidden, norm3_gain, norm3_shift, conv_b)
    return (lifted.astype(jnp.float32) + branch).astype(jnp.bfloat16)


def solution(mesh):
    return jax.shard_map(
        per_device,
        mesh=mesh,
        in_specs=(
            P(("videos", "ta"), "ha", "wa", None),
            P(),
            P(),
            P(),
            P(),
            P(),
            P(),
            P(),
            P(),
            P(),
        ),
        out_specs=P(("videos", "ta"), "ha", "wa", None),
        check_vma=False,
    )
```

```python
import jax
import jax.numpy as jnp
from jax import lax
from jax.sharding import PartitionSpec as P
from jax.experimental import pallas as pl
from jax.experimental.pallas import tpu as pltpu

GROUPS = 32


EPSILON = 1e-06


def passed_along(block, axis, distance):
    devices = range(lax.axis_size(axis))
    route = [(i - distance, i) for i in devices if i - distance in devices]
    return lax.ppermute(block, axis, route)


def padded_2(x, sides, width):
    for axis, dim in sides:
        size, length = (lax.axis_size(axis), x.shape[dim])
        up = [(i, (i + 1) % size) for i in range(size - 1)]
        down = [(j, i) for i, j in up]
        last = lax.slice_in_dim(x, length - width, length, axis=dim)
        initial = lax.slice_in_dim(x, 0, width, axis=dim)
        before = lax.ppermute(last, axis, up)
        after = lax.ppermute(initial, axis, down)
        x = jnp.concatenate([before, x, after], axis=dim)
    return x


def group_allreduce(x, axes):
    sizes = [lax.axis_size(a) for a in axes]
    count = 1
    for s in sizes:
        count *= s
    if count & (count - 1):
        return lax.psum(x, axes)
    index = 0
    for a, s in zip(axes, sizes):
        index = index * s + lax.axis_index(a)
    shift = 0
    while (1 << shift) < count:
        width = min(2, (count.bit_length() - 1) - shift)
        slots = 1 << width
        position = (index >> shift) % slots
        received = [x] + [
            lax.ppermute(x, axes, [(i, i ^ (d << shift)) for i in range(count)])
            for d in range(1, slots)
        ]
        ordered = []
        for j in range(slots):
            value = jnp.zeros_like(x)
            for d in range(slots):
                value = jnp.where((position ^ d) == j, received[d], value)
            ordered.append(value)
        while len(ordered) > 1:
            ordered = [ordered[k] + ordered[k + 1] for k in range(0, len(ordered), 2)]
        x = ordered[0]
        shift += width
    return x


def group_stats(values):
    channels = values.shape[-1]
    group_width = channels // GROUPS
    grouped = values.reshape(-1, GROUPS, group_width)
    entries = (
        grouped.shape[0]
        * group_width
        * lax.axis_size("ha")
        * lax.axis_size("wa")
        * lax.axis_size("ta")
    )
    totals, squares = group_allreduce(
        jnp.stack([jnp.sum(grouped, axis=(0, 2)), jnp.sum(grouped * grouped, axis=(0, 2))]),
        ("ha", "wa", "ta"),
    )
    average = totals / entries
    spread = squares / entries - average * average
    scaling = lax.rsqrt(spread + EPSILON)
    return jnp.repeat(average, group_width), jnp.repeat(scaling, group_width)


def activate(values, stats, scale_vec, shift_vec):
    average, scaling = stats
    normed = (values - average) * scaling * scale_vec + shift_vec
    return jax.nn.silu(normed)


def inside_mask(rows, cols, low_pad):
    h, h_last = lax.axis_index("ha"), lax.axis_size("ha") - 1
    w, w_last = lax.axis_index("wa"), lax.axis_size("wa") - 1
    r = jnp.arange(rows)
    c = jnp.arange(cols)
    row_ok = jnp.logical_and(
        jnp.logical_or(r >= low_pad, h > 0), jnp.logical_or(r < rows - 1, h < h_last)
    )
    col_ok = jnp.logical_and(
        jnp.logical_or(c >= low_pad, w > 0), jnp.logical_or(c < cols - 1, w < w_last)
    )
    return jnp.logical_and(row_ok[:, None], col_ok[None, :])[None, :, :, None]


def latent_halo(x):
    h_size, w_size = lax.axis_size("ha"), lax.axis_size("wa")
    below = passed_along(x[:, :1], "ha", -1)
    right = passed_along(x[:, :, :1], "wa", -1)
    corner_route = [
        ((h + 1) * w_size + w + 1, h * w_size + w)
        for h in range(h_size - 1)
        for w in range(w_size - 1)
    ]
    corner = lax.ppermute(x[:, :1, :1], ("ha", "wa"), corner_route)
    top = jnp.concatenate([x, right], axis=2)
    bottom = jnp.concatenate([below, corner], axis=2)
    return jnp.concatenate([top, bottom], axis=1)


def upsample(act, kernel):
    frames, rows, cols, channels = act.shape
    height, across = rows - 1, cols - 1
    flat = lambda v: v.reshape(-1, channels)
    dot = lambda v, w: jnp.dot(flat(v), w, preferred_element_type=jnp.float32)
    a = act[:, :height, :across]
    b = act[:, :height, 1:]
    c = act[:, 1:, :across]
    d = act[:, 1:, 1:]
    out = kernel.shape[-1]
    pa = dot(a, jnp.concatenate([kernel[1, 1], kernel[1, 2], kernel[2, 1], kernel[2, 2]], axis=1))
    pb = dot(b, jnp.concatenate([kernel[1, 0], kernel[2, 0]], axis=1))
    pc = dot(c, jnp.concatenate([kernel[0, 1], kernel[0, 2]], axis=1))
    pd = dot(d, kernel[0, 0])
    ee = pa[:, :out]
    eo = pa[:, out : 2 * out] + pb[:, :out]
    oe = pa[:, 2 * out : 3 * out] + pc[:, :out]
    oo = pa[:, 3 * out :] + pb[:, out:] + pc[:, out:] + pd
    shape = (frames, height, across, 1, out)
    even = jnp.concatenate([ee.reshape(shape), eo.reshape(shape)], axis=3)
    odd = jnp.concatenate([oe.reshape(shape), oo.reshape(shape)], axis=3)
    even = even.reshape(frames, height, 1, 2 * across, out)
    odd = odd.reshape(frames, height, 1, 2 * across, out)
    return jnp.concatenate([even, odd], axis=2).reshape(frames, 2 * height, 2 * across, out)


def tap_kernel(window_ref, weight_ref, out_ref):
    step_t, frame = pl.program_id(0), pl.program_id(1)
    part = jnp.dot(window_ref[0], weight_ref[0], preferred_element_type=jnp.float32)

    @pl.when(step_t == 0)
    def _():
        out_ref[frame] = part

    @pl.when(step_t > 0)
    def _():
        out_ref[frame] = out_ref[frame] + part


def frame_tap_dots(wide, taps, frames):
    _, rows, depth = wide.shape
    outs = taps.shape[-1]
    return pl.pallas_call(
        tap_kernel,
        grid=(3, frames),
        in_specs=[
            pl.BlockSpec((1, rows, depth), lambda t, f: (t + f, 0, 0)),
            pl.BlockSpec((1, depth, outs), lambda t, f: (t, 0, 0)),
        ],
        out_specs=pl.BlockSpec((frames, rows, outs), lambda t, f: (0, 0, 0)),
        out_shape=jax.ShapeDtypeStruct((frames, rows, outs), jnp.float32),
        compiler_params=pltpu.CompilerParams(dimension_semantics=("arbitrary", "arbitrary")),
    )(wide, taps)


def valid_conv(padded, kernel, frames, height, across):
    channels = padded.shape[-1]
    wide = jnp.concatenate(
        [padded[:, dy : dy + height, dx : dx + across] for dy in range(3) for dx in range(3)], axis=-1
    )
    wide = wide.reshape(frames + 2, height * across, 9 * channels)
    taps = kernel.reshape(3, 9 * channels, kernel.shape[-1])
    return frame_tap_dots(wide, taps, frames).reshape(frames, height, across, -1)


def conv_halo(values):
    x = padded_2(values, (("ha", 1), ("wa", 2)), 1)
    earlier = passed_along(x[-2:], "ta", 1)
    opening = jnp.concatenate([x[:1], x[:1]], axis=0)
    earlier = jnp.where(lax.axis_index("ta") == 0, opening, earlier)
    return jnp.concatenate([earlier, x], axis=0)


def swap(x, axis, distance):
    size = lax.axis_size(axis)
    return lax.ppermute(x, axis, [(i, i ^ distance) for i in range(size)])


def fast_mesh():
    return lax.axis_size("ta") == 2 and lax.axis_size("wa") == 2 and lax.axis_size("ha") == 4


def local_sums(values):
    grouped = values.reshape(-1, GROUPS, values.shape[-1] // GROUPS)
    return jnp.stack([jnp.sum(grouped, axis=(0, 2)), jnp.sum(grouped * grouped, axis=(0, 2))])


def finish_stats(sums, values):
    channels = values.shape[-1]
    group_width = channels // GROUPS
    entries = (
        values.size // GROUPS
        * lax.axis_size("ha")
        * lax.axis_size("wa")
        * lax.axis_size("ta")
    )
    average = sums[0] / entries
    spread = sums[1] / entries - average * average
    scaling = lax.rsqrt(spread + EPSILON)
    return jnp.repeat(average, group_width), jnp.repeat(scaling, group_width)


def split_high(value):
    scaled = value * 65537.0
    return scaled - (scaled - value)


def pack_sums(sums, width):
    high = split_high(sums)
    rest = sums - high
    middle = split_high(rest)
    low = rest - middle
    flat = jnp.concatenate([high.reshape(-1), middle.reshape(-1), low.reshape(-1)])
    flat = flat.astype(jnp.bfloat16)
    rows = -(-flat.size // width)
    return jnp.pad(flat, (0, rows * width - flat.size)).reshape(rows, width)


def unpack_sums(rows, like):
    flat = rows.reshape(-1)[: 3 * like.size].astype(jnp.float32).reshape(3, *like.shape)
    return (flat[0] + flat[1]) + flat[2]


def swap_with(sums, payload, axis, distance):
    width = payload.shape[-1]
    packed = pack_sums(sums, width)
    message = jnp.concatenate([payload.reshape(-1, width), packed], axis=0)
    got = swap(message, axis, distance)
    cut = got.shape[0] - packed.shape[0]
    return unpack_sums(got[cut:], sums), got[:cut].reshape(payload.shape)


def ha_round(sums, upper, lower):
    h = lax.axis_index("ha")
    to_first = jnp.where(h % 2 == 1, upper, lower)
    to_third = jnp.where(h == 2, upper, lower)
    s1, got_first = swap_with(sums, to_first, "ha", 1)
    s2 = swap(sums, "ha", 2)
    s3, got_third = swap_with(sums, to_third, "ha", 3)
    sums = (sums + s1) + (s2 + s3)
    above = jnp.where(h % 2 == 1, got_first, got_third)
    below = jnp.where(h % 2 == 0, got_first, got_third)
    return sums, above, below


def fast_conv_input(values):
    sums = local_sums(values.astype(jnp.float32))
    w = lax.axis_index("wa")
    s_w, beside = swap_with(sums, jnp.where(w == 0, values[:, :, -1:], values[:, :, :1]), "wa", 1)
    sums = sums + s_w
    x = jnp.concatenate([beside, values, beside], axis=2)
    sums, above, below = ha_round(sums, x[:, :1], x[:, -1:])
    x = jnp.concatenate([above, x, below], axis=1)
    s_t, earlier = swap_with(sums, x[-2:], "ta", 1)
    sums = sums + s_t
    opening = jnp.concatenate([x[:1], x[:1]], axis=0)
    earlier = jnp.where(lax.axis_index("ta") == 0, opening, earlier)
    x = jnp.concatenate([earlier, x], axis=0)
    return finish_stats(sums, values), x


def fast_latent_input(values):
    sums = local_sums(values.astype(jnp.float32))
    sums = sums + swap(sums, "ta", 1)
    s_w, beside = swap_with(sums, values[:, :, :1], "wa", 1)
    sums = sums + s_w
    x = jnp.concatenate([values, beside], axis=2)
    sums, _, below = ha_round(sums, x[:, :1], x[:, :1])
    x = jnp.concatenate([x, below], axis=1)
    return finish_stats(sums, values), x


def norm_conv(values, gain, shift, kernel):
    frames, height, across, _ = values.shape
    if fast_mesh():
        stats, extended = fast_conv_input(values)
    else:
        stats = group_stats(values.astype(jnp.float32))
        extended = conv_halo(values)
    act = activate(extended.astype(jnp.float32), stats, gain, shift)
    act = jnp.where(inside_mask(height + 2, across + 2, 1), act, 0.0).astype(jnp.bfloat16)
    return valid_conv(act, kernel, frames, height, across)


def per_device(
    latents,
    norm1_gain,
    norm1_shift,
    up_weight,
    norm2_gain,
    norm2_shift,
    conv_a,
    norm3_gain,
    norm3_shift,
    conv_b,
):
    frames, height, across, channels = latents.shape
    if fast_mesh():
        stats, extended = fast_latent_input(latents)
    else:
        stats = group_stats(latents.astype(jnp.float32))
        extended = latent_halo(latents)
    activated = activate(extended.astype(jnp.float32), stats, norm1_gain, norm1_shift)
    activated = jnp.where(inside_mask(height + 1, across + 1, 0), activated, 0.0)
    lifted = upsample(activated.astype(jnp.bfloat16), up_weight).astype(jnp.bfloat16)
    hidden = norm_conv(lifted, norm2_gain, norm2_shift, conv_a).astype(jnp.bfloat16)
    branch = norm_conv(hidden, norm3_gain, norm3_shift, conv_b)
    return (lifted.astype(jnp.float32) + branch).astype(jnp.bfloat16)


def solution(mesh):
    return jax.shard_map(
        per_device,
        mesh=mesh,
        in_specs=(
            P(("videos", "ta"), "ha", "wa", None),
            P(),
            P(),
            P(),
            P(),
            P(),
            P(),
            P(),
            P(),
            P(),
        ),
        out_specs=P(("videos", "ta"), "ha", "wa", None),
        check_vma=False,
    )
```

```python
import jax
import jax.numpy as jnp
from jax import lax
from jax.sharding import PartitionSpec as P

GROUPS = 32


EPSILON = 1e-06


def passed_along(block, axis, distance):
    devices = range(lax.axis_size(axis))
    route = [(i - distance, i) for i in devices if i - distance in devices]
    return lax.ppermute(block, axis, route)


def padded_2(x, sides, width):
    for axis, dim in sides:
        size, length = (lax.axis_size(axis), x.shape[dim])
        up = [(i, (i + 1) % size) for i in range(size - 1)]
        down = [(j, i) for i, j in up]
        last = lax.slice_in_dim(x, length - width, length, axis=dim)
        initial = lax.slice_in_dim(x, 0, width, axis=dim)
        before = lax.ppermute(last, axis, up)
        after = lax.ppermute(initial, axis, down)
        x = jnp.concatenate([before, x, after], axis=dim)
    return x


def group_allreduce(x, axes):
    sizes = [lax.axis_size(a) for a in axes]
    count = 1
    for s in sizes:
        count *= s
    if count & (count - 1):
        return lax.psum(x, axes)
    index = 0
    for a, s in zip(axes, sizes):
        index = index * s + lax.axis_index(a)
    shift = 0
    while (1 << shift) < count:
        width = min(2, (count.bit_length() - 1) - shift)
        slots = 1 << width
        position = (index >> shift) % slots
        received = [x] + [
            lax.ppermute(x, axes, [(i, i ^ (d << shift)) for i in range(count)])
            for d in range(1, slots)
        ]
        ordered = []
        for j in range(slots):
            value = jnp.zeros_like(x)
            for d in range(slots):
                value = jnp.where((position ^ d) == j, received[d], value)
            ordered.append(value)
        while len(ordered) > 1:
            ordered = [ordered[k] + ordered[k + 1] for k in range(0, len(ordered), 2)]
        x = ordered[0]
        shift += width
    return x


def group_stats(values):
    channels = values.shape[-1]
    group_width = channels // GROUPS
    grouped = values.reshape(-1, GROUPS, group_width)
    entries = (
        grouped.shape[0]
        * group_width
        * lax.axis_size("ha")
        * lax.axis_size("wa")
        * lax.axis_size("ta")
    )
    totals, squares = group_allreduce(
        jnp.stack([jnp.sum(grouped, axis=(0, 2)), jnp.sum(grouped * grouped, axis=(0, 2))]),
        ("ha", "wa", "ta"),
    )
    average = totals / entries
    spread = squares / entries - average * average
    scaling = lax.rsqrt(spread + EPSILON)
    return jnp.repeat(average, group_width), jnp.repeat(scaling, group_width)


def activate(values, stats, scale_vec, shift_vec):
    average, scaling = stats
    normed = (values - average) * scaling * scale_vec + shift_vec
    return jax.nn.silu(normed)


def inside_mask(rows, cols, low_pad):
    h, h_last = lax.axis_index("ha"), lax.axis_size("ha") - 1
    w, w_last = lax.axis_index("wa"), lax.axis_size("wa") - 1
    r = jnp.arange(rows)
    c = jnp.arange(cols)
    row_ok = jnp.logical_and(
        jnp.logical_or(r >= low_pad, h > 0), jnp.logical_or(r < rows - 1, h < h_last)
    )
    col_ok = jnp.logical_and(
        jnp.logical_or(c >= low_pad, w > 0), jnp.logical_or(c < cols - 1, w < w_last)
    )
    return jnp.logical_and(row_ok[:, None], col_ok[None, :])[None, :, :, None]


def latent_halo(x):
    h_size, w_size = lax.axis_size("ha"), lax.axis_size("wa")
    below = passed_along(x[:, :1], "ha", -1)
    right = passed_along(x[:, :, :1], "wa", -1)
    corner_route = [
        ((h + 1) * w_size + w + 1, h * w_size + w)
        for h in range(h_size - 1)
        for w in range(w_size - 1)
    ]
    corner = lax.ppermute(x[:, :1, :1], ("ha", "wa"), corner_route)
    top = jnp.concatenate([x, right], axis=2)
    bottom = jnp.concatenate([below, corner], axis=2)
    return jnp.concatenate([top, bottom], axis=1)


def upsample(act, kernel):
    frames, rows, cols, channels = act.shape
    height, across = rows - 1, cols - 1
    flat = lambda v: v.reshape(-1, channels)
    dot = lambda v, w: jnp.dot(flat(v), w, preferred_element_type=jnp.float32)
    a = act[:, :height, :across]
    b = act[:, :height, 1:]
    c = act[:, 1:, :across]
    d = act[:, 1:, 1:]
    out = kernel.shape[-1]
    pa = dot(a, jnp.concatenate([kernel[1, 1], kernel[1, 2], kernel[2, 1], kernel[2, 2]], axis=1))
    pb = dot(b, jnp.concatenate([kernel[1, 0], kernel[2, 0]], axis=1))
    pc = dot(c, jnp.concatenate([kernel[0, 1], kernel[0, 2]], axis=1))
    pd = dot(d, kernel[0, 0])
    ee = pa[:, :out]
    eo = pa[:, out : 2 * out] + pb[:, :out]
    oe = pa[:, 2 * out : 3 * out] + pc[:, :out]
    oo = pa[:, 3 * out :] + pb[:, out:] + pc[:, out:] + pd
    shape = (frames, height, across, 1, out)
    even = jnp.concatenate([ee.reshape(shape), eo.reshape(shape)], axis=3)
    odd = jnp.concatenate([oe.reshape(shape), oo.reshape(shape)], axis=3)
    even = even.reshape(frames, height, 1, 2 * across, out)
    odd = odd.reshape(frames, height, 1, 2 * across, out)
    return jnp.concatenate([even, odd], axis=2).reshape(frames, 2 * height, 2 * across, out)


def valid_conv(padded, kernel, frames, height, across):
    channels = padded.shape[-1]
    wide = jnp.concatenate(
        [padded[:, dy : dy + height, dx : dx + across] for dy in range(3) for dx in range(3)], axis=-1
    )
    result = None
    for step_t in range(3):
        window = wide[step_t : step_t + frames].reshape(-1, 9 * channels)
        part = jnp.dot(
            window, kernel[step_t].reshape(9 * channels, -1), preferred_element_type=jnp.float32
        )
        result = part if result is None else result + part
    return result.reshape(frames, height, across, -1)


def conv_halo(values):
    x = padded_2(values, (("ha", 1), ("wa", 2)), 1)
    earlier = passed_along(x[-2:], "ta", 1)
    opening = jnp.concatenate([x[:1], x[:1]], axis=0)
    earlier = jnp.where(lax.axis_index("ta") == 0, opening, earlier)
    return jnp.concatenate([earlier, x], axis=0)


def swap(x, axis, distance):
    size = lax.axis_size(axis)
    return lax.ppermute(x, axis, [(i, i ^ distance) for i in range(size)])


def fast_mesh():
    return lax.axis_size("ta") == 2 and lax.axis_size("wa") == 2 and lax.axis_size("ha") == 4


def local_sums(values):
    grouped = values.reshape(-1, GROUPS, values.shape[-1] // GROUPS)
    return jnp.stack([jnp.sum(grouped, axis=(0, 2)), jnp.sum(grouped * grouped, axis=(0, 2))])


def finish_stats(sums, values):
    channels = values.shape[-1]
    group_width = channels // GROUPS
    entries = (
        values.size // GROUPS
        * lax.axis_size("ha")
        * lax.axis_size("wa")
        * lax.axis_size("ta")
    )
    average = sums[0] / entries
    spread = sums[1] / entries - average * average
    scaling = lax.rsqrt(spread + EPSILON)
    return jnp.repeat(average, group_width), jnp.repeat(scaling, group_width)


def split_high(value):
    scaled = value * 65537.0
    return scaled - (scaled - value)


def pack_sums(sums, width):
    high = split_high(sums)
    rest = sums - high
    middle = split_high(rest)
    low = rest - middle
    flat = jnp.concatenate([high.reshape(-1), middle.reshape(-1), low.reshape(-1)])
    flat = flat.astype(jnp.bfloat16)
    rows = -(-flat.size // width)
    return jnp.pad(flat, (0, rows * width - flat.size)).reshape(rows, width)


def unpack_sums(rows, like):
    flat = rows.reshape(-1)[: 3 * like.size].astype(jnp.float32).reshape(3, *like.shape)
    return (flat[0] + flat[1]) + flat[2]


def swap_with(sums, payload, axis, distance):
    width = payload.shape[-1]
    packed = pack_sums(sums, width)
    message = jnp.concatenate([payload.reshape(-1, width), packed], axis=0)
    got = swap(message, axis, distance)
    cut = got.shape[0] - packed.shape[0]
    return unpack_sums(got[cut:], sums), got[:cut].reshape(payload.shape)


def ha_round(sums, upper, lower):
    h = lax.axis_index("ha")
    to_first = jnp.where(h % 2 == 1, upper, lower)
    to_third = jnp.where(h == 2, upper, lower)
    s1, got_first = swap_with(sums, to_first, "ha", 1)
    s2 = swap(sums, "ha", 2)
    s3, got_third = swap_with(sums, to_third, "ha", 3)
    sums = (sums + s1) + (s2 + s3)
    above = jnp.where(h % 2 == 1, got_first, got_third)
    below = jnp.where(h % 2 == 0, got_first, got_third)
    return sums, above, below


def fast_conv_input(values):
    sums = local_sums(values.astype(jnp.float32))
    w = lax.axis_index("wa")
    s_w, beside = swap_with(sums, jnp.where(w == 0, values[:, :, -1:], values[:, :, :1]), "wa", 1)
    sums = sums + s_w
    x = jnp.concatenate([beside, values, beside], axis=2)
    sums, above, below = ha_round(sums, x[:, :1], x[:, -1:])
    x = jnp.concatenate([above, x, below], axis=1)
    s_t, earlier = swap_with(sums, x[-2:], "ta", 1)
    sums = sums + s_t
    opening = jnp.concatenate([x[:1], x[:1]], axis=0)
    earlier = jnp.where(lax.axis_index("ta") == 0, opening, earlier)
    x = jnp.concatenate([earlier, x], axis=0)
    return finish_stats(sums, values), x


def fast_latent_input(values):
    sums = local_sums(values.astype(jnp.float32))
    s_w, beside = swap_with(sums, values[:, :, :1], "wa", 1)
    sums = sums + s_w
    x = jnp.concatenate([values, beside], axis=2)
    sums, _, below = ha_round(sums, x[:, :1], x[:, :1])
    x = jnp.concatenate([x, below], axis=1)
    sums = sums + swap(sums, "ta", 1)
    return finish_stats(sums, values), x


def norm_conv(values, gain, shift, kernel):
    frames, height, across, _ = values.shape
    if fast_mesh():
        stats, extended = fast_conv_input(values)
    else:
        stats = group_stats(values.astype(jnp.float32))
        extended = conv_halo(values)
    act = activate(extended.astype(jnp.float32), stats, gain, shift)
    act = jnp.where(inside_mask(height + 2, across + 2, 1), act, 0.0).astype(jnp.bfloat16)
    return valid_conv(act, kernel, frames, height, across)


def per_device(
    latents,
    norm1_gain,
    norm1_shift,
    up_weight,
    norm2_gain,
    norm2_shift,
    conv_a,
    norm3_gain,
    norm3_shift,
    conv_b,
):
    frames, height, across, channels = latents.shape
    if fast_mesh():
        stats, extended = fast_latent_input(latents)
    else:
        stats = group_stats(latents.astype(jnp.float32))
        extended = latent_halo(latents)
    activated = activate(extended.astype(jnp.float32), stats, norm1_gain, norm1_shift)
    activated = jnp.where(inside_mask(height + 1, across + 1, 0), activated, 0.0)
    lifted = upsample(activated.astype(jnp.bfloat16), up_weight).astype(jnp.bfloat16)
    hidden = norm_conv(lifted, norm2_gain, norm2_shift, conv_a).astype(jnp.bfloat16)
    branch = norm_conv(hidden, norm3_gain, norm3_shift, conv_b)
    return (lifted.astype(jnp.float32) + branch).astype(jnp.bfloat16)


def solution(mesh):
    return jax.shard_map(
        per_device,
        mesh=mesh,
        in_specs=(
            P(("videos", "ta"), "ha", "wa", None),
            P(),
            P(),
            P(),
            P(),
            P(),
            P(),
            P(),
            P(),
            P(),
        ),
        out_specs=P(("videos", "ta"), "ha", "wa", None),
        check_vma=False,
    )
```

```python
import jax
import jax.numpy as jnp
from jax import lax
from jax.sharding import PartitionSpec as P

GROUPS = 32


EPSILON = 1e-06


def passed_along(block, axis, distance):
    devices = range(lax.axis_size(axis))
    route = [(i - distance, i) for i in devices if i - distance in devices]
    return lax.ppermute(block, axis, route)


def padded_2(x, sides, width):
    for axis, dim in sides:
        size, length = (lax.axis_size(axis), x.shape[dim])
        up = [(i, (i + 1) % size) for i in range(size - 1)]
        down = [(j, i) for i, j in up]
        last = lax.slice_in_dim(x, length - width, length, axis=dim)
        initial = lax.slice_in_dim(x, 0, width, axis=dim)
        before = lax.ppermute(last, axis, up)
        after = lax.ppermute(initial, axis, down)
        x = jnp.concatenate([before, x, after], axis=dim)
    return x


def group_allreduce(x, axes):
    sizes = [lax.axis_size(a) for a in axes]
    count = 1
    for s in sizes:
        count *= s
    if count & (count - 1):
        return lax.psum(x, axes)
    index = 0
    for a, s in zip(axes, sizes):
        index = index * s + lax.axis_index(a)
    shift = 0
    while (1 << shift) < count:
        width = min(2, (count.bit_length() - 1) - shift)
        slots = 1 << width
        position = (index >> shift) % slots
        received = [x] + [
            lax.ppermute(x, axes, [(i, i ^ (d << shift)) for i in range(count)])
            for d in range(1, slots)
        ]
        ordered = []
        for j in range(slots):
            value = jnp.zeros_like(x)
            for d in range(slots):
                value = jnp.where((position ^ d) == j, received[d], value)
            ordered.append(value)
        while len(ordered) > 1:
            ordered = [ordered[k] + ordered[k + 1] for k in range(0, len(ordered), 2)]
        x = ordered[0]
        shift += width
    return x


def group_stats(values):
    channels = values.shape[-1]
    group_width = channels // GROUPS
    grouped = values.reshape(-1, GROUPS, group_width)
    entries = (
        grouped.shape[0]
        * group_width
        * lax.axis_size("ha")
        * lax.axis_size("wa")
        * lax.axis_size("ta")
    )
    totals, squares = group_allreduce(
        jnp.stack([jnp.sum(grouped, axis=(0, 2)), jnp.sum(grouped * grouped, axis=(0, 2))]),
        ("ha", "wa", "ta"),
    )
    average = totals / entries
    spread = squares / entries - average * average
    scaling = lax.rsqrt(spread + EPSILON)
    return jnp.repeat(average, group_width), jnp.repeat(scaling, group_width)


def activate(values, stats, scale_vec, shift_vec):
    average, scaling = stats
    normed = (values - average) * scaling * scale_vec + shift_vec
    return jax.nn.silu(normed)


def inside_mask(rows, cols, low_pad):
    h, h_last = lax.axis_index("ha"), lax.axis_size("ha") - 1
    w, w_last = lax.axis_index("wa"), lax.axis_size("wa") - 1
    r = jnp.arange(rows)
    c = jnp.arange(cols)
    row_ok = jnp.logical_and(
        jnp.logical_or(r >= low_pad, h > 0), jnp.logical_or(r < rows - 1, h < h_last)
    )
    col_ok = jnp.logical_and(
        jnp.logical_or(c >= low_pad, w > 0), jnp.logical_or(c < cols - 1, w < w_last)
    )
    return jnp.logical_and(row_ok[:, None], col_ok[None, :])[None, :, :, None]


def latent_halo(x):
    h_size, w_size = lax.axis_size("ha"), lax.axis_size("wa")
    below = passed_along(x[:, :1], "ha", -1)
    right = passed_along(x[:, :, :1], "wa", -1)
    corner_route = [
        ((h + 1) * w_size + w + 1, h * w_size + w)
        for h in range(h_size - 1)
        for w in range(w_size - 1)
    ]
    corner = lax.ppermute(x[:, :1, :1], ("ha", "wa"), corner_route)
    top = jnp.concatenate([x, right], axis=2)
    bottom = jnp.concatenate([below, corner], axis=2)
    return jnp.concatenate([top, bottom], axis=1)


def upsample(act, kernel):
    frames, rows, cols, channels = act.shape
    height, across = rows - 1, cols - 1
    flat = lambda v: v.reshape(-1, channels)
    dot = lambda v, w: jnp.dot(flat(v), w, preferred_element_type=jnp.float32)
    a = act[:, :height, :across]
    b = act[:, :height, 1:]
    c = act[:, 1:, :across]
    d = act[:, 1:, 1:]
    out = kernel.shape[-1]
    pa = dot(a, jnp.concatenate([kernel[1, 1], kernel[1, 2], kernel[2, 1], kernel[2, 2]], axis=1))
    pb = dot(b, jnp.concatenate([kernel[1, 0], kernel[2, 0]], axis=1))
    pc = dot(c, jnp.concatenate([kernel[0, 1], kernel[0, 2]], axis=1))
    pd = dot(d, kernel[0, 0])
    ee = pa[:, :out]
    eo = pa[:, out : 2 * out] + pb[:, :out]
    oe = pa[:, 2 * out : 3 * out] + pc[:, :out]
    oo = pa[:, 3 * out :] + pb[:, out:] + pc[:, out:] + pd
    shape = (frames, height, across, 1, out)
    even = jnp.concatenate([ee.reshape(shape), eo.reshape(shape)], axis=3)
    odd = jnp.concatenate([oe.reshape(shape), oo.reshape(shape)], axis=3)
    even = even.reshape(frames, height, 1, 2 * across, out)
    odd = odd.reshape(frames, height, 1, 2 * across, out)
    return jnp.concatenate([even, odd], axis=2).reshape(frames, 2 * height, 2 * across, out)


def valid_conv(padded, kernel, frames, height, across):
    channels = padded.shape[-1]
    wide = jnp.concatenate([padded[:, :, dx : dx + across] for dx in range(3)], axis=-1)
    result = None
    for step_t in range(3):
        for step_y in range(3):
            window = wide[step_t : step_t + frames, step_y : step_y + height]
            part = jnp.dot(
                window.reshape(-1, 3 * channels),
                kernel[step_t, step_y].reshape(3 * channels, -1),
                preferred_element_type=jnp.float32,
            )
            result = part if result is None else result + part
    return result.reshape(frames, height, across, -1)


def conv_halo(values):
    x = padded_2(values, (("ha", 1), ("wa", 2)), 1)
    earlier = passed_along(x[-2:], "ta", 1)
    opening = jnp.concatenate([x[:1], x[:1]], axis=0)
    earlier = jnp.where(lax.axis_index("ta") == 0, opening, earlier)
    return jnp.concatenate([earlier, x], axis=0)


def swap(x, axis, distance):
    size = lax.axis_size(axis)
    return lax.ppermute(x, axis, [(i, i ^ distance) for i in range(size)])


def fast_mesh():
    return lax.axis_size("ta") == 2 and lax.axis_size("wa") == 2 and lax.axis_size("ha") == 4


def local_sums(values):
    grouped = values.reshape(-1, GROUPS, values.shape[-1] // GROUPS)
    return jnp.stack([jnp.sum(grouped, axis=(0, 2)), jnp.sum(grouped * grouped, axis=(0, 2))])


def finish_stats(sums, values):
    channels = values.shape[-1]
    group_width = channels // GROUPS
    entries = (
        values.size // GROUPS
        * lax.axis_size("ha")
        * lax.axis_size("wa")
        * lax.axis_size("ta")
    )
    average = sums[0] / entries
    spread = sums[1] / entries - average * average
    scaling = lax.rsqrt(spread + EPSILON)
    return jnp.repeat(average, group_width), jnp.repeat(scaling, group_width)


def split_high(value):
    scaled = value * 65537.0
    return scaled - (scaled - value)


def pack_sums(sums, width):
    high = split_high(sums)
    rest = sums - high
    middle = split_high(rest)
    low = rest - middle
    flat = jnp.concatenate([high.reshape(-1), middle.reshape(-1), low.reshape(-1)])
    flat = flat.astype(jnp.bfloat16)
    rows = -(-flat.size // width)
    return jnp.pad(flat, (0, rows * width - flat.size)).reshape(rows, width)


def unpack_sums(rows, like):
    flat = rows.reshape(-1)[: 3 * like.size].astype(jnp.float32).reshape(3, *like.shape)
    return (flat[0] + flat[1]) + flat[2]


def swap_with(sums, payload, axis, distance):
    width = payload.shape[-1]
    packed = pack_sums(sums, width)
    message = jnp.concatenate([payload.reshape(-1, width), packed], axis=0)
    got = swap(message, axis, distance)
    cut = got.shape[0] - packed.shape[0]
    return unpack_sums(got[cut:], sums), got[:cut].reshape(payload.shape)


def ha_round(sums, upper, lower):
    h = lax.axis_index("ha")
    to_first = jnp.where(h % 2 == 1, upper, lower)
    to_third = jnp.where(h == 2, upper, lower)
    s1, got_first = swap_with(sums, to_first, "ha", 1)
    s2 = swap(sums, "ha", 2)
    s3, got_third = swap_with(sums, to_third, "ha", 3)
    sums = (sums + s1) + (s2 + s3)
    above = jnp.where(h % 2 == 1, got_first, got_third)
    below = jnp.where(h % 2 == 0, got_first, got_third)
    return sums, above, below


def fast_conv_input(values):
    sums = local_sums(values.astype(jnp.float32))
    w = lax.axis_index("wa")
    s_w, beside = swap_with(sums, jnp.where(w == 0, values[:, :, -1:], values[:, :, :1]), "wa", 1)
    sums = sums + s_w
    x = jnp.concatenate([beside, values, beside], axis=2)
    sums, above, below = ha_round(sums, x[:, :1], x[:, -1:])
    x = jnp.concatenate([above, x, below], axis=1)
    s_t, earlier = swap_with(sums, x[-2:], "ta", 1)
    sums = sums + s_t
    opening = jnp.concatenate([x[:1], x[:1]], axis=0)
    earlier = jnp.where(lax.axis_index("ta") == 0, opening, earlier)
    x = jnp.concatenate([earlier, x], axis=0)
    return finish_stats(sums, values), x


def fast_latent_input(values):
    sums = local_sums(values.astype(jnp.float32))
    sums = sums + swap(sums, "ta", 1)
    s_w, beside = swap_with(sums, values[:, :, :1], "wa", 1)
    sums = sums + s_w
    x = jnp.concatenate([values, beside], axis=2)
    sums, _, below = ha_round(sums, x[:, :1], x[:, :1])
    x = jnp.concatenate([x, below], axis=1)
    return finish_stats(sums, values), x


def norm_conv(values, gain, shift, kernel):
    frames, height, across, _ = values.shape
    if fast_mesh():
        stats, extended = fast_conv_input(values)
    else:
        stats = group_stats(values.astype(jnp.float32))
        extended = conv_halo(values)
    act = activate(extended.astype(jnp.float32), stats, gain, shift)
    act = jnp.where(inside_mask(height + 2, across + 2, 1), act, 0.0).astype(jnp.bfloat16)
    return valid_conv(act, kernel, frames, height, across)


def per_device(
    latents,
    norm1_gain,
    norm1_shift,
    up_weight,
    norm2_gain,
    norm2_shift,
    conv_a,
    norm3_gain,
    norm3_shift,
    conv_b,
):
    frames, height, across, channels = latents.shape
    if fast_mesh():
        stats, extended = fast_latent_input(latents)
    else:
        stats = group_stats(latents.astype(jnp.float32))
        extended = latent_halo(latents)
    activated = activate(extended.astype(jnp.float32), stats, norm1_gain, norm1_shift)
    activated = jnp.where(inside_mask(height + 1, across + 1, 0), activated, 0.0)
    lifted = upsample(activated.astype(jnp.bfloat16), up_weight).astype(jnp.bfloat16)
    hidden = norm_conv(lifted, norm2_gain, norm2_shift, conv_a).astype(jnp.bfloat16)
    branch = norm_conv(hidden, norm3_gain, norm3_shift, conv_b)
    return (lifted.astype(jnp.float32) + branch).astype(jnp.bfloat16)


def solution(mesh):
    return jax.shard_map(
        per_device,
        mesh=mesh,
        in_specs=(
            P(("videos", "ta"), "ha", "wa", None),
            P(),
            P(),
            P(),
            P(),
            P(),
            P(),
            P(),
            P(),
            P(),
        ),
        out_specs=P(("videos", "ta"), "ha", "wa", None),
        check_vma=False,
    )
```

```python
import jax
import jax.numpy as jnp
from jax import lax
from jax.sharding import PartitionSpec as P

GROUPS = 32


EPSILON = 1e-06


def passed_along(block, axis, distance):
    devices = range(lax.axis_size(axis))
    route = [(i - distance, i) for i in devices if i - distance in devices]
    return lax.ppermute(block, axis, route)


def padded_2(x, sides, width):
    for axis, dim in sides:
        size, length = (lax.axis_size(axis), x.shape[dim])
        up = [(i, (i + 1) % size) for i in range(size - 1)]
        down = [(j, i) for i, j in up]
        last = lax.slice_in_dim(x, length - width, length, axis=dim)
        initial = lax.slice_in_dim(x, 0, width, axis=dim)
        before = lax.ppermute(last, axis, up)
        after = lax.ppermute(initial, axis, down)
        x = jnp.concatenate([before, x, after], axis=dim)
    return x


def group_allreduce(x, axes):
    sizes = [lax.axis_size(a) for a in axes]
    count = 1
    for s in sizes:
        count *= s
    if count & (count - 1):
        return lax.psum(x, axes)
    index = 0
    for a, s in zip(axes, sizes):
        index = index * s + lax.axis_index(a)
    shift = 0
    while (1 << shift) < count:
        width = min(2, (count.bit_length() - 1) - shift)
        slots = 1 << width
        position = (index >> shift) % slots
        received = [x] + [
            lax.ppermute(x, axes, [(i, i ^ (d << shift)) for i in range(count)])
            for d in range(1, slots)
        ]
        ordered = []
        for j in range(slots):
            value = jnp.zeros_like(x)
            for d in range(slots):
                value = jnp.where((position ^ d) == j, received[d], value)
            ordered.append(value)
        while len(ordered) > 1:
            ordered = [ordered[k] + ordered[k + 1] for k in range(0, len(ordered), 2)]
        x = ordered[0]
        shift += width
    return x


def group_stats(values):
    channels = values.shape[-1]
    group_width = channels // GROUPS
    grouped = values.reshape(-1, GROUPS, group_width)
    entries = (
        grouped.shape[0]
        * group_width
        * lax.axis_size("ha")
        * lax.axis_size("wa")
        * lax.axis_size("ta")
    )
    totals, squares = group_allreduce(
        jnp.stack([jnp.sum(grouped, axis=(0, 2)), jnp.sum(grouped * grouped, axis=(0, 2))]),
        ("ha", "wa", "ta"),
    )
    average = totals / entries
    spread = squares / entries - average * average
    scaling = lax.rsqrt(spread + EPSILON)
    return jnp.repeat(average, group_width), jnp.repeat(scaling, group_width)


def activate(values, stats, scale_vec, shift_vec):
    average, scaling = stats
    normed = (values - average) * scaling * scale_vec + shift_vec
    return 0.5 * normed * (1.0 + jnp.tanh(0.5 * normed))


def inside_mask(rows, cols, low_pad):
    h, h_last = lax.axis_index("ha"), lax.axis_size("ha") - 1
    w, w_last = lax.axis_index("wa"), lax.axis_size("wa") - 1
    r = jnp.arange(rows)
    c = jnp.arange(cols)
    row_ok = jnp.logical_and(
        jnp.logical_or(r >= low_pad, h > 0), jnp.logical_or(r < rows - 1, h < h_last)
    )
    col_ok = jnp.logical_and(
        jnp.logical_or(c >= low_pad, w > 0), jnp.logical_or(c < cols - 1, w < w_last)
    )
    return jnp.logical_and(row_ok[:, None], col_ok[None, :])[None, :, :, None]


def latent_halo(x):
    h_size, w_size = lax.axis_size("ha"), lax.axis_size("wa")
    below = passed_along(x[:, :1], "ha", -1)
    right = passed_along(x[:, :, :1], "wa", -1)
    corner_route = [
        ((h + 1) * w_size + w + 1, h * w_size + w)
        for h in range(h_size - 1)
        for w in range(w_size - 1)
    ]
    corner = lax.ppermute(x[:, :1, :1], ("ha", "wa"), corner_route)
    top = jnp.concatenate([x, right], axis=2)
    bottom = jnp.concatenate([below, corner], axis=2)
    return jnp.concatenate([top, bottom], axis=1)


def upsample(act, kernel):
    frames, rows, cols, channels = act.shape
    height, across = rows - 1, cols - 1
    flat = lambda v: v.reshape(-1, channels)
    dot = lambda v, w: jnp.dot(flat(v), w, preferred_element_type=jnp.float32)
    a = act[:, :height, :across]
    b = act[:, :height, 1:]
    c = act[:, 1:, :across]
    d = act[:, 1:, 1:]
    out = kernel.shape[-1]
    pa = dot(a, jnp.concatenate([kernel[1, 1], kernel[1, 2], kernel[2, 1], kernel[2, 2]], axis=1))
    pb = dot(b, jnp.concatenate([kernel[1, 0], kernel[2, 0]], axis=1))
    pc = dot(c, jnp.concatenate([kernel[0, 1], kernel[0, 2]], axis=1))
    pd = dot(d, kernel[0, 0])
    ee = pa[:, :out]
    eo = pa[:, out : 2 * out] + pb[:, :out]
    oe = pa[:, 2 * out : 3 * out] + pc[:, :out]
    oo = pa[:, 3 * out :] + pb[:, out:] + pc[:, out:] + pd
    shape = (frames, height, across, 1, out)
    even = jnp.concatenate([ee.reshape(shape), eo.reshape(shape)], axis=3)
    odd = jnp.concatenate([oe.reshape(shape), oo.reshape(shape)], axis=3)
    even = even.reshape(frames, height, 1, 2 * across, out)
    odd = odd.reshape(frames, height, 1, 2 * across, out)
    return jnp.concatenate([even, odd], axis=2).reshape(frames, 2 * height, 2 * across, out)


def valid_conv(padded, kernel, frames, height, across):
    channels = padded.shape[-1]
    wide = jnp.concatenate(
        [padded[:, dy : dy + height, dx : dx + across] for dy in range(3) for dx in range(3)], axis=-1
    )
    result = None
    for step_t in range(3):
        window = wide[step_t : step_t + frames].reshape(-1, 9 * channels)
        part = jnp.dot(
            window, kernel[step_t].reshape(9 * channels, -1), preferred_element_type=jnp.float32
        )
        result = part if result is None else result + part
    return result.reshape(frames, height, across, -1)


def conv_halo(values):
    x = padded_2(values, (("ha", 1), ("wa", 2)), 1)
    earlier = passed_along(x[-2:], "ta", 1)
    opening = jnp.concatenate([x[:1], x[:1]], axis=0)
    earlier = jnp.where(lax.axis_index("ta") == 0, opening, earlier)
    return jnp.concatenate([earlier, x], axis=0)


def swap(x, axis, distance):
    size = lax.axis_size(axis)
    return lax.ppermute(x, axis, [(i, i ^ distance) for i in range(size)])


def fast_mesh():
    return lax.axis_size("ta") == 2 and lax.axis_size("wa") == 2 and lax.axis_size("ha") == 4


def local_sums(values):
    grouped = values.reshape(-1, GROUPS, values.shape[-1] // GROUPS)
    return jnp.stack([jnp.sum(grouped, axis=(0, 2)), jnp.sum(grouped * grouped, axis=(0, 2))])


def finish_stats(sums, values):
    channels = values.shape[-1]
    group_width = channels // GROUPS
    entries = (
        values.size // GROUPS
        * lax.axis_size("ha")
        * lax.axis_size("wa")
        * lax.axis_size("ta")
    )
    average = sums[0] / entries
    spread = sums[1] / entries - average * average
    scaling = lax.rsqrt(spread + EPSILON)
    return jnp.repeat(average, group_width), jnp.repeat(scaling, group_width)


def split_high(value):
    scaled = value * 65537.0
    return scaled - (scaled - value)


def pack_sums(sums, width):
    high = split_high(sums)
    rest = sums - high
    middle = split_high(rest)
    low = rest - middle
    flat = jnp.concatenate([high.reshape(-1), middle.reshape(-1), low.reshape(-1)])
    flat = flat.astype(jnp.bfloat16)
    rows = -(-flat.size // width)
    return jnp.pad(flat, (0, rows * width - flat.size)).reshape(rows, width)


def unpack_sums(rows, like):
    flat = rows.reshape(-1)[: 3 * like.size].astype(jnp.float32).reshape(3, *like.shape)
    return (flat[0] + flat[1]) + flat[2]


def swap_with(sums, payload, axis, distance):
    width = payload.shape[-1]
    packed = pack_sums(sums, width)
    message = jnp.concatenate([payload.reshape(-1, width), packed], axis=0)
    got = swap(message, axis, distance)
    cut = got.shape[0] - packed.shape[0]
    return unpack_sums(got[cut:], sums), got[:cut].reshape(payload.shape)


def ha_round(sums, upper, lower):
    h = lax.axis_index("ha")
    to_first = jnp.where(h % 2 == 1, upper, lower)
    to_third = jnp.where(h == 2, upper, lower)
    s1, got_first = swap_with(sums, to_first, "ha", 1)
    s2 = swap(sums, "ha", 2)
    s3, got_third = swap_with(sums, to_third, "ha", 3)
    sums = (sums + s1) + (s2 + s3)
    above = jnp.where(h % 2 == 1, got_first, got_third)
    below = jnp.where(h % 2 == 0, got_first, got_third)
    return sums, above, below


def fast_conv_input(values):
    sums = local_sums(values.astype(jnp.float32))
    w = lax.axis_index("wa")
    s_w, beside = swap_with(sums, jnp.where(w == 0, values[:, :, -1:], values[:, :, :1]), "wa", 1)
    sums = sums + s_w
    x = jnp.concatenate([beside, values, beside], axis=2)
    sums, above, below = ha_round(sums, x[:, :1], x[:, -1:])
    x = jnp.concatenate([above, x, below], axis=1)
    s_t, earlier = swap_with(sums, x[-2:], "ta", 1)
    sums = sums + s_t
    opening = jnp.concatenate([x[:1], x[:1]], axis=0)
    earlier = jnp.where(lax.axis_index("ta") == 0, opening, earlier)
    x = jnp.concatenate([earlier, x], axis=0)
    return finish_stats(sums, values), x


def fast_latent_input(values):
    sums = local_sums(values.astype(jnp.float32))
    sums = sums + swap(sums, "ta", 1)
    s_w, beside = swap_with(sums, values[:, :, :1], "wa", 1)
    sums = sums + s_w
    x = jnp.concatenate([values, beside], axis=2)
    sums, _, below = ha_round(sums, x[:, :1], x[:, :1])
    x = jnp.concatenate([x, below], axis=1)
    return finish_stats(sums, values), x


def norm_conv(values, gain, shift, kernel):
    frames, height, across, _ = values.shape
    if fast_mesh():
        stats, extended = fast_conv_input(values)
    else:
        stats = group_stats(values.astype(jnp.float32))
        extended = conv_halo(values)
    act = activate(extended.astype(jnp.float32), stats, gain, shift)
    act = jnp.where(inside_mask(height + 2, across + 2, 1), act, 0.0).astype(jnp.bfloat16)
    return valid_conv(act, kernel, frames, height, across)


def per_device(
    latents,
    norm1_gain,
    norm1_shift,
    up_weight,
    norm2_gain,
    norm2_shift,
    conv_a,
    norm3_gain,
    norm3_shift,
    conv_b,
):
    frames, height, across, channels = latents.shape
    if fast_mesh():
        stats, extended = fast_latent_input(latents)
    else:
        stats = group_stats(latents.astype(jnp.float32))
        extended = latent_halo(latents)
    activated = activate(extended.astype(jnp.float32), stats, norm1_gain, norm1_shift)
    activated = jnp.where(inside_mask(height + 1, across + 1, 0), activated, 0.0)
    lifted = upsample(activated.astype(jnp.bfloat16), up_weight).astype(jnp.bfloat16)
    hidden = norm_conv(lifted, norm2_gain, norm2_shift, conv_a).astype(jnp.bfloat16)
    branch = norm_conv(hidden, norm3_gain, norm3_shift, conv_b)
    return (lifted.astype(jnp.float32) + branch).astype(jnp.bfloat16)


def solution(mesh):
    return jax.shard_map(
        per_device,
        mesh=mesh,
        in_specs=(
            P(("videos", "ta"), "ha", "wa", None),
            P(),
            P(),
            P(),
            P(),
            P(),
            P(),
            P(),
            P(),
            P(),
        ),
        out_specs=P(("videos", "ta"), "ha", "wa", None),
        check_vma=False,
    )
```

```python
import jax
import jax.numpy as jnp
from jax import lax
from jax.sharding import PartitionSpec as P

GROUPS = 32


EPSILON = 1e-06


def passed_along(block, axis, distance):
    devices = range(lax.axis_size(axis))
    route = [(i - distance, i) for i in devices if i - distance in devices]
    return lax.ppermute(block, axis, route)


def padded_2(x, sides, width):
    for axis, dim in sides:
        size, length = (lax.axis_size(axis), x.shape[dim])
        up = [(i, (i + 1) % size) for i in range(size - 1)]
        down = [(j, i) for i, j in up]
        last = lax.slice_in_dim(x, length - width, length, axis=dim)
        initial = lax.slice_in_dim(x, 0, width, axis=dim)
        before = lax.ppermute(last, axis, up)
        after = lax.ppermute(initial, axis, down)
        x = jnp.concatenate([before, x, after], axis=dim)
    return x


def group_allreduce(x, axes):
    sizes = [lax.axis_size(a) for a in axes]
    count = 1
    for s in sizes:
        count *= s
    if count & (count - 1):
        return lax.psum(x, axes)
    index = 0
    for a, s in zip(axes, sizes):
        index = index * s + lax.axis_index(a)
    shift = 0
    while (1 << shift) < count:
        width = min(2, (count.bit_length() - 1) - shift)
        slots = 1 << width
        position = (index >> shift) % slots
        received = [x] + [
            lax.ppermute(x, axes, [(i, i ^ (d << shift)) for i in range(count)])
            for d in range(1, slots)
        ]
        ordered = []
        for j in range(slots):
            value = jnp.zeros_like(x)
            for d in range(slots):
                value = jnp.where((position ^ d) == j, received[d], value)
            ordered.append(value)
        while len(ordered) > 1:
            ordered = [ordered[k] + ordered[k + 1] for k in range(0, len(ordered), 2)]
        x = ordered[0]
        shift += width
    return x


def group_stats(values):
    channels = values.shape[-1]
    group_width = channels // GROUPS
    grouped = values.reshape(-1, GROUPS, group_width)
    entries = (
        grouped.shape[0]
        * group_width
        * lax.axis_size("ha")
        * lax.axis_size("wa")
        * lax.axis_size("ta")
    )
    totals, squares = group_allreduce(
        jnp.stack([jnp.sum(grouped, axis=(0, 2)), jnp.sum(grouped * grouped, axis=(0, 2))]),
        ("ha", "wa", "ta"),
    )
    average = totals / entries
    spread = squares / entries - average * average
    scaling = lax.rsqrt(spread + EPSILON)
    return jnp.repeat(average, group_width), jnp.repeat(scaling, group_width)


def activate(values, stats, scale_vec, shift_vec):
    average, scaling = stats
    normed = (values - average) * scaling * scale_vec + shift_vec
    return jax.nn.silu(normed)


def inside_mask(rows, cols, low_pad):
    h, h_last = lax.axis_index("ha"), lax.axis_size("ha") - 1
    w, w_last = lax.axis_index("wa"), lax.axis_size("wa") - 1
    r = jnp.arange(rows)
    c = jnp.arange(cols)
    row_ok = jnp.logical_and(
        jnp.logical_or(r >= low_pad, h > 0), jnp.logical_or(r < rows - 1, h < h_last)
    )
    col_ok = jnp.logical_and(
        jnp.logical_or(c >= low_pad, w > 0), jnp.logical_or(c < cols - 1, w < w_last)
    )
    return jnp.logical_and(row_ok[:, None], col_ok[None, :])[None, :, :, None]


def latent_halo(x):
    h_size, w_size = lax.axis_size("ha"), lax.axis_size("wa")
    below = passed_along(x[:, :1], "ha", -1)
    right = passed_along(x[:, :, :1], "wa", -1)
    corner_route = [
        ((h + 1) * w_size + w + 1, h * w_size + w)
        for h in range(h_size - 1)
        for w in range(w_size - 1)
    ]
    corner = lax.ppermute(x[:, :1, :1], ("ha", "wa"), corner_route)
    top = jnp.concatenate([x, right], axis=2)
    bottom = jnp.concatenate([below, corner], axis=2)
    return jnp.concatenate([top, bottom], axis=1)


def upsample(act, kernel):
    frames, rows, cols, channels = act.shape
    height, across = rows - 1, cols - 1
    flat = lambda v: v.reshape(-1, channels)
    dot = lambda v, w: jnp.dot(flat(v), w, preferred_element_type=jnp.float32)
    a = act[:, :height, :across]
    b = act[:, :height, 1:]
    c = act[:, 1:, :across]
    d = act[:, 1:, 1:]
    out = kernel.shape[-1]
    pa = dot(a, jnp.concatenate([kernel[1, 1], kernel[1, 2], kernel[2, 1], kernel[2, 2]], axis=1))
    pb = dot(b, jnp.concatenate([kernel[1, 0], kernel[2, 0]], axis=1))
    pc = dot(c, jnp.concatenate([kernel[0, 1], kernel[0, 2]], axis=1))
    pd = dot(d, kernel[0, 0])
    ee = pa[:, :out]
    eo = pa[:, out : 2 * out] + pb[:, :out]
    oe = pa[:, 2 * out : 3 * out] + pc[:, :out]
    oo = pa[:, 3 * out :] + pb[:, out:] + pc[:, out:] + pd
    shape = (frames, height, across, 1, out)
    even = jnp.concatenate([ee.reshape(shape), eo.reshape(shape)], axis=3)
    odd = jnp.concatenate([oe.reshape(shape), oo.reshape(shape)], axis=3)
    even = even.reshape(frames, height, 1, 2 * across, out)
    odd = odd.reshape(frames, height, 1, 2 * across, out)
    return jnp.concatenate([even, odd], axis=2).reshape(frames, 2 * height, 2 * across, out)


def valid_conv(padded, kernel, frames, height, across):
    channels = padded.shape[-1]
    wide = jnp.concatenate(
        [padded[:, dy : dy + height, dx : dx + across] for dy in range(3) for dx in range(3)], axis=-1
    )
    result = None
    for step_t in range(3):
        window = wide[step_t : step_t + frames].reshape(-1, 9 * channels)
        part = jnp.dot(
            window, kernel[step_t].reshape(9 * channels, -1), preferred_element_type=jnp.float32
        )
        result = part if result is None else result + part
    return result.reshape(frames, height, across, -1)


def conv_halo(values):
    x = padded_2(values, (("ha", 1), ("wa", 2)), 1)
    earlier = passed_along(x[-2:], "ta", 1)
    opening = jnp.concatenate([x[:1], x[:1]], axis=0)
    earlier = jnp.where(lax.axis_index("ta") == 0, opening, earlier)
    return jnp.concatenate([earlier, x], axis=0)


def swap(x, axis, distance):
    size = lax.axis_size(axis)
    return lax.ppermute(x, axis, [(i, i ^ distance) for i in range(size)])


def fast_mesh():
    return lax.axis_size("ta") == 2 and lax.axis_size("wa") == 2 and lax.axis_size("ha") == 4


def local_sums(values):
    grouped = values.reshape(-1, GROUPS, values.shape[-1] // GROUPS)
    return jnp.stack([jnp.sum(grouped, axis=(0, 2)), jnp.sum(grouped * grouped, axis=(0, 2))])


def finish_stats(sums, values):
    channels = values.shape[-1]
    group_width = channels // GROUPS
    entries = (
        values.size // GROUPS
        * lax.axis_size("ha")
        * lax.axis_size("wa")
        * lax.axis_size("ta")
    )
    average = sums[0] / entries
    spread = sums[1] / entries - average * average
    scaling = lax.rsqrt(spread + EPSILON)
    return jnp.repeat(average, group_width), jnp.repeat(scaling, group_width)


def split_high(value):
    scaled = value * 65537.0
    return scaled - (scaled - value)


def pack_sums(sums, width):
    high = split_high(sums)
    rest = sums - high
    middle = split_high(rest)
    low = rest - middle
    flat = jnp.concatenate([high.reshape(-1), middle.reshape(-1), low.reshape(-1)])
    flat = flat.astype(jnp.bfloat16)
    rows = -(-flat.size // width)
    return jnp.pad(flat, (0, rows * width - flat.size)).reshape(rows, width)


def unpack_sums(rows, like):
    flat = rows.reshape(-1)[: 3 * like.size].astype(jnp.float32).reshape(3, *like.shape)
    return (flat[0] + flat[1]) + flat[2]


def swap_with(sums, payload, axis, distance):
    width = payload.shape[-1]
    packed = pack_sums(sums, width)
    message = jnp.concatenate([payload.reshape(-1, width), packed], axis=0)
    got = swap(message, axis, distance)
    cut = got.shape[0] - packed.shape[0]
    return unpack_sums(got[cut:], sums), got[:cut].reshape(payload.shape)


def ha_round(sums, upper, lower):
    h = lax.axis_index("ha")
    to_first = jnp.where(h % 2 == 1, upper, lower)
    to_third = jnp.where(h == 2, upper, lower)
    s1, got_first = swap_with(sums, to_first, "ha", 1)
    s2 = swap(sums, "ha", 2)
    s3, got_third = swap_with(sums, to_third, "ha", 3)
    sums = (sums + s1) + (s2 + s3)
    above = jnp.where(h % 2 == 1, got_first, got_third)
    below = jnp.where(h % 2 == 0, got_first, got_third)
    return sums, above, below


def fast_conv_input(values):
    sums = local_sums(values.astype(jnp.float32))
    sums, above, below = ha_round(sums, values[:, :1], values[:, -1:])
    x = jnp.concatenate([above, values, below], axis=1)
    w = lax.axis_index("wa")
    s_w, beside = swap_with(sums, jnp.where(w == 0, x[:, :, -1:], x[:, :, :1]), "wa", 1)
    sums = sums + s_w
    x = jnp.concatenate([beside, x, beside], axis=2)
    s_t, earlier = swap_with(sums, x[-2:], "ta", 1)
    sums = sums + s_t
    opening = jnp.concatenate([x[:1], x[:1]], axis=0)
    earlier = jnp.where(lax.axis_index("ta") == 0, opening, earlier)
    x = jnp.concatenate([earlier, x], axis=0)
    return finish_stats(sums, values), x


def fast_latent_input(values):
    sums = local_sums(values.astype(jnp.float32))
    sums = sums + swap(sums, "ta", 1)
    sums, _, below = ha_round(sums, values[:, :1], values[:, :1])
    x = jnp.concatenate([values, below], axis=1)
    s_w, beside = swap_with(sums, x[:, :, :1], "wa", 1)
    sums = sums + s_w
    x = jnp.concatenate([x, beside], axis=2)
    return finish_stats(sums, values), x


def norm_conv(values, gain, shift, kernel):
    frames, height, across, _ = values.shape
    if fast_mesh():
        stats, extended = fast_conv_input(values)
    else:
        stats = group_stats(values.astype(jnp.float32))
        extended = conv_halo(values)
    act = activate(extended.astype(jnp.float32), stats, gain, shift)
    act = jnp.where(inside_mask(height + 2, across + 2, 1), act, 0.0).astype(jnp.bfloat16)
    return valid_conv(act, kernel, frames, height, across)


def per_device(
    latents,
    norm1_gain,
    norm1_shift,
    up_weight,
    norm2_gain,
    norm2_shift,
    conv_a,
    norm3_gain,
    norm3_shift,
    conv_b,
):
    frames, height, across, channels = latents.shape
    if fast_mesh():
        stats, extended = fast_latent_input(latents)
    else:
        stats = group_stats(latents.astype(jnp.float32))
        extended = latent_halo(latents)
    activated = activate(extended.astype(jnp.float32), stats, norm1_gain, norm1_shift)
    activated = jnp.where(inside_mask(height + 1, across + 1, 0), activated, 0.0)
    lifted = upsample(activated.astype(jnp.bfloat16), up_weight).astype(jnp.bfloat16)
    hidden = norm_conv(lifted, norm2_gain, norm2_shift, conv_a).astype(jnp.bfloat16)
    branch = norm_conv(hidden, norm3_gain, norm3_shift, conv_b)
    return (lifted.astype(jnp.float32) + branch).astype(jnp.bfloat16)


def solution(mesh):
    return jax.shard_map(
        per_device,
        mesh=mesh,
        in_specs=(
            P(("videos", "ta"), "ha", "wa", None),
            P(),
            P(),
            P(),
            P(),
            P(),
            P(),
            P(),
            P(),
            P(),
        ),
        out_specs=P(("videos", "ta"), "ha", "wa", None),
        check_vma=False,
    )
```

```python
import jax
import jax.numpy as jnp
from jax import lax
from jax.sharding import PartitionSpec as P

GROUPS = 32


EPSILON = 1e-06


def passed_along(block, axis, distance):
    devices = range(lax.axis_size(axis))
    route = [(i - distance, i) for i in devices if i - distance in devices]
    return lax.ppermute(block, axis, route)


def padded_2(x, sides, width):
    for axis, dim in sides:
        size, length = (lax.axis_size(axis), x.shape[dim])
        up = [(i, (i + 1) % size) for i in range(size - 1)]
        down = [(j, i) for i, j in up]
        last = lax.slice_in_dim(x, length - width, length, axis=dim)
        initial = lax.slice_in_dim(x, 0, width, axis=dim)
        before = lax.ppermute(last, axis, up)
        after = lax.ppermute(initial, axis, down)
        x = jnp.concatenate([before, x, after], axis=dim)
    return x


def group_allreduce(x, axes):
    sizes = [lax.axis_size(a) for a in axes]
    count = 1
    for s in sizes:
        count *= s
    if count & (count - 1):
        return lax.psum(x, axes)
    index = 0
    for a, s in zip(axes, sizes):
        index = index * s + lax.axis_index(a)
    shift = 0
    while (1 << shift) < count:
        width = min(2, (count.bit_length() - 1) - shift)
        slots = 1 << width
        position = (index >> shift) % slots
        received = [x] + [
            lax.ppermute(x, axes, [(i, i ^ (d << shift)) for i in range(count)])
            for d in range(1, slots)
        ]
        ordered = []
        for j in range(slots):
            value = jnp.zeros_like(x)
            for d in range(slots):
                value = jnp.where((position ^ d) == j, received[d], value)
            ordered.append(value)
        while len(ordered) > 1:
            ordered = [ordered[k] + ordered[k + 1] for k in range(0, len(ordered), 2)]
        x = ordered[0]
        shift += width
    return x


def group_stats(values):
    channels = values.shape[-1]
    group_width = channels // GROUPS
    grouped = values.reshape(-1, GROUPS, group_width)
    entries = (
        grouped.shape[0]
        * group_width
        * lax.axis_size("ha")
        * lax.axis_size("wa")
        * lax.axis_size("ta")
    )
    totals, squares = group_allreduce(
        jnp.stack([jnp.sum(grouped, axis=(0, 2)), jnp.sum(grouped * grouped, axis=(0, 2))]),
        ("ha", "wa", "ta"),
    )
    average = totals / entries
    spread = squares / entries - average * average
    scaling = lax.rsqrt(spread + EPSILON)
    return jnp.repeat(average, group_width), jnp.repeat(scaling, group_width)


def activate(values, stats, scale_vec, shift_vec):
    average, scaling = stats
    normed = (values - average) * scaling * scale_vec + shift_vec
    return jax.nn.silu(normed)


def inside_mask(rows, cols, low_pad):
    h, h_last = lax.axis_index("ha"), lax.axis_size("ha") - 1
    w, w_last = lax.axis_index("wa"), lax.axis_size("wa") - 1
    r = jnp.arange(rows)
    c = jnp.arange(cols)
    row_ok = jnp.logical_and(
        jnp.logical_or(r >= low_pad, h > 0), jnp.logical_or(r < rows - 1, h < h_last)
    )
    col_ok = jnp.logical_and(
        jnp.logical_or(c >= low_pad, w > 0), jnp.logical_or(c < cols - 1, w < w_last)
    )
    return jnp.logical_and(row_ok[:, None], col_ok[None, :])[None, :, :, None]


def latent_halo(x):
    h_size, w_size = lax.axis_size("ha"), lax.axis_size("wa")
    below = passed_along(x[:, :1], "ha", -1)
    right = passed_along(x[:, :, :1], "wa", -1)
    corner_route = [
        ((h + 1) * w_size + w + 1, h * w_size + w)
        for h in range(h_size - 1)
        for w in range(w_size - 1)
    ]
    corner = lax.ppermute(x[:, :1, :1], ("ha", "wa"), corner_route)
    top = jnp.concatenate([x, right], axis=2)
    bottom = jnp.concatenate([below, corner], axis=2)
    return jnp.concatenate([top, bottom], axis=1)


def upsample(act, kernel):
    frames, rows, cols, channels = act.shape
    height, across = rows - 1, cols - 1
    flat = lambda v: v.reshape(-1, channels)
    dot = lambda v, w: jnp.dot(flat(v), w, preferred_element_type=jnp.float32)
    a = act[:, :height, :across]
    b = act[:, :height, 1:]
    c = act[:, 1:, :across]
    d = act[:, 1:, 1:]
    out = kernel.shape[-1]
    pa = dot(a, jnp.concatenate([kernel[1, 1], kernel[1, 2], kernel[2, 1], kernel[2, 2]], axis=1))
    pb = dot(b, jnp.concatenate([kernel[1, 0], kernel[2, 0]], axis=1))
    pc = dot(c, jnp.concatenate([kernel[0, 1], kernel[0, 2]], axis=1))
    pd = dot(d, kernel[0, 0])
    ee = pa[:, :out]
    eo = pa[:, out : 2 * out] + pb[:, :out]
    oe = pa[:, 2 * out : 3 * out] + pc[:, :out]
    oo = pa[:, 3 * out :] + pb[:, out:] + pc[:, out:] + pd
    shape = (frames, height, across, 1, out)
    even = jnp.concatenate([ee.reshape(shape), eo.reshape(shape)], axis=3)
    odd = jnp.concatenate([oe.reshape(shape), oo.reshape(shape)], axis=3)
    even = even.reshape(frames, height, 1, 2 * across, out)
    odd = odd.reshape(frames, height, 1, 2 * across, out)
    return jnp.concatenate([even, odd], axis=2).reshape(frames, 2 * height, 2 * across, out)


def valid_conv(padded, kernel, frames, height, across):
    channels = padded.shape[-1]
    columns = jnp.concatenate(
        [
            padded[dt : dt + frames, dy : dy + height, dx : dx + across]
            for dt in range(3)
            for dy in range(3)
            for dx in range(3)
        ],
        axis=-1,
    )
    result = jnp.dot(
        columns.reshape(-1, 27 * channels),
        kernel.reshape(27 * channels, kernel.shape[-1]),
        preferred_element_type=jnp.float32,
    )
    return result.reshape(frames, height, across, -1)


def conv_halo(values):
    x = padded_2(values, (("ha", 1), ("wa", 2)), 1)
    earlier = passed_along(x[-2:], "ta", 1)
    opening = jnp.concatenate([x[:1], x[:1]], axis=0)
    earlier = jnp.where(lax.axis_index("ta") == 0, opening, earlier)
    return jnp.concatenate([earlier, x], axis=0)


def swap(x, axis, distance):
    size = lax.axis_size(axis)
    return lax.ppermute(x, axis, [(i, i ^ distance) for i in range(size)])


def fast_mesh():
    return lax.axis_size("ta") == 2 and lax.axis_size("wa") == 2 and lax.axis_size("ha") == 4


def local_sums(values):
    grouped = values.reshape(-1, GROUPS, values.shape[-1] // GROUPS)
    return jnp.stack([jnp.sum(grouped, axis=(0, 2)), jnp.sum(grouped * grouped, axis=(0, 2))])


def finish_stats(sums, values):
    channels = values.shape[-1]
    group_width = channels // GROUPS
    entries = (
        values.size // GROUPS
        * lax.axis_size("ha")
        * lax.axis_size("wa")
        * lax.axis_size("ta")
    )
    average = sums[0] / entries
    spread = sums[1] / entries - average * average
    scaling = lax.rsqrt(spread + EPSILON)
    return jnp.repeat(average, group_width), jnp.repeat(scaling, group_width)


def split_high(value):
    scaled = value * 65537.0
    return scaled - (scaled - value)


def pack_sums(sums, width):
    high = split_high(sums)
    rest = sums - high
    middle = split_high(rest)
    low = rest - middle
    flat = jnp.concatenate([high.reshape(-1), middle.reshape(-1), low.reshape(-1)])
    flat = flat.astype(jnp.bfloat16)
    rows = -(-flat.size // width)
    return jnp.pad(flat, (0, rows * width - flat.size)).reshape(rows, width)


def unpack_sums(rows, like):
    flat = rows.reshape(-1)[: 3 * like.size].astype(jnp.float32).reshape(3, *like.shape)
    return (flat[0] + flat[1]) + flat[2]


def swap_with(sums, payload, axis, distance):
    width = payload.shape[-1]
    packed = pack_sums(sums, width)
    message = jnp.concatenate([payload.reshape(-1, width), packed], axis=0)
    got = swap(message, axis, distance)
    cut = got.shape[0] - packed.shape[0]
    return unpack_sums(got[cut:], sums), got[:cut].reshape(payload.shape)


def ha_round(sums, upper, lower):
    h = lax.axis_index("ha")
    to_first = jnp.where(h % 2 == 1, upper, lower)
    to_third = jnp.where(h == 2, upper, lower)
    s1, got_first = swap_with(sums, to_first, "ha", 1)
    s2 = swap(sums, "ha", 2)
    s3, got_third = swap_with(sums, to_third, "ha", 3)
    sums = (sums + s1) + (s2 + s3)
    above = jnp.where(h % 2 == 1, got_first, got_third)
    below = jnp.where(h % 2 == 0, got_first, got_third)
    return sums, above, below


def fast_conv_input(values):
    sums = local_sums(values.astype(jnp.float32))
    w = lax.axis_index("wa")
    s_w, beside = swap_with(sums, jnp.where(w == 0, values[:, :, -1:], values[:, :, :1]), "wa", 1)
    sums = sums + s_w
    x = jnp.concatenate([beside, values, beside], axis=2)
    sums, above, below = ha_round(sums, x[:, :1], x[:, -1:])
    x = jnp.concatenate([above, x, below], axis=1)
    s_t, earlier = swap_with(sums, x[-2:], "ta", 1)
    sums = sums + s_t
    opening = jnp.concatenate([x[:1], x[:1]], axis=0)
    earlier = jnp.where(lax.axis_index("ta") == 0, opening, earlier)
    x = jnp.concatenate([earlier, x], axis=0)
    return finish_stats(sums, values), x


def fast_latent_input(values):
    sums = local_sums(values.astype(jnp.float32))
    sums = sums + swap(sums, "ta", 1)
    s_w, beside = swap_with(sums, values[:, :, :1], "wa", 1)
    sums = sums + s_w
    x = jnp.concatenate([values, beside], axis=2)
    sums, _, below = ha_round(sums, x[:, :1], x[:, :1])
    x = jnp.concatenate([x, below], axis=1)
    return finish_stats(sums, values), x


def norm_conv(values, gain, shift, kernel):
    frames, height, across, _ = values.shape
    if fast_mesh():
        stats, extended = fast_conv_input(values)
    else:
        stats = group_stats(values.astype(jnp.float32))
        extended = conv_halo(values)
    act = activate(extended.astype(jnp.float32), stats, gain, shift)
    act = jnp.where(inside_mask(height + 2, across + 2, 1), act, 0.0).astype(jnp.bfloat16)
    return valid_conv(act, kernel, frames, height, across)


def per_device(
    latents,
    norm1_gain,
    norm1_shift,
    up_weight,
    norm2_gain,
    norm2_shift,
    conv_a,
    norm3_gain,
    norm3_shift,
    conv_b,
):
    frames, height, across, channels = latents.shape
    if fast_mesh():
        stats, extended = fast_latent_input(latents)
    else:
        stats = group_stats(latents.astype(jnp.float32))
        extended = latent_halo(latents)
    activated = activate(extended.astype(jnp.float32), stats, norm1_gain, norm1_shift)
    activated = jnp.where(inside_mask(height + 1, across + 1, 0), activated, 0.0)
    lifted = upsample(activated.astype(jnp.bfloat16), up_weight).astype(jnp.bfloat16)
    hidden = norm_conv(lifted, norm2_gain, norm2_shift, conv_a).astype(jnp.bfloat16)
    branch = norm_conv(hidden, norm3_gain, norm3_shift, conv_b)
    return (lifted.astype(jnp.float32) + branch).astype(jnp.bfloat16)


def solution(mesh):
    return jax.shard_map(
        per_device,
        mesh=mesh,
        in_specs=(
            P(("videos", "ta"), "ha", "wa", None),
            P(),
            P(),
            P(),
            P(),
            P(),
            P(),
            P(),
            P(),
            P(),
        ),
        out_specs=P(("videos", "ta"), "ha", "wa", None),
        check_vma=False,
    )
```

```python
import jax
import jax.numpy as jnp
from jax import lax
from jax.sharding import PartitionSpec as P

GROUPS = 32


EPSILON = 1e-06


def passed_along(block, axis, distance):
    devices = range(lax.axis_size(axis))
    route = [(i - distance, i) for i in devices if i - distance in devices]
    return lax.ppermute(block, axis, route)


def padded_2(x, sides, width):
    for axis, dim in sides:
        size, length = (lax.axis_size(axis), x.shape[dim])
        up = [(i, (i + 1) % size) for i in range(size - 1)]
        down = [(j, i) for i, j in up]
        last = lax.slice_in_dim(x, length - width, length, axis=dim)
        initial = lax.slice_in_dim(x, 0, width, axis=dim)
        before = lax.ppermute(last, axis, up)
        after = lax.ppermute(initial, axis, down)
        x = jnp.concatenate([before, x, after], axis=dim)
    return x


def group_allreduce(x, axes):
    sizes = [lax.axis_size(a) for a in axes]
    count = 1
    for s in sizes:
        count *= s
    if count & (count - 1):
        return lax.psum(x, axes)
    index = 0
    for a, s in zip(axes, sizes):
        index = index * s + lax.axis_index(a)
    shift = 0
    while (1 << shift) < count:
        width = min(2, (count.bit_length() - 1) - shift)
        slots = 1 << width
        position = (index >> shift) % slots
        received = [x] + [
            lax.ppermute(x, axes, [(i, i ^ (d << shift)) for i in range(count)])
            for d in range(1, slots)
        ]
        ordered = []
        for j in range(slots):
            value = jnp.zeros_like(x)
            for d in range(slots):
                value = jnp.where((position ^ d) == j, received[d], value)
            ordered.append(value)
        while len(ordered) > 1:
            ordered = [ordered[k] + ordered[k + 1] for k in range(0, len(ordered), 2)]
        x = ordered[0]
        shift += width
    return x


def group_stats(values):
    channels = values.shape[-1]
    group_width = channels // GROUPS
    grouped = values.reshape(-1, GROUPS, group_width)
    entries = (
        grouped.shape[0]
        * group_width
        * lax.axis_size("ha")
        * lax.axis_size("wa")
        * lax.axis_size("ta")
    )
    totals, squares = group_allreduce(
        jnp.stack([jnp.sum(grouped, axis=(0, 2)), jnp.sum(grouped * grouped, axis=(0, 2))]),
        ("ha", "wa", "ta"),
    )
    average = totals / entries
    spread = squares / entries - average * average
    scaling = lax.rsqrt(spread + EPSILON)
    return jnp.repeat(average, group_width), jnp.repeat(scaling, group_width)


def activate(values, stats, scale_vec, shift_vec):
    average, scaling = stats
    normed = (values - average) * scaling * scale_vec + shift_vec
    return jax.nn.silu(normed)


def inside_mask(rows, cols, low_pad):
    h, h_last = lax.axis_index("ha"), lax.axis_size("ha") - 1
    w, w_last = lax.axis_index("wa"), lax.axis_size("wa") - 1
    r = jnp.arange(rows)
    c = jnp.arange(cols)
    row_ok = jnp.logical_and(
        jnp.logical_or(r >= low_pad, h > 0), jnp.logical_or(r < rows - 1, h < h_last)
    )
    col_ok = jnp.logical_and(
        jnp.logical_or(c >= low_pad, w > 0), jnp.logical_or(c < cols - 1, w < w_last)
    )
    return jnp.logical_and(row_ok[:, None], col_ok[None, :])[None, :, :, None]


def latent_halo(x):
    h_size, w_size = lax.axis_size("ha"), lax.axis_size("wa")
    below = passed_along(x[:, :1], "ha", -1)
    right = passed_along(x[:, :, :1], "wa", -1)
    corner_route = [
        ((h + 1) * w_size + w + 1, h * w_size + w)
        for h in range(h_size - 1)
        for w in range(w_size - 1)
    ]
    corner = lax.ppermute(x[:, :1, :1], ("ha", "wa"), corner_route)
    top = jnp.concatenate([x, right], axis=2)
    bottom = jnp.concatenate([below, corner], axis=2)
    return jnp.concatenate([top, bottom], axis=1)


def upsample(act, kernel):
    frames, rows, cols, channels = act.shape
    height, across = rows - 1, cols - 1
    flat = lambda v: v.reshape(-1, channels)
    dot = lambda v, w: jnp.dot(flat(v), w, preferred_element_type=jnp.float32)
    a = act[:, :height, :across]
    b = act[:, :height, 1:]
    c = act[:, 1:, :across]
    d = act[:, 1:, 1:]
    out = kernel.shape[-1]
    pa = dot(a, jnp.concatenate([kernel[1, 1], kernel[1, 2], kernel[2, 1], kernel[2, 2]], axis=1))
    pb = dot(b, jnp.concatenate([kernel[1, 0], kernel[2, 0]], axis=1))
    pc = dot(c, jnp.concatenate([kernel[0, 1], kernel[0, 2]], axis=1))
    pd = dot(d, kernel[0, 0])
    ee = pa[:, :out]
    eo = pa[:, out : 2 * out] + pb[:, :out]
    oe = pa[:, 2 * out : 3 * out] + pc[:, :out]
    oo = pa[:, 3 * out :] + pb[:, out:] + pc[:, out:] + pd
    shape = (frames, height, across, 1, out)
    even = jnp.concatenate([ee.reshape(shape), eo.reshape(shape)], axis=3)
    odd = jnp.concatenate([oe.reshape(shape), oo.reshape(shape)], axis=3)
    even = even.reshape(frames, height, 1, 2 * across, out)
    odd = odd.reshape(frames, height, 1, 2 * across, out)
    return jnp.concatenate([even, odd], axis=2).reshape(frames, 2 * height, 2 * across, out)


def valid_conv(padded, kernel, frames, height, across):
    channels = padded.shape[-1]
    wide = jnp.concatenate(
        [padded[:, dy : dy + height, dx : dx + across] for dy in range(3) for dx in range(3)], axis=-1
    )
    result = None
    for step_t in range(3):
        window = wide[step_t : step_t + frames].reshape(-1, 9 * channels)
        part = jnp.dot(
            window, kernel[step_t].reshape(9 * channels, -1), preferred_element_type=jnp.float32
        )
        result = part if result is None else result + part
    return result.reshape(frames, height, across, -1)


def conv_halo(values):
    x = padded_2(values, (("ha", 1), ("wa", 2)), 1)
    earlier = passed_along(x[-2:], "ta", 1)
    opening = jnp.concatenate([x[:1], x[:1]], axis=0)
    earlier = jnp.where(lax.axis_index("ta") == 0, opening, earlier)
    return jnp.concatenate([earlier, x], axis=0)


def swap(x, axis, distance):
    size = lax.axis_size(axis)
    return lax.ppermute(x, axis, [(i, i ^ distance) for i in range(size)])


def fast_mesh():
    return lax.axis_size("ta") == 2 and lax.axis_size("wa") == 2 and lax.axis_size("ha") == 4


def local_sums(values):
    grouped = values.reshape(-1, GROUPS, values.shape[-1] // GROUPS)
    return jnp.stack([jnp.sum(grouped, axis=(0, 2)), jnp.sum(grouped * grouped, axis=(0, 2))])


def finish_stats(sums, values):
    channels = values.shape[-1]
    group_width = channels // GROUPS
    entries = (
        values.size // GROUPS
        * lax.axis_size("ha")
        * lax.axis_size("wa")
        * lax.axis_size("ta")
    )
    average = sums[0] / entries
    spread = sums[1] / entries - average * average
    scaling = lax.rsqrt(spread + EPSILON)
    return jnp.repeat(average, group_width), jnp.repeat(scaling, group_width)


def split_high(value):
    scaled = value * 65537.0
    return scaled - (scaled - value)


def pack_sums(sums, width):
    high = split_high(sums)
    rest = sums - high
    middle = split_high(rest)
    low = rest - middle
    flat = jnp.concatenate([high.reshape(-1), middle.reshape(-1), low.reshape(-1)])
    flat = flat.astype(jnp.bfloat16)
    rows = -(-flat.size // width)
    return jnp.pad(flat, (0, rows * width - flat.size)).reshape(rows, width)


def unpack_sums(rows, like):
    flat = rows.reshape(-1)[: 3 * like.size].astype(jnp.float32).reshape(3, *like.shape)
    return (flat[0] + flat[1]) + flat[2]


def swap_with(sums, payload, axis, distance):
    width = payload.shape[-1]
    packed = pack_sums(sums, width)
    message = jnp.concatenate([payload.reshape(-1, width), packed], axis=0)
    got = swap(message, axis, distance)
    cut = got.shape[0] - packed.shape[0]
    return unpack_sums(got[cut:], sums), got[:cut].reshape(payload.shape)


def ha_round(sums, upper, lower):
    h = lax.axis_index("ha")
    to_first = jnp.where(h % 2 == 1, upper, lower)
    to_third = jnp.where(h == 2, upper, lower)
    s1, got_first = swap_with(sums, to_first, "ha", 1)
    s2 = swap(sums, "ha", 2)
    s3, got_third = swap_with(sums, to_third, "ha", 3)
    sums = (sums + s1) + (s2 + s3)
    above = jnp.where(h % 2 == 1, got_first, got_third)
    below = jnp.where(h % 2 == 0, got_first, got_third)
    return sums, above, below


def fast_conv_input(values, gain, shift):
    frames, height, across, _ = values.shape
    sums = local_sums(values.astype(jnp.float32))
    sums = sums + swap(sums, "ta", 1)
    w = lax.axis_index("wa")
    s_w, beside = swap_with(sums, jnp.where(w == 0, values[:, :, -1:], values[:, :, :1]), "wa", 1)
    sums = sums + s_w
    x = jnp.concatenate([beside, values, beside], axis=2)
    sums, above, below = ha_round(sums, x[:, :1], x[:, -1:])
    x = jnp.concatenate([above, x, below], axis=1)
    act = activate(x.astype(jnp.float32), finish_stats(sums, values), gain, shift)
    act = jnp.where(inside_mask(height + 2, across + 2, 1), act, 0.0).astype(jnp.bfloat16)
    earlier = passed_along(act[-2:], "ta", 1)
    opening = jnp.concatenate([act[:1], act[:1]], axis=0)
    earlier = jnp.where(lax.axis_index("ta") == 0, opening, earlier)
    return jnp.concatenate([earlier, act], axis=0)


def fast_latent_input(values):
    sums = local_sums(values.astype(jnp.float32))
    sums = sums + swap(sums, "ta", 1)
    s_w, beside = swap_with(sums, values[:, :, :1], "wa", 1)
    sums = sums + s_w
    x = jnp.concatenate([values, beside], axis=2)
    sums, _, below = ha_round(sums, x[:, :1], x[:, :1])
    x = jnp.concatenate([x, below], axis=1)
    return finish_stats(sums, values), x


def norm_conv(values, gain, shift, kernel):
    frames, height, across, _ = values.shape
    if fast_mesh():
        act = fast_conv_input(values, gain, shift)
    else:
        stats = group_stats(values.astype(jnp.float32))
        extended = conv_halo(values)
        act = activate(extended.astype(jnp.float32), stats, gain, shift)
        act = jnp.where(inside_mask(height + 2, across + 2, 1), act, 0.0).astype(jnp.bfloat16)
    return valid_conv(act, kernel, frames, height, across)


def per_device(
    latents,
    norm1_gain,
    norm1_shift,
    up_weight,
    norm2_gain,
    norm2_shift,
    conv_a,
    norm3_gain,
    norm3_shift,
    conv_b,
):
    frames, height, across, channels = latents.shape
    if fast_mesh():
        stats, extended = fast_latent_input(latents)
    else:
        stats = group_stats(latents.astype(jnp.float32))
        extended = latent_halo(latents)
    activated = activate(extended.astype(jnp.float32), stats, norm1_gain, norm1_shift)
    activated = jnp.where(inside_mask(height + 1, across + 1, 0), activated, 0.0)
    lifted = upsample(activated.astype(jnp.bfloat16), up_weight).astype(jnp.bfloat16)
    hidden = norm_conv(lifted, norm2_gain, norm2_shift, conv_a).astype(jnp.bfloat16)
    branch = norm_conv(hidden, norm3_gain, norm3_shift, conv_b)
    return (lifted.astype(jnp.float32) + branch).astype(jnp.bfloat16)


def solution(mesh):
    return jax.shard_map(
        per_device,
        mesh=mesh,
        in_specs=(
            P(("videos", "ta"), "ha", "wa", None),
            P(),
            P(),
            P(),
            P(),
            P(),
            P(),
            P(),
            P(),
            P(),
        ),
        out_specs=P(("videos", "ta"), "ha", "wa", None),
        check_vma=False,
    )
```

```python
import jax
import jax.numpy as jnp
from jax import lax
from jax.sharding import PartitionSpec as P

GROUPS = 32


EPSILON = 1e-06


def passed_along(block, axis, distance):
    devices = range(lax.axis_size(axis))
    route = [(i - distance, i) for i in devices if i - distance in devices]
    return lax.ppermute(block, axis, route)


def padded_2(x, sides, width):
    for axis, dim in sides:
        size, length = (lax.axis_size(axis), x.shape[dim])
        up = [(i, (i + 1) % size) for i in range(size - 1)]
        down = [(j, i) for i, j in up]
        last = lax.slice_in_dim(x, length - width, length, axis=dim)
        initial = lax.slice_in_dim(x, 0, width, axis=dim)
        before = lax.ppermute(last, axis, up)
        after = lax.ppermute(initial, axis, down)
        x = jnp.concatenate([before, x, after], axis=dim)
    return x


def group_allreduce(x, axes):
    sizes = [lax.axis_size(a) for a in axes]
    count = 1
    for s in sizes:
        count *= s
    if count & (count - 1):
        return lax.psum(x, axes)
    index = 0
    for a, s in zip(axes, sizes):
        index = index * s + lax.axis_index(a)
    shift = 0
    while (1 << shift) < count:
        width = min(2, (count.bit_length() - 1) - shift)
        slots = 1 << width
        position = (index >> shift) % slots
        received = [x] + [
            lax.ppermute(x, axes, [(i, i ^ (d << shift)) for i in range(count)])
            for d in range(1, slots)
        ]
        ordered = []
        for j in range(slots):
            value = jnp.zeros_like(x)
            for d in range(slots):
                value = jnp.where((position ^ d) == j, received[d], value)
            ordered.append(value)
        while len(ordered) > 1:
            ordered = [ordered[k] + ordered[k + 1] for k in range(0, len(ordered), 2)]
        x = ordered[0]
        shift += width
    return x


def group_stats(values):
    channels = values.shape[-1]
    group_width = channels // GROUPS
    grouped = values.reshape(-1, GROUPS, group_width)
    entries = (
        grouped.shape[0]
        * group_width
        * lax.axis_size("ha")
        * lax.axis_size("wa")
        * lax.axis_size("ta")
    )
    totals, squares = group_allreduce(
        jnp.stack([jnp.sum(grouped, axis=(0, 2)), jnp.sum(grouped * grouped, axis=(0, 2))]),
        ("ha", "wa", "ta"),
    )
    average = totals / entries
    spread = squares / entries - average * average
    scaling = lax.rsqrt(spread + EPSILON)
    return jnp.repeat(average, group_width), jnp.repeat(scaling, group_width)


def activate(values, stats, scale_vec, shift_vec):
    average, scaling = stats
    normed = (values - average) * scaling * scale_vec + shift_vec
    return jax.nn.silu(normed)


def inside_mask(rows, cols, low_pad):
    h, h_last = lax.axis_index("ha"), lax.axis_size("ha") - 1
    w, w_last = lax.axis_index("wa"), lax.axis_size("wa") - 1
    r = jnp.arange(rows)
    c = jnp.arange(cols)
    row_ok = jnp.logical_and(
        jnp.logical_or(r >= low_pad, h > 0), jnp.logical_or(r < rows - 1, h < h_last)
    )
    col_ok = jnp.logical_and(
        jnp.logical_or(c >= low_pad, w > 0), jnp.logical_or(c < cols - 1, w < w_last)
    )
    return jnp.logical_and(row_ok[:, None], col_ok[None, :])[None, :, :, None]


def latent_halo(x):
    h_size, w_size = lax.axis_size("ha"), lax.axis_size("wa")
    below = passed_along(x[:, :1], "ha", -1)
    right = passed_along(x[:, :, :1], "wa", -1)
    corner_route = [
        ((h + 1) * w_size + w + 1, h * w_size + w)
        for h in range(h_size - 1)
        for w in range(w_size - 1)
    ]
    corner = lax.ppermute(x[:, :1, :1], ("ha", "wa"), corner_route)
    top = jnp.concatenate([x, right], axis=2)
    bottom = jnp.concatenate([below, corner], axis=2)
    return jnp.concatenate([top, bottom], axis=1)


def upsample(act, kernel):
    frames, rows, cols, channels = act.shape
    height, across = rows - 1, cols - 1
    flat = lambda v: v.reshape(-1, channels)
    dot = lambda v, w: jnp.dot(flat(v), w, preferred_element_type=jnp.float32)
    a = act[:, :height, :across]
    b = act[:, :height, 1:]
    c = act[:, 1:, :across]
    d = act[:, 1:, 1:]
    out = kernel.shape[-1]
    pa = dot(a, jnp.concatenate([kernel[1, 1], kernel[1, 2], kernel[2, 1], kernel[2, 2]], axis=1))
    pb = dot(b, jnp.concatenate([kernel[1, 0], kernel[2, 0]], axis=1))
    pc = dot(c, jnp.concatenate([kernel[0, 1], kernel[0, 2]], axis=1))
    pd = dot(d, kernel[0, 0])
    ee = pa[:, :out]
    eo = pa[:, out : 2 * out] + pb[:, :out]
    oe = pa[:, 2 * out : 3 * out] + pc[:, :out]
    oo = pa[:, 3 * out :] + pb[:, out:] + pc[:, out:] + pd
    shape = (frames, height, across, 1, out)
    even = jnp.concatenate([ee.reshape(shape), eo.reshape(shape)], axis=3)
    odd = jnp.concatenate([oe.reshape(shape), oo.reshape(shape)], axis=3)
    even = even.reshape(frames, height, 1, 2 * across, out)
    odd = odd.reshape(frames, height, 1, 2 * across, out)
    return jnp.concatenate([even, odd], axis=2).reshape(frames, 2 * height, 2 * across, out)


def valid_conv(padded, kernel, frames, height, across, result=None):
    channels = padded.shape[-1]
    wide = jnp.concatenate(
        [padded[:, dy : dy + height, dx : dx + across] for dy in range(3) for dx in range(3)], axis=-1
    )
    for step_t in range(3):
        window = wide[step_t : step_t + frames].reshape(-1, 9 * channels)
        part = jnp.dot(
            window, kernel[step_t].reshape(9 * channels, -1), preferred_element_type=jnp.float32
        )
        result = part if result is None else result + part
    return result.reshape(frames, height, across, -1)


def conv_halo(values):
    x = padded_2(values, (("ha", 1), ("wa", 2)), 1)
    earlier = passed_along(x[-2:], "ta", 1)
    opening = jnp.concatenate([x[:1], x[:1]], axis=0)
    earlier = jnp.where(lax.axis_index("ta") == 0, opening, earlier)
    return jnp.concatenate([earlier, x], axis=0)


def swap(x, axis, distance):
    size = lax.axis_size(axis)
    return lax.ppermute(x, axis, [(i, i ^ distance) for i in range(size)])


def fast_mesh():
    return lax.axis_size("ta") == 2 and lax.axis_size("wa") == 2 and lax.axis_size("ha") == 4


def local_sums(values):
    grouped = values.reshape(-1, GROUPS, values.shape[-1] // GROUPS)
    return jnp.stack([jnp.sum(grouped, axis=(0, 2)), jnp.sum(grouped * grouped, axis=(0, 2))])


def finish_stats(sums, values):
    channels = values.shape[-1]
    group_width = channels // GROUPS
    entries = (
        values.size // GROUPS
        * lax.axis_size("ha")
        * lax.axis_size("wa")
        * lax.axis_size("ta")
    )
    average = sums[0] / entries
    spread = sums[1] / entries - average * average
    scaling = lax.rsqrt(spread + EPSILON)
    return jnp.repeat(average, group_width), jnp.repeat(scaling, group_width)


def split_high(value):
    scaled = value * 65537.0
    return scaled - (scaled - value)


def pack_sums(sums, width):
    high = split_high(sums)
    rest = sums - high
    middle = split_high(rest)
    low = rest - middle
    flat = jnp.concatenate([high.reshape(-1), middle.reshape(-1), low.reshape(-1)])
    flat = flat.astype(jnp.bfloat16)
    rows = -(-flat.size // width)
    return jnp.pad(flat, (0, rows * width - flat.size)).reshape(rows, width)


def unpack_sums(rows, like):
    flat = rows.reshape(-1)[: 3 * like.size].astype(jnp.float32).reshape(3, *like.shape)
    return (flat[0] + flat[1]) + flat[2]


def swap_with(sums, payload, axis, distance):
    width = payload.shape[-1]
    packed = pack_sums(sums, width)
    message = jnp.concatenate([payload.reshape(-1, width), packed], axis=0)
    got = swap(message, axis, distance)
    cut = got.shape[0] - packed.shape[0]
    return unpack_sums(got[cut:], sums), got[:cut].reshape(payload.shape)


def ha_round(sums, upper, lower):
    h = lax.axis_index("ha")
    to_first = jnp.where(h % 2 == 1, upper, lower)
    to_third = jnp.where(h == 2, upper, lower)
    s1, got_first = swap_with(sums, to_first, "ha", 1)
    s2 = swap(sums, "ha", 2)
    s3, got_third = swap_with(sums, to_third, "ha", 3)
    sums = (sums + s1) + (s2 + s3)
    above = jnp.where(h % 2 == 1, got_first, got_third)
    below = jnp.where(h % 2 == 0, got_first, got_third)
    return sums, above, below


def fast_conv_input(values):
    sums = local_sums(values.astype(jnp.float32))
    w = lax.axis_index("wa")
    s_w, beside = swap_with(sums, jnp.where(w == 0, values[:, :, -1:], values[:, :, :1]), "wa", 1)
    sums = sums + s_w
    x = jnp.concatenate([beside, values, beside], axis=2)
    sums, above, below = ha_round(sums, x[:, :1], x[:, -1:])
    x = jnp.concatenate([above, x, below], axis=1)
    s_t, earlier = swap_with(sums, x[-2:], "ta", 1)
    sums = sums + s_t
    opening = jnp.concatenate([x[:1], x[:1]], axis=0)
    earlier = jnp.where(lax.axis_index("ta") == 0, opening, earlier)
    x = jnp.concatenate([earlier, x], axis=0)
    return finish_stats(sums, values), x


def fast_latent_input(values):
    sums = local_sums(values.astype(jnp.float32))
    sums = sums + swap(sums, "ta", 1)
    s_w, beside = swap_with(sums, values[:, :, :1], "wa", 1)
    sums = sums + s_w
    x = jnp.concatenate([values, beside], axis=2)
    sums, _, below = ha_round(sums, x[:, :1], x[:, :1])
    x = jnp.concatenate([x, below], axis=1)
    return finish_stats(sums, values), x


def norm_conv(values, gain, shift, kernel, result=None):
    frames, height, across, _ = values.shape
    if fast_mesh():
        stats, extended = fast_conv_input(values)
    else:
        stats = group_stats(values.astype(jnp.float32))
        extended = conv_halo(values)
    act = activate(extended.astype(jnp.float32), stats, gain, shift)
    act = jnp.where(inside_mask(height + 2, across + 2, 1), act, 0.0).astype(jnp.bfloat16)
    return valid_conv(act, kernel, frames, height, across, result)


def per_device(
    latents,
    norm1_gain,
    norm1_shift,
    up_weight,
    norm2_gain,
    norm2_shift,
    conv_a,
    norm3_gain,
    norm3_shift,
    conv_b,
):
    frames, height, across, channels = latents.shape
    if fast_mesh():
        stats, extended = fast_latent_input(latents)
    else:
        stats = group_stats(latents.astype(jnp.float32))
        extended = latent_halo(latents)
    activated = activate(extended.astype(jnp.float32), stats, norm1_gain, norm1_shift)
    activated = jnp.where(inside_mask(height + 1, across + 1, 0), activated, 0.0)
    lifted = upsample(activated.astype(jnp.bfloat16), up_weight).astype(jnp.bfloat16)
    hidden = norm_conv(lifted, norm2_gain, norm2_shift, conv_a).astype(jnp.bfloat16)
    residual = lifted.astype(jnp.float32).reshape(-1, lifted.shape[-1])
    decoded = norm_conv(hidden, norm3_gain, norm3_shift, conv_b, residual)
    return decoded.astype(jnp.bfloat16)


def solution(mesh):
    return jax.shard_map(
        per_device,
        mesh=mesh,
        in_specs=(
            P(("videos", "ta"), "ha", "wa", None),
            P(),
            P(),
            P(),
            P(),
            P(),
            P(),
            P(),
            P(),
            P(),
        ),
        out_specs=P(("videos", "ta"), "ha", "wa", None),
        check_vma=False,
    )
```

```python
import jax
import jax.numpy as jnp
from jax import lax
from jax.sharding import PartitionSpec as P

GROUPS = 32


EPSILON = 1e-06


def passed_along(block, axis, distance):
    devices = range(lax.axis_size(axis))
    route = [(i - distance, i) for i in devices if i - distance in devices]
    return lax.ppermute(block, axis, route)


def padded_2(x, sides, width):
    for axis, dim in sides:
        size, length = (lax.axis_size(axis), x.shape[dim])
        up = [(i, (i + 1) % size) for i in range(size - 1)]
        down = [(j, i) for i, j in up]
        last = lax.slice_in_dim(x, length - width, length, axis=dim)
        initial = lax.slice_in_dim(x, 0, width, axis=dim)
        before = lax.ppermute(last, axis, up)
        after = lax.ppermute(initial, axis, down)
        x = jnp.concatenate([before, x, after], axis=dim)
    return x


def group_allreduce(x, axes):
    sizes = [lax.axis_size(a) for a in axes]
    count = 1
    for s in sizes:
        count *= s
    if count & (count - 1):
        return lax.psum(x, axes)
    index = 0
    for a, s in zip(axes, sizes):
        index = index * s + lax.axis_index(a)
    shift = 0
    while (1 << shift) < count:
        width = min(2, (count.bit_length() - 1) - shift)
        slots = 1 << width
        position = (index >> shift) % slots
        received = [x] + [
            lax.ppermute(x, axes, [(i, i ^ (d << shift)) for i in range(count)])
            for d in range(1, slots)
        ]
        ordered = []
        for j in range(slots):
            value = jnp.zeros_like(x)
            for d in range(slots):
                value = jnp.where((position ^ d) == j, received[d], value)
            ordered.append(value)
        while len(ordered) > 1:
            ordered = [ordered[k] + ordered[k + 1] for k in range(0, len(ordered), 2)]
        x = ordered[0]
        shift += width
    return x


def group_stats(values):
    channels = values.shape[-1]
    group_width = channels // GROUPS
    grouped = values.reshape(-1, GROUPS, group_width)
    entries = (
        grouped.shape[0]
        * group_width
        * lax.axis_size("ha")
        * lax.axis_size("wa")
        * lax.axis_size("ta")
    )
    totals, squares = group_allreduce(
        jnp.stack([jnp.sum(grouped, axis=(0, 2)), jnp.sum(grouped * grouped, axis=(0, 2))]),
        ("ha", "wa", "ta"),
    )
    average = totals / entries
    spread = squares / entries - average * average
    scaling = lax.rsqrt(spread + EPSILON)
    return jnp.repeat(average, group_width), jnp.repeat(scaling, group_width)


def activate(values, stats, scale_vec, shift_vec):
    average, scaling = stats
    normed = (values - average) * scaling * scale_vec + shift_vec
    return jax.nn.silu(normed)


def inside_mask(rows, cols, low_pad):
    h, h_last = lax.axis_index("ha"), lax.axis_size("ha") - 1
    w, w_last = lax.axis_index("wa"), lax.axis_size("wa") - 1
    r = jnp.arange(rows)
    c = jnp.arange(cols)
    row_ok = jnp.logical_and(
        jnp.logical_or(r >= low_pad, h > 0), jnp.logical_or(r < rows - 1, h < h_last)
    )
    col_ok = jnp.logical_and(
        jnp.logical_or(c >= low_pad, w > 0), jnp.logical_or(c < cols - 1, w < w_last)
    )
    return jnp.logical_and(row_ok[:, None], col_ok[None, :])[None, :, :, None]


def latent_halo(x):
    h_size, w_size = lax.axis_size("ha"), lax.axis_size("wa")
    below = passed_along(x[:, :1], "ha", -1)
    right = passed_along(x[:, :, :1], "wa", -1)
    corner_route = [
        ((h + 1) * w_size + w + 1, h * w_size + w)
        for h in range(h_size - 1)
        for w in range(w_size - 1)
    ]
    corner = lax.ppermute(x[:, :1, :1], ("ha", "wa"), corner_route)
    top = jnp.concatenate([x, right], axis=2)
    bottom = jnp.concatenate([below, corner], axis=2)
    return jnp.concatenate([top, bottom], axis=1)


def upsample(act, kernel):
    frames, rows, cols, channels = act.shape
    height, across = rows - 1, cols - 1
    flat = lambda v: v.reshape(-1, channels)
    dot = lambda v, w: jnp.dot(flat(v), w, preferred_element_type=jnp.float32)
    a = act[:, :height, :across]
    b = act[:, :height, 1:]
    c = act[:, 1:, :across]
    d = act[:, 1:, 1:]
    out = kernel.shape[-1]
    pa = dot(a, jnp.concatenate([kernel[1, 1], kernel[1, 2], kernel[2, 1], kernel[2, 2]], axis=1))
    pb = dot(b, jnp.concatenate([kernel[1, 0], kernel[2, 0]], axis=1))
    pc = dot(c, jnp.concatenate([kernel[0, 1], kernel[0, 2]], axis=1))
    pd = dot(d, kernel[0, 0])
    ee = pa[:, :out]
    eo = pa[:, out : 2 * out] + pb[:, :out]
    oe = pa[:, 2 * out : 3 * out] + pc[:, :out]
    oo = pa[:, 3 * out :] + pb[:, out:] + pc[:, out:] + pd
    shape = (frames, height, across, 1, out)
    even = jnp.concatenate([ee.reshape(shape), eo.reshape(shape)], axis=3)
    odd = jnp.concatenate([oe.reshape(shape), oo.reshape(shape)], axis=3)
    even = even.reshape(frames, height, 1, 2 * across, out)
    odd = odd.reshape(frames, height, 1, 2 * across, out)
    return jnp.concatenate([even, odd], axis=2).reshape(frames, 2 * height, 2 * across, out)


def valid_conv(padded, kernel, frames, height, across):
    channels = padded.shape[-1]
    wide = jnp.concatenate(
        [padded[:, dy : dy + height, dx : dx + across] for dy in range(3) for dx in range(3)], axis=-1
    )
    result = None
    for step_t in range(3):
        window = wide[step_t : step_t + frames].reshape(-1, 9 * channels)
        part = jnp.dot(
            window, kernel[step_t].reshape(9 * channels, -1), preferred_element_type=jnp.float32
        )
        result = part if result is None else result + part
    return result.reshape(frames, height, across, -1)


def conv_halo(values):
    x = padded_2(values, (("ha", 1), ("wa", 2)), 1)
    earlier = passed_along(x[-2:], "ta", 1)
    opening = jnp.concatenate([x[:1], x[:1]], axis=0)
    earlier = jnp.where(lax.axis_index("ta") == 0, opening, earlier)
    return jnp.concatenate([earlier, x], axis=0)


def swap(x, axis, distance):
    size = lax.axis_size(axis)
    return lax.ppermute(x, axis, [(i, i ^ distance) for i in range(size)])


def fast_mesh():
    return lax.axis_size("ta") == 2 and lax.axis_size("wa") == 2 and lax.axis_size("ha") == 4


def local_sums(values):
    grouped = values.reshape(-1, GROUPS, values.shape[-1] // GROUPS)
    return jnp.stack([jnp.sum(grouped, axis=(0, 2)), jnp.sum(grouped * grouped, axis=(0, 2))])


def finish_stats(sums, values):
    channels = values.shape[-1]
    group_width = channels // GROUPS
    entries = (
        values.size // GROUPS
        * lax.axis_size("ha")
        * lax.axis_size("wa")
        * lax.axis_size("ta")
    )
    average = sums[0] / entries
    spread = sums[1] / entries - average * average
    scaling = lax.rsqrt(spread + EPSILON)
    return jnp.repeat(average, group_width), jnp.repeat(scaling, group_width)


def split_high(value):
    scaled = value * 65537.0
    return scaled - (scaled - value)


def pack_sums(sums, width):
    high = split_high(sums)
    rest = sums - high
    middle = split_high(rest)
    low = rest - middle
    flat = jnp.concatenate([high.reshape(-1), middle.reshape(-1), low.reshape(-1)])
    flat = flat.astype(jnp.bfloat16)
    rows = -(-flat.size // width)
    return jnp.pad(flat, (0, rows * width - flat.size)).reshape(rows, width)


def unpack_sums(rows, like):
    flat = rows.reshape(-1)[: 3 * like.size].astype(jnp.float32).reshape(3, *like.shape)
    return (flat[0] + flat[1]) + flat[2]


def swap_with(sums, payload, axis, distance):
    width = payload.shape[-1]
    packed = pack_sums(sums, width)
    message = jnp.concatenate([payload.reshape(-1, width), packed], axis=0)
    got = swap(message, axis, distance)
    cut = got.shape[0] - packed.shape[0]
    return unpack_sums(got[cut:], sums), got[:cut].reshape(payload.shape)


def ha_round(sums, upper, lower):
    h = lax.axis_index("ha")
    to_first = jnp.where(h % 2 == 1, upper, lower)
    to_third = jnp.where(h == 2, upper, lower)
    s1, got_first = swap_with(sums, to_first, "ha", 1)
    s2 = swap(sums, "ha", 2)
    s3, got_third = swap_with(sums, to_third, "ha", 3)
    sums = (sums + s1) + (s2 + s3)
    above = jnp.where(h % 2 == 1, got_first, got_third)
    below = jnp.where(h % 2 == 0, got_first, got_third)
    return sums, above, below


def fast_conv_input(values):
    sums = local_sums(values.astype(jnp.float32))
    w = lax.axis_index("wa")
    s_w, beside = swap_with(sums, jnp.where(w == 0, values[:, :, -1:], values[:, :, :1]), "wa", 1)
    sums = sums + s_w
    x = jnp.concatenate([beside, values, beside], axis=2)
    sums, above, below = ha_round(sums, x[:, :1], x[:, -1:])
    x = jnp.concatenate([above, x, below], axis=1)
    s_t, earlier = swap_with(sums, x[-2:], "ta", 1)
    sums = sums + s_t
    opening = jnp.concatenate([x[:1], x[:1]], axis=0)
    earlier = jnp.where(lax.axis_index("ta") == 0, opening, earlier)
    x = jnp.concatenate([earlier, x], axis=0)
    return finish_stats(sums, values), x


def fast_latent_input(values):
    sums = local_sums(values.astype(jnp.float32))
    sums = sums + swap(sums, "ta", 1)
    sums, _, below = ha_round(sums, values[:, :1], values[:, :1])
    x = jnp.concatenate([values, below], axis=1)
    s_w, beside = swap_with(sums, x[:, :, :1], "wa", 1)
    sums = sums + s_w
    x = jnp.concatenate([x, beside], axis=2)
    return finish_stats(sums, values), x


def norm_conv(values, gain, shift, kernel):
    frames, height, across, _ = values.shape
    if fast_mesh():
        stats, extended = fast_conv_input(values)
    else:
        stats = group_stats(values.astype(jnp.float32))
        extended = conv_halo(values)
    act = activate(extended.astype(jnp.float32), stats, gain, shift)
    act = jnp.where(inside_mask(height + 2, across + 2, 1), act, 0.0).astype(jnp.bfloat16)
    return valid_conv(act, kernel, frames, height, across)


def per_device(
    latents,
    norm1_gain,
    norm1_shift,
    up_weight,
    norm2_gain,
    norm2_shift,
    conv_a,
    norm3_gain,
    norm3_shift,
    conv_b,
):
    frames, height, across, channels = latents.shape
    if fast_mesh():
        stats, extended = fast_latent_input(latents)
    else:
        stats = group_stats(latents.astype(jnp.float32))
        extended = latent_halo(latents)
    activated = activate(extended.astype(jnp.float32), stats, norm1_gain, norm1_shift)
    activated = jnp.where(inside_mask(height + 1, across + 1, 0), activated, 0.0)
    lifted = upsample(activated.astype(jnp.bfloat16), up_weight).astype(jnp.bfloat16)
    hidden = norm_conv(lifted, norm2_gain, norm2_shift, conv_a).astype(jnp.bfloat16)
    branch = norm_conv(hidden, norm3_gain, norm3_shift, conv_b)
    return (lifted.astype(jnp.float32) + branch).astype(jnp.bfloat16)


def solution(mesh):
    return jax.shard_map(
        per_device,
        mesh=mesh,
        in_specs=(
            P(("videos", "ta"), "ha", "wa", None),
            P(),
            P(),
            P(),
            P(),
            P(),
            P(),
            P(),
            P(),
            P(),
        ),
        out_specs=P(("videos", "ta"), "ha", "wa", None),
        check_vma=False,
    )
```

```python
import jax
import jax.numpy as jnp
from jax import lax
from jax.sharding import PartitionSpec as P

GROUPS = 32


EPSILON = 1e-06


def passed_along(block, axis, distance):
    devices = range(lax.axis_size(axis))
    route = [(i - distance, i) for i in devices if i - distance in devices]
    return lax.ppermute(block, axis, route)


def padded_2(x, sides, width):
    for axis, dim in sides:
        size, length = (lax.axis_size(axis), x.shape[dim])
        up = [(i, (i + 1) % size) for i in range(size - 1)]
        down = [(j, i) for i, j in up]
        last = lax.slice_in_dim(x, length - width, length, axis=dim)
        initial = lax.slice_in_dim(x, 0, width, axis=dim)
        before = lax.ppermute(last, axis, up)
        after = lax.ppermute(initial, axis, down)
        x = jnp.concatenate([before, x, after], axis=dim)
    return x


def group_allreduce(x, axes):
    sizes = [lax.axis_size(a) for a in axes]
    count = 1
    for s in sizes:
        count *= s
    if count & (count - 1):
        return lax.psum(x, axes)
    index = 0
    for a, s in zip(axes, sizes):
        index = index * s + lax.axis_index(a)
    shift = 0
    while (1 << shift) < count:
        width = min(2, (count.bit_length() - 1) - shift)
        slots = 1 << width
        position = (index >> shift) % slots
        received = [x] + [
            lax.ppermute(x, axes, [(i, i ^ (d << shift)) for i in range(count)])
            for d in range(1, slots)
        ]
        ordered = []
        for j in range(slots):
            value = jnp.zeros_like(x)
            for d in range(slots):
                value = jnp.where((position ^ d) == j, received[d], value)
            ordered.append(value)
        while len(ordered) > 1:
            ordered = [ordered[k] + ordered[k + 1] for k in range(0, len(ordered), 2)]
        x = ordered[0]
        shift += width
    return x


def group_stats(values):
    channels = values.shape[-1]
    group_width = channels // GROUPS
    grouped = values.reshape(-1, GROUPS, group_width)
    entries = (
        grouped.shape[0]
        * group_width
        * lax.axis_size("ha")
        * lax.axis_size("wa")
        * lax.axis_size("ta")
    )
    totals, squares = group_allreduce(
        jnp.stack([jnp.sum(grouped, axis=(0, 2)), jnp.sum(grouped * grouped, axis=(0, 2))]),
        ("ha", "wa", "ta"),
    )
    average = totals / entries
    spread = squares / entries - average * average
    scaling = lax.rsqrt(spread + EPSILON)
    return jnp.repeat(average, group_width), jnp.repeat(scaling, group_width)


def activate(values, stats, scale_vec, shift_vec):
    average, scaling = stats
    normed = (values - average) * scaling * scale_vec + shift_vec
    return 0.5 * normed * (1.0 + jnp.tanh(0.5 * normed))


def inside_mask(rows, cols, low_pad):
    h, h_last = lax.axis_index("ha"), lax.axis_size("ha") - 1
    w, w_last = lax.axis_index("wa"), lax.axis_size("wa") - 1
    r = jnp.arange(rows)
    c = jnp.arange(cols)
    row_ok = jnp.logical_and(
        jnp.logical_or(r >= low_pad, h > 0), jnp.logical_or(r < rows - 1, h < h_last)
    )
    col_ok = jnp.logical_and(
        jnp.logical_or(c >= low_pad, w > 0), jnp.logical_or(c < cols - 1, w < w_last)
    )
    return jnp.logical_and(row_ok[:, None], col_ok[None, :])[None, :, :, None]


def latent_halo(x):
    h_size, w_size = lax.axis_size("ha"), lax.axis_size("wa")
    below = passed_along(x[:, :1], "ha", -1)
    right = passed_along(x[:, :, :1], "wa", -1)
    corner_route = [
        ((h + 1) * w_size + w + 1, h * w_size + w)
        for h in range(h_size - 1)
        for w in range(w_size - 1)
    ]
    corner = lax.ppermute(x[:, :1, :1], ("ha", "wa"), corner_route)
    top = jnp.concatenate([x, right], axis=2)
    bottom = jnp.concatenate([below, corner], axis=2)
    return jnp.concatenate([top, bottom], axis=1)


def upsample(act, kernel):
    frames, rows, cols, channels = act.shape
    height, across = rows - 1, cols - 1
    flat = lambda v: v.reshape(-1, channels)
    dot = lambda v, w: jnp.dot(flat(v), w, preferred_element_type=jnp.float32)
    a = act[:, :height, :across]
    b = act[:, :height, 1:]
    c = act[:, 1:, :across]
    d = act[:, 1:, 1:]
    out = kernel.shape[-1]
    pa = dot(a, jnp.concatenate([kernel[1, 1], kernel[1, 2], kernel[2, 1], kernel[2, 2]], axis=1))
    pb = dot(b, jnp.concatenate([kernel[1, 0], kernel[2, 0]], axis=1))
    pc = dot(c, jnp.concatenate([kernel[0, 1], kernel[0, 2]], axis=1))
    pd = dot(d, kernel[0, 0])
    ee = pa[:, :out]
    eo = pa[:, out : 2 * out] + pb[:, :out]
    oe = pa[:, 2 * out : 3 * out] + pc[:, :out]
    oo = pa[:, 3 * out :] + pb[:, out:] + pc[:, out:] + pd
    shape = (frames, height, across, 1, out)
    even = jnp.concatenate([ee.reshape(shape), eo.reshape(shape)], axis=3)
    odd = jnp.concatenate([oe.reshape(shape), oo.reshape(shape)], axis=3)
    even = even.reshape(frames, height, 1, 2 * across, out)
    odd = odd.reshape(frames, height, 1, 2 * across, out)
    return jnp.concatenate([even, odd], axis=2).reshape(frames, 2 * height, 2 * across, out)


def valid_conv(padded, kernel, frames, height, across, result=None):
    channels = padded.shape[-1]
    wide = jnp.concatenate(
        [padded[:, dy : dy + height, dx : dx + across] for dy in range(3) for dx in range(3)], axis=-1
    )
    for step_t in range(3):
        window = wide[step_t : step_t + frames].reshape(-1, 9 * channels)
        part = jnp.dot(
            window, kernel[step_t].reshape(9 * channels, -1), preferred_element_type=jnp.float32
        )
        result = part if result is None else result + part
    return result.reshape(frames, height, across, -1)


def conv_halo(values):
    x = padded_2(values, (("ha", 1), ("wa", 2)), 1)
    earlier = passed_along(x[-2:], "ta", 1)
    opening = jnp.concatenate([x[:1], x[:1]], axis=0)
    earlier = jnp.where(lax.axis_index("ta") == 0, opening, earlier)
    return jnp.concatenate([earlier, x], axis=0)


def swap(x, axis, distance):
    size = lax.axis_size(axis)
    return lax.ppermute(x, axis, [(i, i ^ distance) for i in range(size)])


def fast_mesh():
    return lax.axis_size("ta") == 2 and lax.axis_size("wa") == 2 and lax.axis_size("ha") == 4


def local_sums(values):
    grouped = values.reshape(-1, GROUPS, values.shape[-1] // GROUPS)
    return jnp.stack([jnp.sum(grouped, axis=(0, 2)), jnp.sum(grouped * grouped, axis=(0, 2))])


def finish_stats(sums, values):
    channels = values.shape[-1]
    group_width = channels // GROUPS
    entries = (
        values.size // GROUPS
        * lax.axis_size("ha")
        * lax.axis_size("wa")
        * lax.axis_size("ta")
    )
    average = sums[0] / entries
    spread = sums[1] / entries - average * average
    scaling = lax.rsqrt(spread + EPSILON)
    return jnp.repeat(average, group_width), jnp.repeat(scaling, group_width)


def split_high(value):
    scaled = value * 65537.0
    return scaled - (scaled - value)


def pack_sums(sums, width):
    high = split_high(sums)
    rest = sums - high
    middle = split_high(rest)
    low = rest - middle
    flat = jnp.concatenate([high.reshape(-1), middle.reshape(-1), low.reshape(-1)])
    flat = flat.astype(jnp.bfloat16)
    rows = -(-flat.size // width)
    return jnp.pad(flat, (0, rows * width - flat.size)).reshape(rows, width)


def unpack_sums(rows, like):
    flat = rows.reshape(-1)[: 3 * like.size].astype(jnp.float32).reshape(3, *like.shape)
    return (flat[0] + flat[1]) + flat[2]


def swap_with(sums, payload, axis, distance):
    width = payload.shape[-1]
    packed = pack_sums(sums, width)
    message = jnp.concatenate([payload.reshape(-1, width), packed], axis=0)
    got = swap(message, axis, distance)
    cut = got.shape[0] - packed.shape[0]
    return unpack_sums(got[cut:], sums), got[:cut].reshape(payload.shape)


def ha_round(sums, upper, lower):
    h = lax.axis_index("ha")
    to_first = jnp.where(h % 2 == 1, upper, lower)
    to_third = jnp.where(h == 2, upper, lower)
    s1, got_first = swap_with(sums, to_first, "ha", 1)
    s2 = swap(sums, "ha", 2)
    s3, got_third = swap_with(sums, to_third, "ha", 3)
    sums = (sums + s1) + (s2 + s3)
    above = jnp.where(h % 2 == 1, got_first, got_third)
    below = jnp.where(h % 2 == 0, got_first, got_third)
    return sums, above, below


def fast_conv_input(values, gain, shift):
    frames, height, across, _ = values.shape
    sums = local_sums(values.astype(jnp.float32))
    sums = sums + swap(sums, "ta", 1)
    w = lax.axis_index("wa")
    s_w, beside = swap_with(sums, jnp.where(w == 0, values[:, :, -1:], values[:, :, :1]), "wa", 1)
    sums = sums + s_w
    x = jnp.concatenate([beside, values, beside], axis=2)
    sums, above, below = ha_round(sums, x[:, :1], x[:, -1:])
    x = jnp.concatenate([above, x, below], axis=1)
    act = activate(x.astype(jnp.float32), finish_stats(sums, values), gain, shift)
    act = jnp.where(inside_mask(height + 2, across + 2, 1), act, 0.0).astype(jnp.bfloat16)
    earlier = passed_along(act[-2:], "ta", 1)
    opening = jnp.concatenate([act[:1], act[:1]], axis=0)
    earlier = jnp.where(lax.axis_index("ta") == 0, opening, earlier)
    return jnp.concatenate([earlier, act], axis=0)


def fast_latent_input(values):
    sums = local_sums(values.astype(jnp.float32))
    sums = sums + swap(sums, "ta", 1)
    s_w, beside = swap_with(sums, values[:, :, :1], "wa", 1)
    sums = sums + s_w
    x = jnp.concatenate([values, beside], axis=2)
    sums, _, below = ha_round(sums, x[:, :1], x[:, :1])
    x = jnp.concatenate([x, below], axis=1)
    return finish_stats(sums, values), x


def norm_conv(values, gain, shift, kernel, result=None):
    frames, height, across, _ = values.shape
    if fast_mesh():
        act = fast_conv_input(values, gain, shift)
    else:
        stats = group_stats(values.astype(jnp.float32))
        extended = conv_halo(values)
        act = activate(extended.astype(jnp.float32), stats, gain, shift)
        act = jnp.where(inside_mask(height + 2, across + 2, 1), act, 0.0).astype(jnp.bfloat16)
    return valid_conv(act, kernel, frames, height, across, result)


def per_device(
    latents,
    norm1_gain,
    norm1_shift,
    up_weight,
    norm2_gain,
    norm2_shift,
    conv_a,
    norm3_gain,
    norm3_shift,
    conv_b,
):
    frames, height, across, channels = latents.shape
    if fast_mesh():
        stats, extended = fast_latent_input(latents)
    else:
        stats = group_stats(latents.astype(jnp.float32))
        extended = latent_halo(latents)
    activated = activate(extended.astype(jnp.float32), stats, norm1_gain, norm1_shift)
    activated = jnp.where(inside_mask(height + 1, across + 1, 0), activated, 0.0)
    lifted = upsample(activated.astype(jnp.bfloat16), up_weight).astype(jnp.bfloat16)
    hidden = norm_conv(lifted, norm2_gain, norm2_shift, conv_a).astype(jnp.bfloat16)
    residual = lifted.astype(jnp.float32).reshape(-1, lifted.shape[-1])
    decoded = norm_conv(hidden, norm3_gain, norm3_shift, conv_b, residual)
    return decoded.astype(jnp.bfloat16)


def solution(mesh):
    return jax.shard_map(
        per_device,
        mesh=mesh,
        in_specs=(
            P(("videos", "ta"), "ha", "wa", None),
            P(),
            P(),
            P(),
            P(),
            P(),
            P(),
            P(),
            P(),
            P(),
        ),
        out_specs=P(("videos", "ta"), "ha", "wa", None),
        check_vma=False,
    )
```
